128 devices in a mesh: head: 4 (over z), page: 32 (over x, y, core).
Axes of the slice: x: 4, y: 4, z: 4, core: 2. Of those that a mesh axis runs over, the one named last changes fastest.
Arguments:
- hidden_in: bfloat16 [32, 1024, 1024], P('page', 'head'), may hold values from -6 to 6
- norm_gain: float32 [1024], replicated, may hold values from 0.1 to 1.9
- w_qkv: bfloat16 [1024, 3, 1024], P(None, None, 'head'), may hold values from -0.1875 to 0.1875
- w_out: bfloat16 [1024, 1024], P('head'), may hold values from -0.75 to 0.75
- cache_kv: bfloat16 [2, 64, 128, 1024], P(None, 'page', None, 'head'), may hold values from -110 to 110, as said below
- page_node: int32 [64], replicated, may hold values from 0 to 18, as said below
- page_fill: int32 [64], replicated, may hold values from 1 to 128
- node_parent: int32 [19], replicated, may hold values from 0 to 2, as said below
- tok_seg: int32 [32, 1024], P('page'), may hold values from 0 to 7, never falling along the last dimension, each value on 1 to 256 neighbouring positions
- req_leaf: int32 [32, 8], P('page'), may hold values from 3 to 18, as said below
Outputs:
- attn_out: bfloat16 [32, 1024, 1024], P('page', 'head')
The draws below stay inside these ranges and needn't reach their ends.
Inputs may be any that keep to these rules, and one draw needn't show every extreme that they name: `cache_kv`: entries of the cache; keys and values. `page_node`: every node owns at least one page. `node_parent`: node 0 is the root and its own parent; nodes 1 to 2 have parent 0; the others have a parent among nodes 1 to 2, and each of those has a child. `req_leaf`: each request names a lowest-level node; every lowest-level node is named by some request.
All inputs are finite; a program needn't handle non-finite values.
Results may differ from the reference program's by a relative error of at most 0.018.
Values may be sent and summed in bfloat16 or wider, within the bound.
No kernel may reach another device: no remote copies, remote signals or barrier semaphores. Data moves between devices by JAX's collectives and lax.ppermute only.
A program may use at most 64 MiB of HBM per device.

```python
import math
import jax
import jax.numpy as jnp
import numpy as np
from jax import lax

D = 1024
H = 16
HD = 64
PAGE = 128
SEGS = 8
BRANCHES = 2
TQ = 1024
MOST = 256
SHARDS = 32
PAGES = 64
LEAVES = 16
NODES = 19
N_PAGE = 32


def draw_cache_kv(key, part):
    key_base = jax.random.fold_in(key, 0)
    shape = (2, PAGES, PAGE, H, HD)
    whole = jnp.clip(jax.random.normal(key_base, shape, jnp.float32), -4.0, 4.0)
    return whole.reshape(2, PAGES, PAGE, H * HD).astype(jnp.bfloat16)


def draw_page_node(key, part):
    key_rest, key_order = jax.random.split(jax.random.fold_in(key, 11), 2)
    covered = jnp.arange(NODES, dtype=jnp.int32)
    others = jax.random.randint(key_rest, (PAGES - NODES,), 0, NODES, dtype=jnp.int32)
    return jax.random.permutation(key_order, jnp.concatenate([covered, others])).astype(jnp.int32)


def draw_page_fill(key, part):
    key_pick, key_fill = jax.random.split(jax.random.fold_in(key, 12), 2)
    partial_page = jax.random.randint(key_pick, (PAGES,), 0, 2, dtype=jnp.int32) == 0
    fill_values = jax.random.randint(key_fill, (PAGES,), 1, PAGE + 1, dtype=jnp.int32)
    fill_values = jnp.where(partial_page, fill_values, PAGE)
    return jnp.where(jnp.arange(PAGES, dtype=jnp.int32) == 0, PAGE, fill_values).astype(jnp.int32)


def draw_node_parent(key, part):
    order = jax.random.permutation(jax.random.fold_in(key, 13), LEAVES).astype(jnp.int32)
    lower = 1 + order % BRANCHES
    upper = jnp.zeros((1 + BRANCHES,), jnp.int32)
    return jnp.concatenate([upper, lower]).astype(jnp.int32)


def draw_req_leaf(key, part):
    order = jax.random.permutation(jax.random.fold_in(key, 14), N_PAGE * SEGS).astype(jnp.int32)
    return (1 + BRANCHES + order % LEAVES).reshape(N_PAGE, SEGS).astype(jnp.int32)


def shard_levels(stream_key, shape, shards, low, top_value):
    loudness = 1.0
    for axis_at, blocks in shards:
        steps = jax.random.uniform(jax.random.fold_in(jax.random.fold_in(stream_key, 6), axis_at), (blocks,), jnp.float32, low / len(shards), top_value / len(shards))
        loudness = loudness * jnp.repeat(jnp.exp(steps), shape[axis_at] // blocks).reshape((-1,) + (1,) * (len(shape) - 1 - axis_at))
    return loudness


def profile(count, total, limit, slope):
    weights = [(1 << 20) // math.isqrt(grade ** slope) + 1 for grade in range(2, count + 1)]
    spare, counts = total - limit - (count - 1), [1] * (count - 1)
    while spare > 0:
        movable = [i for i in range(count - 1) if counts[i] < limit]
        whole, remaining = sum([weights[i] for i in movable]), spare
        for i in movable:
            more = min(limit - counts[i], max(1, remaining * weights[i] // whole), spare)
            counts[i] = counts[i] + more
            spare = spare - more
    return np.array([limit] + counts)


def uneven_parts(own_key, number_of, total, reach, skew):
    if number_of == 2:
        one = jax.random.randint(own_key, (), max(1, total - reach), min(reach, total - 1) + 1)
        return jnp.stack([one, total - one])
    sizes = jnp.asarray(profile(number_of, total, reach, skew), jnp.int32)
    pairs = (number_of - 1) // 2
    donor, receiver = sizes[1:1 + 2 * pairs:2], sizes[2:2 + 2 * pairs:2]
    margin = jnp.minimum(donor - 1, reach - receiver)
    passed = jax.random.randint(jax.random.fold_in(own_key, 1), (pairs,), 0, 1 << 20) % (margin + 1)
    sizes = sizes.at[1:1 + 2 * pairs:2].set(donor - passed).at[2:2 + 2 * pairs:2].set(receiver + passed)
    return sizes[jax.random.permutation(jax.random.fold_in(own_key, 2), number_of)]


def bell_draw(stream_key, dims, deviation, limit, shards=(), held_as=jnp.bfloat16):
    array = deviation * jax.random.normal(stream_key, dims, jnp.float32)
    if shards:
        array = array * shard_levels(stream_key, dims, shards, -0.22, 0.18)
    return jnp.clip(array, -limit, limit).astype(held_as)


def setup_inputs(seed: int = 0) -> dict:
    key_of = jax.random.split(jax.random.key(seed), 11)
    hidden_in = bell_draw(key_of[0], (SHARDS, TQ, D), 1.0, 6.0, ((0, 32), (1, 4)))
    norm_gain = jnp.clip(1.0 + 0.18 * jax.random.normal(key_of[1], (D,), jnp.float32), 0.1, 1.9)
    w_qkv = bell_draw(key_of[2], (D, 3, H * HD), D ** -0.5, 0.1875, ((2, 4),))
    w_out = bell_draw(key_of[3], (H * HD, D), HD ** -0.5, 0.75, ((0, 4),))
    cache_kv = draw_cache_kv(jax.random.fold_in(key_of[10], 71), 0)
    page_node = draw_page_node(jax.random.fold_in(key_of[10], 71), 0)
    page_fill = draw_page_fill(jax.random.fold_in(key_of[10], 71), 0)
    node_parent = draw_node_parent(jax.random.fold_in(key_of[10], 71), 0)
    tok_seg = jax.vmap(lambda own: jnp.searchsorted(jnp.cumsum(uneven_parts(own, SEGS, TQ, MOST, 2)), jnp.arange(TQ), side="right"))(jax.random.split(key_of[8], SHARDS)).reshape((SHARDS, TQ)).astype(jnp.int32)
    req_leaf = draw_req_leaf(jax.random.fold_in(key_of[10], 71), 0)
    return dict(hidden_in=hidden_in, norm_gain=norm_gain, w_qkv=w_qkv, w_out=w_out, cache_kv=cache_kv, page_node=page_node, page_fill=page_fill, node_parent=node_parent, tok_seg=tok_seg, req_leaf=req_leaf)


EPSILON = 1e-06
FLOOR_SCORE = -1e+30

def reference(hidden_in, norm_gain, w_qkv, w_out, cache_kv, page_node, page_fill, node_parent, tok_seg, req_leaf):
    key_count = PAGES * PAGE
    cache_keys = jnp.transpose(cache_kv[0].reshape(key_count, H, HD), (1, 0, 2))
    cache_values = jnp.transpose(cache_kv[1].reshape(key_count, H, HD), (1, 0, 2))
    key_node = jnp.repeat(page_node, PAGE).astype(jnp.int32)
    slot_ok = (jnp.arange(PAGE, dtype=jnp.int32)[None, :] < page_fill[:, None]).reshape(key_count)
    position = jnp.arange(TQ, dtype=jnp.int32)

    def shard_out(inputs):
        shard_rows, segment, leaves = inputs
        widened = shard_rows.astype(jnp.float32)
        normed = (widened * lax.rsqrt(lax.optimization_barrier(jnp.mean(widened * widened, axis=1, keepdims=True)) + EPSILON) * norm_gain).astype(jnp.bfloat16)
        projected = jnp.dot(normed, w_qkv.reshape(D, 3 * H * HD), preferred_element_type=jnp.float32).astype(jnp.bfloat16)
        projected = jnp.transpose(projected.reshape(TQ, 3, H, HD), (1, 2, 0, 3))
        leaf_node = leaves[segment].astype(jnp.int32)
        upper_node = node_parent[leaf_node].astype(jnp.int32)
        root_node = node_parent[upper_node].astype(jnp.int32)
        prefix_seen = ((key_node[None, :] == leaf_node[:, None]) | (key_node[None, :] == upper_node[:, None]) | (key_node[None, :] == root_node[:, None])) & slot_ok[None, :]
        suffix_seen = (segment[:, None] == segment[None, :]) & (position[None, :] <= position[:, None])
        visible = jnp.concatenate([prefix_seen, suffix_seen], axis=1)

        def head_out(head_inputs):
            queries, new_keys, new_values, old_keys, old_values = head_inputs
            all_keys = jnp.concatenate([old_keys, new_keys], axis=0)
            all_values = jnp.concatenate([old_values, new_values], axis=0)
            scores = jnp.dot(queries, all_keys.T, preferred_element_type=jnp.float32) * HD ** (-0.5)
            scores = jnp.where(visible, scores, FLOOR_SCORE)
            row_max = lax.optimization_barrier(jnp.max(scores, axis=1, keepdims=True))
            expo = jnp.where(visible, jnp.exp(scores - row_max), 0.0)
            row_sum = lax.optimization_barrier(jnp.sum(expo, axis=1, keepdims=True))
            weighted = jnp.dot(expo.astype(jnp.bfloat16), all_values, preferred_element_type=jnp.float32)
            return (weighted / row_sum).astype(jnp.bfloat16)
        head_outputs = lax.map(head_out, (projected[0], projected[1], projected[2], cache_keys, cache_values))
        attention = jnp.transpose(head_outputs, (1, 0, 2)).reshape(TQ, H * HD)
        return jnp.dot(attention, w_out, preferred_element_type=jnp.float32).astype(jnp.bfloat16)
    return lax.map(shard_out, (hidden_in, tok_seg, req_leaf))
```

```python
import functools

import jax
import jax.numpy as jnp
from jax import lax
from jax.experimental import pallas as pl
from jax.experimental.pallas import tpu as pltpu
from jax.sharding import PartitionSpec as P

HD = 64
EPSILON = 1e-06
FLOOR_SCORE = -1e30
Q_BLOCK = 128
K_BLOCK = 128
INTERPRET = False


def lookup(indices, lookup_table):
    matches = indices[:, None] == jnp.arange(lookup_table.shape[0], dtype=jnp.int32)[None, :]
    return jnp.sum(jnp.where(matches, lookup_table[None, :], 0), axis=1)


def attn_kernel(
    vis_ref, pnode_ref, pfill_ref, kfirst_ref,
    q_ref, tok_ref, kn_ref, vn_ref, segk_ref, cache_ref,
    o_ref,
    m_sc, l_sc, acc_sc,
):
    i = pl.program_id(0)
    tq, width = q_ref.shape
    groups = width // HD
    pages = cache_ref.shape[1]
    kb = cache_ref.shape[2]
    q = q_ref[...] * jnp.asarray(0.125, jnp.bfloat16)
    seg_q = tok_ref[:, 0:1]
    leaf = tok_ref[:, 1:2]
    upper = tok_ref[:, 2:3]
    root = tok_ref[:, 3:4]
    m_sc[...] = jnp.full(m_sc.shape, FLOOR_SCORE, jnp.float32)
    l_sc[...] = jnp.zeros(l_sc.shape, jnp.float32)
    acc_sc[...] = jnp.zeros(acc_sc.shape, jnp.float32)
    col_head = lax.broadcasted_iota(jnp.int32, (kb, width), 1) // HD
    lane = lax.broadcasted_iota(jnp.int32, (1, kb), 1)
    half = lax.broadcasted_iota(jnp.int32, (1, 128), 1) < HD

    def block_diag(x):
        zero = jnp.zeros_like(x)
        return jnp.concatenate([jnp.where(col_head == h, x, zero) for h in range(groups)], axis=0)

    def update(k, v, mask):
        s = lax.dot_general(
            q, block_diag(k), (((1,), (1,)), ((), ())), preferred_element_type=jnp.float32
        )
        probs = []
        alphas = []
        for h in range(groups):
            s_h = jnp.where(mask, s[:, h * kb:(h + 1) * kb], FLOOR_SCORE)
            m_old = m_sc[h]
            m_new = jnp.maximum(m_old, jnp.max(s_h, axis=1, keepdims=True))
            alpha = jnp.exp(m_old - m_new)
            p_h = jnp.where(mask, jnp.exp(s_h - m_new), 0.0)
            l_sc[h] = alpha * l_sc[h] + jnp.sum(p_h, axis=1, keepdims=True)
            m_sc[h] = m_new
            probs.append(p_h.astype(jnp.bfloat16))
            alphas.append(alpha)
        pv = jnp.dot(
            jnp.concatenate(probs, axis=1), block_diag(v), preferred_element_type=jnp.float32
        )
        scale = jnp.concatenate(
            [
                jnp.where(half, alphas[2 * c], alphas[2 * c + 1])
                for c in range(groups // 2)
            ],
            axis=1,
        )
        acc_sc[...] = acc_sc[...] * scale + pv

    def page_step(g, carry):
        @pl.when(vis_ref[i * pages + g] > 0)
        def _():
            node = pnode_ref[g]
            fill = pfill_ref[g]
            tok_ok = (leaf == node) | (upper == node) | (root == node)
            mask = tok_ok & (lane < fill)
            update(cache_ref[0, g], cache_ref[1, g], mask)

        return carry

    lax.fori_loop(0, pages, page_step, 0)

    qpos = i * tq + lax.broadcasted_iota(jnp.int32, (tq, 1), 0)

    def suffix_step(b, carry):
        start = pl.multiple_of(b * kb, kb)
        kpos = start + lane
        mask = (seg_q == segk_ref[pl.ds(b, 1), :]) & (kpos <= qpos)
        update(kn_ref[pl.ds(start, kb), :], vn_ref[pl.ds(start, kb), :], mask)
        return carry

    last = (i * tq + tq - 1) // kb
    lax.fori_loop(kfirst_ref[i], last + 1, suffix_step, 0)

    norm = jnp.concatenate(
        [jnp.where(half, l_sc[2 * c], l_sc[2 * c + 1]) for c in range(groups // 2)], axis=1
    )
    o_ref[...] = (acc_sc[...] / norm).astype(o_ref.dtype)


def attention(vis, page_node, page_fill, kfirst, proj, tok, segk, cache):
    tokens = proj.shape[0]
    width = proj.shape[1] // 3
    groups = width // HD
    nqb = tokens // Q_BLOCK
    grid_spec = pltpu.PrefetchScalarGridSpec(
        num_scalar_prefetch=4,
        grid=(nqb,),
        in_specs=[
            pl.BlockSpec((Q_BLOCK, width), lambda i, *_: (i, 0)),
            pl.BlockSpec((Q_BLOCK, tok.shape[1]), lambda i, *_: (i, 0)),
            pl.BlockSpec((tokens, width), lambda i, *_: (0, 1)),
            pl.BlockSpec((tokens, width), lambda i, *_: (0, 2)),
            pl.BlockSpec(memory_space=pltpu.VMEM),
            pl.BlockSpec(memory_space=pltpu.VMEM),
        ],
        out_specs=pl.BlockSpec((Q_BLOCK, width), lambda i, *_: (i, 0)),
        scratch_shapes=[
            pltpu.VMEM((groups, Q_BLOCK, 1), jnp.float32),
            pltpu.VMEM((groups, Q_BLOCK, 1), jnp.float32),
            pltpu.VMEM((Q_BLOCK, width), jnp.float32),
        ],
    )
    return pl.pallas_call(
        attn_kernel,
        grid_spec=grid_spec,
        interpret=INTERPRET,
        out_shape=jax.ShapeDtypeStruct((tokens, width), jnp.bfloat16),
        compiler_params=pltpu.CompilerParams(
            dimension_semantics=("arbitrary",), vmem_limit_bytes=48 * 1024 * 1024
        ),
    )(vis, page_node, page_fill, kfirst, proj, tok, proj, proj, segk, cache)


def shards(
    hidden_in,
    norm_gain,
    w_qkv,
    w_out,
    cache_kv,
    page_node,
    page_fill,
    node_parent,
    tok_seg,
    req_leaf,
):
    widened = hidden_in[0].astype(jnp.float32)
    normed = (
        widened
        * lax.rsqrt(jnp.mean(widened * widened, axis=1, keepdims=True) + EPSILON)
        * norm_gain
    ).astype(jnp.bfloat16)
    model_width = widened.shape[1]
    group_width = w_qkv.shape[2]
    weight_flat = w_qkv.reshape(model_width, 3 * group_width)
    projected = jnp.dot(
        lax.all_gather(normed, "head", axis=0, tiled=True),
        weight_flat,
        preferred_element_type=jnp.float32,
    ).astype(jnp.bfloat16)
    tokens = projected.shape[0]
    segment = tok_seg[0]
    leaf_node = lookup(segment, req_leaf[0])
    upper_node = lookup(leaf_node, node_parent)
    root_node = lookup(upper_node, node_parent)
    tok = jnp.stack([segment, leaf_node, upper_node, root_node], axis=1)
    page_len = cache_kv.shape[2]
    pages = page_node.shape[0]
    seen = (
        (page_node[None, :] == leaf_node[:, None])
        | (page_node[None, :] == upper_node[:, None])
        | (page_node[None, :] == root_node[:, None])
    )
    nqb = tokens // Q_BLOCK
    vis = jnp.any(seen.reshape(nqb, Q_BLOCK, pages), axis=1).astype(jnp.int32).reshape(-1)
    first_seg = segment[::Q_BLOCK]
    kfirst = (
        jnp.sum((segment[None, :] < first_seg[:, None]).astype(jnp.int32), axis=1) // K_BLOCK
    ).astype(jnp.int32)
    segk = segment.reshape(tokens // K_BLOCK, K_BLOCK)
    cache = lax.all_gather(cache_kv, "page", axis=1, tiled=True)
    attn = attention(vis, page_node, page_fill, kfirst, projected, tok, segk, cache)
    result = lax.psum_scatter(
        jnp.dot(attn, w_out, preferred_element_type=jnp.float32).astype(jnp.bfloat16),
        "head",
        scatter_dimension=0,
        tiled=True,
    )
    return result[None]


def solution(mesh):
    placed = (
        P("page", "head", None),
        P(),
        P(None, None, "head"),
        P("head", None),
        P(None, "page", None, "head"),
        P(),
        P(),
        P(),
        P("page", None),
        P("page", None),
    )
    return jax.shard_map(
        shards, mesh=mesh, in_specs=placed, out_specs=P("page", "head", None), check_vma=False
    )
```

```python
import jax
import jax.numpy as jnp
from jax import lax
from jax.experimental import pallas as pl
from jax.experimental.pallas import tpu as pltpu
from jax.sharding import PartitionSpec as P

HD = 64
EPSILON = 1e-06
FLOOR_SCORE = -1e30
Q_BLOCK = 128
K_BLOCK = 128
INTERPRET = False


def lookup(indices, lookup_table):
    matches = indices[:, None] == jnp.arange(lookup_table.shape[0], dtype=jnp.int32)[None, :]
    return jnp.sum(jnp.where(matches, lookup_table[None, :], 0), axis=1)


def attn_kernel(
    vis_ref, pnode_ref, pfill_ref, kfirst_ref,
    qt_ref, tok_ref, kn_ref, vnt_ref, segk_ref, ck_ref, cvt_ref,
    o_ref,
    m_sc, l_sc, acc_sc,
):
    i = pl.program_id(0)
    width, tq = qt_ref.shape
    groups = width // HD
    pages = ck_ref.shape[0]
    kb = ck_ref.shape[1]
    qt = qt_ref[...] * jnp.asarray(0.125, jnp.bfloat16)
    seg_q = tok_ref[0:1, :]
    leaf = tok_ref[1:2, :]
    upper = tok_ref[2:3, :]
    root = tok_ref[3:4, :]
    m_sc[...] = jnp.full(m_sc.shape, FLOOR_SCORE, jnp.float32)
    l_sc[...] = jnp.zeros(l_sc.shape, jnp.float32)
    acc_sc[...] = jnp.zeros(acc_sc.shape, jnp.float32)
    col_head = lax.broadcasted_iota(jnp.int32, (kb, width), 1) // HD
    row_head = lax.broadcasted_iota(jnp.int32, (width, kb), 0) // HD
    slot = lax.broadcasted_iota(jnp.int32, (kb, 1), 0)

    def update(k, vt, mask):
        zk = jnp.zeros_like(k)
        kbd = jnp.concatenate([jnp.where(col_head == h, k, zk) for h in range(groups)], axis=0)
        st = jnp.dot(kbd, qt, preferred_element_type=jnp.float32)
        probs = []
        scales = []
        for h in range(groups):
            s_h = jnp.where(mask, st[h * kb:(h + 1) * kb, :], FLOOR_SCORE)
            m_old = m_sc[h]
            m_new = jnp.maximum(m_old, jnp.max(s_h, axis=0, keepdims=True))
            alpha = jnp.exp(m_old - m_new)
            p_h = jnp.exp(s_h - m_new)
            l_sc[h] = alpha * l_sc[h] + jnp.sum(p_h, axis=0, keepdims=True)
            m_sc[h] = m_new
            probs.append(p_h.astype(jnp.bfloat16))
            scales.append(jnp.broadcast_to(alpha, (HD, tq)))
        zv = jnp.zeros_like(vt)
        vbdt = jnp.concatenate([jnp.where(row_head == h, vt, zv) for h in range(groups)], axis=1)
        pv = jnp.dot(vbdt, jnp.concatenate(probs, axis=0), preferred_element_type=jnp.float32)
        acc_sc[...] = acc_sc[...] * jnp.concatenate(scales, axis=0) + pv

    qpos = i * tq + lax.broadcasted_iota(jnp.int32, (1, tq), 1)

    def suffix_step(b, carry):
        start = pl.multiple_of(b * kb, kb)
        kpos = start + slot
        mask = (segk_ref[pl.ds(start, kb), :] == seg_q) & (kpos <= qpos)
        update(kn_ref[pl.ds(start, kb), :], vnt_ref[:, pl.ds(start, kb)], mask)
        return carry

    last = (i * tq + tq - 1) // kb
    lax.fori_loop(kfirst_ref[i], last + 1, suffix_step, 0)

    def page_step(g, carry):
        @pl.when(vis_ref[i * pages + g] > 0)
        def _():
            node = pnode_ref[g]
            fill = pfill_ref[g]
            tok_ok = (leaf == node) | (upper == node) | (root == node)
            mask = tok_ok & (slot < fill)
            update(ck_ref[g], cvt_ref[g], mask)

        return carry

    lax.fori_loop(0, pages, page_step, 0)

    norm = jnp.concatenate([jnp.broadcast_to(l_sc[h], (HD, tq)) for h in range(groups)], axis=0)
    o_ref[...] = (acc_sc[...] / norm).astype(o_ref.dtype)


def attention(vis, page_node, page_fill, kfirst, qt, tok, proj, vnt, segk, ck, cvt):
    width, tokens = qt.shape
    groups = width // HD
    nqb = tokens // Q_BLOCK
    grid_spec = pltpu.PrefetchScalarGridSpec(
        num_scalar_prefetch=4,
        grid=(nqb,),
        in_specs=[
            pl.BlockSpec((width, Q_BLOCK), lambda i, *_: (0, i)),
            pl.BlockSpec((tok.shape[0], Q_BLOCK), lambda i, *_: (0, i)),
            pl.BlockSpec((tokens, width), lambda i, *_: (0, 1)),
            pl.BlockSpec(memory_space=pltpu.VMEM),
            pl.BlockSpec(memory_space=pltpu.VMEM),
            pl.BlockSpec(memory_space=pltpu.VMEM),
            pl.BlockSpec(memory_space=pltpu.VMEM),
        ],
        out_specs=pl.BlockSpec((width, Q_BLOCK), lambda i, *_: (0, i)),
        scratch_shapes=[
            pltpu.VMEM((groups, 1, Q_BLOCK), jnp.float32),
            pltpu.VMEM((groups, 1, Q_BLOCK), jnp.float32),
            pltpu.VMEM((width, Q_BLOCK), jnp.float32),
        ],
    )
    return pl.pallas_call(
        attn_kernel,
        grid_spec=grid_spec,
        interpret=INTERPRET,
        out_shape=jax.ShapeDtypeStruct((width, tokens), jnp.bfloat16),
        compiler_params=pltpu.CompilerParams(
            dimension_semantics=("arbitrary",), vmem_limit_bytes=48 * 1024 * 1024
        ),
    )(vis, page_node, page_fill, kfirst, qt, tok, proj, vnt, segk, ck, cvt)


def shards(
    hidden_in,
    norm_gain,
    w_qkv,
    w_out,
    cache_kv,
    page_node,
    page_fill,
    node_parent,
    tok_seg,
    req_leaf,
):
    widened = hidden_in[0].astype(jnp.float32)
    normed = (
        widened
        * lax.rsqrt(jnp.mean(widened * widened, axis=1, keepdims=True) + EPSILON)
        * norm_gain
    ).astype(jnp.bfloat16)
    model_width = widened.shape[1]
    group_width = w_qkv.shape[2]
    weight_flat = w_qkv.reshape(model_width, 3 * group_width)
    projected = jnp.dot(
        lax.all_gather(normed, "head", axis=0, tiled=True),
        weight_flat,
        preferred_element_type=jnp.float32,
    ).astype(jnp.bfloat16)
    tokens = projected.shape[0]
    segment = tok_seg[0]
    leaf_node = lookup(segment, req_leaf[0])
    upper_node = lookup(leaf_node, node_parent)
    root_node = lookup(upper_node, node_parent)
    zero_row = jnp.zeros_like(segment)
    tok = jnp.stack(
        [segment, leaf_node, upper_node, root_node] + [zero_row] * 4, axis=0
    )
    pages = page_node.shape[0]
    seen = (
        (page_node[None, :] == leaf_node[:, None])
        | (page_node[None, :] == upper_node[:, None])
        | (page_node[None, :] == root_node[:, None])
    )
    nqb = tokens // Q_BLOCK
    vis = jnp.any(seen.reshape(nqb, Q_BLOCK, pages), axis=1).astype(jnp.int32).reshape(-1)
    first_seg = segment[::Q_BLOCK]
    kfirst = (
        jnp.sum((segment[None, :] < first_seg[:, None]).astype(jnp.int32), axis=1) // K_BLOCK
    ).astype(jnp.int32)
    segk = segment[:, None]
    qt = projected[:, :group_width].T
    vnt = projected[:, 2 * group_width:].T
    ck = lax.all_gather(cache_kv[0], "page", axis=0, tiled=True)
    cvt = lax.all_gather(jnp.swapaxes(cache_kv[1], 1, 2), "page", axis=0, tiled=True)
    attn_t = attention(vis, page_node, page_fill, kfirst, qt, tok, projected, vnt, segk, ck, cvt)
    result = lax.psum_scatter(
        lax.dot_general(
            attn_t, w_out, (((0,), (0,)), ((), ())), preferred_element_type=jnp.float32
        ).astype(jnp.bfloat16),
        "head",
        scatter_dimension=0,
        tiled=True,
    )
    return result[None]


def solution(mesh):
    placed = (
        P("page", "head", None),
        P(),
        P(None, None, "head"),
        P("head", None),
        P(None, "page", None, "head"),
        P(),
        P(),
        P(),
        P("page", None),
        P("page", None),
    )
    return jax.shard_map(
        shards, mesh=mesh, in_specs=placed, out_specs=P("page", "head", None), check_vma=False
    )
```

```python
import jax
import jax.numpy as jnp
from jax import lax
from jax.experimental import pallas as pl
from jax.experimental.pallas import tpu as pltpu
from jax.sharding import PartitionSpec as P

HD = 64
EPSILON = 1e-06
FLOOR_SCORE = -1e30
Q_BLOCK = 128
K_BLOCK = 128
INTERPRET = False


def lookup(indices, lookup_table):
    matches = indices[:, None] == jnp.arange(lookup_table.shape[0], dtype=jnp.int32)[None, :]
    return jnp.sum(jnp.where(matches, lookup_table[None, :], 0), axis=1)


def attn_kernel(
    vis_ref, pnode_ref, pfill_ref, kfirst_ref,
    qt_ref, tok_ref, kn_ref, vnt_ref, segk_ref, cache_ref,
    o_ref,
    m_sc, l_sc, acc_sc, cvt_ref,
):
    i = pl.program_id(0)
    width, tq = qt_ref.shape
    groups = width // HD
    pages = cache_ref.shape[1]
    kb = cache_ref.shape[2]

    @pl.when(i == 0)
    def _():
        def transpose_page(g, carry):
            cvt_ref[g] = cache_ref[1, g].astype(jnp.float32).T.astype(cvt_ref.dtype)
            return carry

        lax.fori_loop(0, pages, transpose_page, 0)

    qt = qt_ref[...] * jnp.asarray(0.125, jnp.bfloat16)
    seg_q = tok_ref[0:1, :]
    leaf = tok_ref[1:2, :]
    upper = tok_ref[2:3, :]
    root = tok_ref[3:4, :]
    m_sc[...] = jnp.full(m_sc.shape, FLOOR_SCORE, jnp.float32)
    l_sc[...] = jnp.zeros(l_sc.shape, jnp.float32)
    acc_sc[...] = jnp.zeros(acc_sc.shape, jnp.float32)
    col_head = lax.broadcasted_iota(jnp.int32, (kb, width), 1) // HD
    row_head = lax.broadcasted_iota(jnp.int32, (width, kb), 0) // HD
    slot = lax.broadcasted_iota(jnp.int32, (kb, 1), 0)

    def update(k, vt, mask):
        zk = jnp.zeros_like(k)
        kbd = jnp.concatenate([jnp.where(col_head == h, k, zk) for h in range(groups)], axis=0)
        st = jnp.dot(kbd, qt, preferred_element_type=jnp.float32)
        probs = []
        scales = []
        for h in range(groups):
            s_h = jnp.where(mask, st[h * kb:(h + 1) * kb, :], FLOOR_SCORE)
            m_old = m_sc[h]
            m_new = jnp.maximum(m_old, jnp.max(s_h, axis=0, keepdims=True))
            alpha = jnp.exp(m_old - m_new)
            p_h = jnp.exp(s_h - m_new)
            l_sc[h] = alpha * l_sc[h] + jnp.sum(p_h, axis=0, keepdims=True)
            m_sc[h] = m_new
            probs.append(p_h.astype(jnp.bfloat16))
            scales.append(jnp.broadcast_to(alpha, (HD, tq)))
        zv = jnp.zeros_like(vt)
        vbdt = jnp.concatenate([jnp.where(row_head == h, vt, zv) for h in range(groups)], axis=1)
        pv = jnp.dot(vbdt, jnp.concatenate(probs, axis=0), preferred_element_type=jnp.float32)
        acc_sc[...] = acc_sc[...] * jnp.concatenate(scales, axis=0) + pv

    qpos = i * tq + lax.broadcasted_iota(jnp.int32, (1, tq), 1)

    def suffix_step(b, carry):
        start = pl.multiple_of(b * kb, kb)
        kpos = start + slot
        mask = (segk_ref[pl.ds(start, kb), :] == seg_q) & (kpos <= qpos)
        update(kn_ref[pl.ds(start, kb), :], vnt_ref[:, pl.ds(start, kb)], mask)
        return carry

    last = (i * tq + tq - 1) // kb
    lax.fori_loop(kfirst_ref[i], last + 1, suffix_step, 0)

    def page_step(g, carry):
        @pl.when(vis_ref[i * pages + g] > 0)
        def _():
            node = pnode_ref[g]
            fill = pfill_ref[g]
            tok_ok = (leaf == node) | (upper == node) | (root == node)
            mask = tok_ok & (slot < fill)
            update(cache_ref[0, g], cvt_ref[g], mask)

        return carry

    lax.fori_loop(0, pages, page_step, 0)

    norm = jnp.concatenate([jnp.broadcast_to(l_sc[h], (HD, tq)) for h in range(groups)], axis=0)
    o_ref[...] = (acc_sc[...] / norm).astype(o_ref.dtype)


def attention(vis, page_node, page_fill, kfirst, qt, tok, proj, vnt, segk, cache):
    width, tokens = qt.shape
    groups = width // HD
    nqb = tokens // Q_BLOCK
    grid_spec = pltpu.PrefetchScalarGridSpec(
        num_scalar_prefetch=4,
        grid=(nqb,),
        in_specs=[
            pl.BlockSpec((width, Q_BLOCK), lambda i, *_: (0, i)),
            pl.BlockSpec((tok.shape[0], Q_BLOCK), lambda i, *_: (0, i)),
            pl.BlockSpec((tokens, width), lambda i, *_: (0, 1)),
            pl.BlockSpec(memory_space=pltpu.VMEM),
            pl.BlockSpec(memory_space=pltpu.VMEM),
            pl.BlockSpec(memory_space=pltpu.VMEM),
        ],
        out_specs=pl.BlockSpec((width, Q_BLOCK), lambda i, *_: (0, i)),
        scratch_shapes=[
            pltpu.VMEM((groups, 1, Q_BLOCK), jnp.float32),
            pltpu.VMEM((groups, 1, Q_BLOCK), jnp.float32),
            pltpu.VMEM((width, Q_BLOCK), jnp.float32),
            pltpu.VMEM((cache.shape[1], width, cache.shape[2]), jnp.bfloat16),
        ],
    )
    return pl.pallas_call(
        attn_kernel,
        grid_spec=grid_spec,
        interpret=INTERPRET,
        out_shape=jax.ShapeDtypeStruct((width, tokens), jnp.bfloat16),
        compiler_params=pltpu.CompilerParams(
            dimension_semantics=("arbitrary",), vmem_limit_bytes=48 * 1024 * 1024
        ),
    )(vis, page_node, page_fill, kfirst, qt, tok, proj, vnt, segk, cache)


def shards(
    hidden_in,
    norm_gain,
    w_qkv,
    w_out,
    cache_kv,
    page_node,
    page_fill,
    node_parent,
    tok_seg,
    req_leaf,
):
    widened = hidden_in[0].astype(jnp.float32)
    normed = (
        widened
        * lax.rsqrt(jnp.mean(widened * widened, axis=1, keepdims=True) + EPSILON)
        * norm_gain
    ).astype(jnp.bfloat16)
    model_width = widened.shape[1]
    group_width = w_qkv.shape[2]
    weight_flat = w_qkv.reshape(model_width, 3 * group_width)
    projected = jnp.dot(
        lax.all_gather(normed, "head", axis=0, tiled=True),
        weight_flat,
        preferred_element_type=jnp.float32,
    ).astype(jnp.bfloat16)
    tokens = projected.shape[0]
    segment = tok_seg[0]
    leaf_node = lookup(segment, req_leaf[0])
    upper_node = lookup(leaf_node, node_parent)
    root_node = lookup(upper_node, node_parent)
    zero_row = jnp.zeros_like(segment)
    tok = jnp.stack(
        [segment, leaf_node, upper_node, root_node] + [zero_row] * 4, axis=0
    )
    pages = page_node.shape[0]
    seen = (
        (page_node[None, :] == leaf_node[:, None])
        | (page_node[None, :] == upper_node[:, None])
        | (page_node[None, :] == root_node[:, None])
    )
    nqb = tokens // Q_BLOCK
    vis = jnp.any(seen.reshape(nqb, Q_BLOCK, pages), axis=1).astype(jnp.int32).reshape(-1)
    first_seg = segment[::Q_BLOCK]
    kfirst = (
        jnp.sum((segment[None, :] < first_seg[:, None]).astype(jnp.int32), axis=1) // K_BLOCK
    ).astype(jnp.int32)
    segk = segment[:, None]
    qt = projected[:, :group_width].T
    vnt = projected[:, 2 * group_width:].T
    cache = lax.all_gather(cache_kv, "page", axis=1, tiled=True)
    attn_t = attention(vis, page_node, page_fill, kfirst, qt, tok, projected, vnt, segk, cache)
    result = lax.psum_scatter(
        lax.dot_general(
            attn_t, w_out, (((0,), (0,)), ((), ())), preferred_element_type=jnp.float32
        ).astype(jnp.bfloat16),
        "head",
        scatter_dimension=0,
        tiled=True,
    )
    return result[None]


def solution(mesh):
    placed = (
        P("page", "head", None),
        P(),
        P(None, None, "head"),
        P("head", None),
        P(None, "page", None, "head"),
        P(),
        P(),
        P(),
        P("page", None),
        P("page", None),
    )
    return jax.shard_map(
        shards, mesh=mesh, in_specs=placed, out_specs=P("page", "head", None), check_vma=False
    )
```

```python
import jax
import jax.numpy as jnp
from jax import lax
from jax.experimental import pallas as pl
from jax.experimental.pallas import tpu as pltpu
from jax.sharding import PartitionSpec as P

HD = 64
EPSILON = 1e-06
FLOOR_SCORE = -1e30
Q_BLOCK = 128
K_BLOCK = 128
INTERPRET = False


def lookup(indices, lookup_table):
    matches = indices[:, None] == jnp.arange(lookup_table.shape[0], dtype=jnp.int32)[None, :]
    return jnp.sum(jnp.where(matches, lookup_table[None, :], 0), axis=1)


def attn_kernel(
    vis_ref, pnode_ref, pfill_ref, kfirst_ref,
    qt_ref, tok_ref, kn_ref, vnt_ref, segk_ref, cache_ref,
    o_ref,
    m_sc, l_sc, acc_sc, cvt_ref,
):
    i = pl.program_id(0)
    width, tq = qt_ref.shape
    groups = width // HD
    pages = cache_ref.shape[1]
    kb = cache_ref.shape[2]

    @pl.when(i == 0)
    def _():
        def transpose_page(g, carry):
            cvt_ref[g] = cache_ref[1, g].astype(jnp.float32).T.astype(cvt_ref.dtype)
            return carry

        lax.fori_loop(0, pages, transpose_page, 0)

    qt = qt_ref[...] * jnp.asarray(0.125, jnp.bfloat16)
    seg_q = tok_ref[0:1, :]
    leaf = tok_ref[1:2, :]
    upper = tok_ref[2:3, :]
    root = tok_ref[3:4, :]
    m_sc[...] = jnp.full(m_sc.shape, FLOOR_SCORE, jnp.float32)
    l_sc[...] = jnp.zeros(l_sc.shape, jnp.float32)
    acc_sc[...] = jnp.zeros(acc_sc.shape, jnp.float32)
    col_head = lax.broadcasted_iota(jnp.int32, (kb, width), 1) // HD
    row_head = lax.broadcasted_iota(jnp.int32, (width, kb), 0) // HD
    slot = lax.broadcasted_iota(jnp.int32, (kb, 1), 0)

    def update(k, vt, mask):
        zk = jnp.zeros_like(k)
        kbd = jnp.concatenate([jnp.where(col_head == h, k, zk) for h in range(groups)], axis=0)
        st = jnp.dot(kbd, qt, preferred_element_type=jnp.float32)
        probs = []
        scales = []
        for h in range(groups):
            s_h = jnp.where(mask, st[h * kb:(h + 1) * kb, :], FLOOR_SCORE)
            m_old = m_sc[h]
            m_new = jnp.maximum(m_old, jnp.max(s_h, axis=0, keepdims=True))
            alpha = jnp.exp(m_old - m_new)
            p_h = jnp.exp(s_h - m_new)
            l_sc[h] = alpha * l_sc[h] + jnp.sum(p_h, axis=0, keepdims=True)
            m_sc[h] = m_new
            probs.append(p_h.astype(jnp.bfloat16))
            scales.append(jnp.broadcast_to(alpha, (HD, tq)))
        zv = jnp.zeros_like(vt)
        vbdt = jnp.concatenate([jnp.where(row_head == h, vt, zv) for h in range(groups)], axis=1)
        pv = jnp.dot(vbdt, jnp.concatenate(probs, axis=0), preferred_element_type=jnp.float32)
        acc_sc[...] = acc_sc[...] * jnp.concatenate(scales, axis=0) + pv

    qpos = i * tq + lax.broadcasted_iota(jnp.int32, (1, tq), 1)

    def suffix_step(b, carry):
        start = pl.multiple_of(b * kb, kb)
        kpos = start + slot
        mask = (segk_ref[pl.ds(start, kb), :] == seg_q) & (kpos <= qpos)
        update(kn_ref[pl.ds(start, kb), :], vnt_ref[:, pl.ds(start, kb)], mask)
        return carry

    last = (i * tq + tq - 1) // kb
    lax.fori_loop(kfirst_ref[i], last + 1, suffix_step, 0)

    def page_step(g, carry):
        @pl.when(vis_ref[i * pages + g] > 0)
        def _():
            node = pnode_ref[g]
            fill = pfill_ref[g]
            tok_ok = (leaf == node) | (upper == node) | (root == node)
            mask = tok_ok & (slot < fill)
            update(cache_ref[0, g], cvt_ref[g], mask)

        return carry

    lax.fori_loop(0, pages, page_step, 0)

    norm = jnp.concatenate([jnp.broadcast_to(l_sc[h], (HD, tq)) for h in range(groups)], axis=0)
    o_ref[...] = (acc_sc[...] / norm).astype(o_ref.dtype)


def attention(vis, page_node, page_fill, kfirst, qt, tok, proj, vnt, segk, cache):
    width, tokens = qt.shape
    groups = width // HD
    nqb = tokens // Q_BLOCK
    grid_spec = pltpu.PrefetchScalarGridSpec(
        num_scalar_prefetch=4,
        grid=(nqb,),
        in_specs=[
            pl.BlockSpec((width, Q_BLOCK), lambda i, *_: (0, i)),
            pl.BlockSpec((tok.shape[0], Q_BLOCK), lambda i, *_: (0, i)),
            pl.BlockSpec((tokens, width), lambda i, *_: (0, 1)),
            pl.BlockSpec(memory_space=pltpu.VMEM),
            pl.BlockSpec(memory_space=pltpu.VMEM),
            pl.BlockSpec(memory_space=pltpu.VMEM),
        ],
        out_specs=pl.BlockSpec((width, Q_BLOCK), lambda i, *_: (0, i)),
        scratch_shapes=[
            pltpu.VMEM((groups, 1, Q_BLOCK), jnp.float32),
            pltpu.VMEM((groups, 1, Q_BLOCK), jnp.float32),
            pltpu.VMEM((width, Q_BLOCK), jnp.float32),
            pltpu.VMEM((cache.shape[1], width, cache.shape[2]), jnp.bfloat16),
        ],
    )
    return pl.pallas_call(
        attn_kernel,
        grid_spec=grid_spec,
        interpret=INTERPRET,
        out_shape=jax.ShapeDtypeStruct((width, tokens), jnp.bfloat16),
        compiler_params=pltpu.CompilerParams(
            dimension_semantics=("arbitrary",), vmem_limit_bytes=48 * 1024 * 1024
        ),
    )(vis, page_node, page_fill, kfirst, qt, tok, proj, vnt, segk, cache)


def shift_perm(n, d):
    return [(j, (j + d) % n) for j in range(n)]


def head_gather(x, n):
    me = lax.axis_index("head")
    parts = [x] + [lax.ppermute(x, "head", shift_perm(n, d)) for d in range(1, n)]
    stacked = jnp.stack(parts)
    order = (me - jnp.arange(n, dtype=jnp.int32)) % n
    gathered = jnp.take(stacked, order, axis=0)
    return gathered.reshape(n * x.shape[0], x.shape[1])


def head_reduce_scatter(partial, n):
    me = lax.axis_index("head")
    rows = partial.shape[0] // n
    chunks = partial.reshape(n, rows, partial.shape[1])
    total = lax.dynamic_index_in_dim(chunks, me, 0, keepdims=False)
    for d in range(1, n):
        send = lax.dynamic_index_in_dim(chunks, (me + d) % n, 0, keepdims=False)
        recv = lax.ppermute(send.astype(jnp.bfloat16), "head", shift_perm(n, d))
        total = total + recv.astype(jnp.float32)
    return total.astype(jnp.bfloat16)


def shards(
    hidden_in,
    norm_gain,
    w_qkv,
    w_out,
    cache_kv,
    page_node,
    page_fill,
    node_parent,
    tok_seg,
    req_leaf,
):
    widened = hidden_in[0].astype(jnp.float32)
    normed = (
        widened
        * lax.rsqrt(jnp.mean(widened * widened, axis=1, keepdims=True) + EPSILON)
        * norm_gain
    ).astype(jnp.bfloat16)
    model_width = widened.shape[1]
    group_width = w_qkv.shape[2]
    weight_flat = w_qkv.reshape(model_width, 3 * group_width)
    n_head = tok_seg.shape[1] // hidden_in.shape[1]
    projected = jnp.dot(
        head_gather(normed, n_head),
        weight_flat,
        preferred_element_type=jnp.float32,
    ).astype(jnp.bfloat16)
    tokens = projected.shape[0]
    segment = tok_seg[0]
    leaf_node = lookup(segment, req_leaf[0])
    upper_node = lookup(leaf_node, node_parent)
    root_node = lookup(upper_node, node_parent)
    zero_row = jnp.zeros_like(segment)
    tok = jnp.stack(
        [segment, leaf_node, upper_node, root_node] + [zero_row] * 4, axis=0
    )
    pages = page_node.shape[0]
    seen = (
        (page_node[None, :] == leaf_node[:, None])
        | (page_node[None, :] == upper_node[:, None])
        | (page_node[None, :] == root_node[:, None])
    )
    nqb = tokens // Q_BLOCK
    vis = jnp.any(seen.reshape(nqb, Q_BLOCK, pages), axis=1).astype(jnp.int32).reshape(-1)
    first_seg = segment[::Q_BLOCK]
    kfirst = (
        jnp.sum((segment[None, :] < first_seg[:, None]).astype(jnp.int32), axis=1) // K_BLOCK
    ).astype(jnp.int32)
    segk = segment[:, None]
    qt = projected[:, :group_width].T
    vnt = projected[:, 2 * group_width:].T
    cache = lax.all_gather(cache_kv, "page", axis=1, tiled=True)
    attn_t = attention(vis, page_node, page_fill, kfirst, qt, tok, projected, vnt, segk, cache)
    result = head_reduce_scatter(
        lax.dot_general(
            attn_t, w_out, (((0,), (0,)), ((), ())), preferred_element_type=jnp.float32
        ),
        n_head,
    )
    return result[None]


def solution(mesh):
    placed = (
        P("page", "head", None),
        P(),
        P(None, None, "head"),
        P("head", None),
        P(None, "page", None, "head"),
        P(),
        P(),
        P(),
        P("page", None),
        P("page", None),
    )
    return jax.shard_map(
        shards, mesh=mesh, in_specs=placed, out_specs=P("page", "head", None), check_vma=False
    )
```

```python
import jax
import jax.numpy as jnp
from jax import lax
from jax.experimental import pallas as pl
from jax.experimental.pallas import tpu as pltpu
from jax.sharding import PartitionSpec as P

HD = 64
EPSILON = 1e-06
FLOOR_SCORE = -1e30
Q_BLOCK = 256
K_BLOCK = 128
INTERPRET = False


def lookup(indices, lookup_table):
    matches = indices[:, None] == jnp.arange(lookup_table.shape[0], dtype=jnp.int32)[None, :]
    return jnp.sum(jnp.where(matches, lookup_table[None, :], 0), axis=1)


def attn_kernel(
    vis_ref, pnode_ref, pfill_ref, kfirst_ref,
    qt_ref, tok_ref, kn_ref, vnt_ref, segk_ref, cache_ref,
    o_ref,
    m_sc, l_sc, acc_sc, cvt_ref,
):
    i = pl.program_id(0)
    width, tq = qt_ref.shape
    groups = width // HD
    pages = cache_ref.shape[1]
    kb = cache_ref.shape[2]

    @pl.when(i == 0)
    def _():
        def transpose_page(g, carry):
            cvt_ref[g] = cache_ref[1, g].astype(jnp.float32).T.astype(cvt_ref.dtype)
            return carry

        lax.fori_loop(0, pages, transpose_page, 0)

    qt = qt_ref[...] * jnp.asarray(0.125, jnp.bfloat16)
    seg_q = tok_ref[0:1, :]
    leaf = tok_ref[1:2, :]
    upper = tok_ref[2:3, :]
    root = tok_ref[3:4, :]
    m_sc[...] = jnp.full(m_sc.shape, FLOOR_SCORE, jnp.float32)
    l_sc[...] = jnp.zeros(l_sc.shape, jnp.float32)
    acc_sc[...] = jnp.zeros(acc_sc.shape, jnp.float32)
    col_head = lax.broadcasted_iota(jnp.int32, (kb, width), 1) // HD
    row_head = lax.broadcasted_iota(jnp.int32, (width, kb), 0) // HD
    slot = lax.broadcasted_iota(jnp.int32, (kb, 1), 0)

    def update(k, vt, mask):
        zk = jnp.zeros_like(k)
        kbd = jnp.concatenate([jnp.where(col_head == h, k, zk) for h in range(groups)], axis=0)
        st = jnp.dot(kbd, qt, preferred_element_type=jnp.float32)
        probs = []
        scales = []
        for h in range(groups):
            s_h = jnp.where(mask, st[h * kb:(h + 1) * kb, :], FLOOR_SCORE)
            m_old = m_sc[h]
            m_new = jnp.maximum(m_old, jnp.max(s_h, axis=0, keepdims=True))
            alpha = jnp.exp(m_old - m_new)
            p_h = jnp.exp(s_h - m_new)
            l_sc[h] = alpha * l_sc[h] + jnp.sum(p_h, axis=0, keepdims=True)
            m_sc[h] = m_new
            probs.append(p_h.astype(jnp.bfloat16))
            scales.append(jnp.broadcast_to(alpha, (HD, tq)))
        zv = jnp.zeros_like(vt)
        vbdt = jnp.concatenate([jnp.where(row_head == h, vt, zv) for h in range(groups)], axis=1)
        pv = jnp.dot(vbdt, jnp.concatenate(probs, axis=0), preferred_element_type=jnp.float32)
        acc_sc[...] = acc_sc[...] * jnp.concatenate(scales, axis=0) + pv

    qpos = i * tq + lax.broadcasted_iota(jnp.int32, (1, tq), 1)

    def suffix_step(b, carry):
        start = pl.multiple_of(b * kb, kb)
        kpos = start + slot
        mask = (segk_ref[pl.ds(start, kb), :] == seg_q) & (kpos <= qpos)
        update(kn_ref[pl.ds(start, kb), :], vnt_ref[:, pl.ds(start, kb)], mask)
        return carry

    last = (i * tq + tq - 1) // kb
    lax.fori_loop(kfirst_ref[i], last + 1, suffix_step, 0)

    def page_step(g, carry):
        @pl.when(vis_ref[i * pages + g] > 0)
        def _():
            node = pnode_ref[g]
            fill = pfill_ref[g]
            tok_ok = (leaf == node) | (upper == node) | (root == node)
            mask = tok_ok & (slot < fill)
            update(cache_ref[0, g], cvt_ref[g], mask)

        return carry

    lax.fori_loop(0, pages, page_step, 0)

    norm = jnp.concatenate([jnp.broadcast_to(l_sc[h], (HD, tq)) for h in range(groups)], axis=0)
    o_ref[...] = (acc_sc[...] / norm).astype(o_ref.dtype)


def attention(vis, page_node, page_fill, kfirst, qt, tok, proj, vnt, segk, cache):
    width, tokens = qt.shape
    groups = width // HD
    nqb = tokens // Q_BLOCK
    grid_spec = pltpu.PrefetchScalarGridSpec(
        num_scalar_prefetch=4,
        grid=(nqb,),
        in_specs=[
            pl.BlockSpec((width, Q_BLOCK), lambda i, *_: (0, i)),
            pl.BlockSpec((tok.shape[0], Q_BLOCK), lambda i, *_: (0, i)),
            pl.BlockSpec((tokens, width), lambda i, *_: (0, 1)),
            pl.BlockSpec(memory_space=pltpu.VMEM),
            pl.BlockSpec(memory_space=pltpu.VMEM),
            pl.BlockSpec(memory_space=pltpu.VMEM),
        ],
        out_specs=pl.BlockSpec((width, Q_BLOCK), lambda i, *_: (0, i)),
        scratch_shapes=[
            pltpu.VMEM((groups, 1, Q_BLOCK), jnp.float32),
            pltpu.VMEM((groups, 1, Q_BLOCK), jnp.float32),
            pltpu.VMEM((width, Q_BLOCK), jnp.float32),
            pltpu.VMEM((cache.shape[1], width, cache.shape[2]), jnp.bfloat16),
        ],
    )
    return pl.pallas_call(
        attn_kernel,
        grid_spec=grid_spec,
        interpret=INTERPRET,
        out_shape=jax.ShapeDtypeStruct((width, tokens), jnp.bfloat16),
        compiler_params=pltpu.CompilerParams(
            dimension_semantics=("arbitrary",), vmem_limit_bytes=48 * 1024 * 1024
        ),
    )(vis, page_node, page_fill, kfirst, qt, tok, proj, vnt, segk, cache)


def shift_perm(n, d):
    return [(j, (j + d) % n) for j in range(n)]


def head_gather(x, n):
    me = lax.axis_index("head")
    parts = [x] + [lax.ppermute(x, "head", shift_perm(n, d)) for d in range(1, n)]
    stacked = jnp.stack(parts)
    order = (me - jnp.arange(n, dtype=jnp.int32)) % n
    gathered = jnp.take(stacked, order, axis=0)
    return gathered.reshape(n * x.shape[0], x.shape[1])


def head_reduce_scatter(partial, n):
    me = lax.axis_index("head")
    rows = partial.shape[0] // n
    chunks = partial.reshape(n, rows, partial.shape[1])
    total = lax.dynamic_index_in_dim(chunks, me, 0, keepdims=False)
    for d in range(1, n):
        send = lax.dynamic_index_in_dim(chunks, (me + d) % n, 0, keepdims=False)
        recv = lax.ppermute(send.astype(jnp.bfloat16), "head", shift_perm(n, d))
        total = total + recv.astype(jnp.float32)
    return total.astype(jnp.bfloat16)


def shards(
    hidden_in,
    norm_gain,
    w_qkv,
    w_out,
    cache_kv,
    page_node,
    page_fill,
    node_parent,
    tok_seg,
    req_leaf,
):
    widened = hidden_in[0].astype(jnp.float32)
    normed = (
        widened
        * lax.rsqrt(jnp.mean(widened * widened, axis=1, keepdims=True) + EPSILON)
        * norm_gain
    ).astype(jnp.bfloat16)
    model_width = widened.shape[1]
    group_width = w_qkv.shape[2]
    weight_flat = w_qkv.reshape(model_width, 3 * group_width)
    n_head = tok_seg.shape[1] // hidden_in.shape[1]
    projected = jnp.dot(
        head_gather(normed, n_head),
        weight_flat,
        preferred_element_type=jnp.float32,
    ).astype(jnp.bfloat16)
    tokens = projected.shape[0]
    segment = tok_seg[0]
    leaf_node = lookup(segment, req_leaf[0])
    upper_node = lookup(leaf_node, node_parent)
    root_node = lookup(upper_node, node_parent)
    zero_row = jnp.zeros_like(segment)
    tok = jnp.stack(
        [segment, leaf_node, upper_node, root_node] + [zero_row] * 4, axis=0
    )
    pages = page_node.shape[0]
    seen = (
        (page_node[None, :] == leaf_node[:, None])
        | (page_node[None, :] == upper_node[:, None])
        | (page_node[None, :] == root_node[:, None])
    )
    nqb = tokens // Q_BLOCK
    vis = jnp.any(seen.reshape(nqb, Q_BLOCK, pages), axis=1).astype(jnp.int32).reshape(-1)
    first_seg = segment[::Q_BLOCK]
    kfirst = (
        jnp.sum((segment[None, :] < first_seg[:, None]).astype(jnp.int32), axis=1) // K_BLOCK
    ).astype(jnp.int32)
    segk = segment[:, None]
    qt = projected[:, :group_width].T
    vnt = projected[:, 2 * group_width:].T
    cache = lax.all_gather(cache_kv, "page", axis=1, tiled=True)
    attn_t = attention(vis, page_node, page_fill, kfirst, qt, tok, projected, vnt, segk, cache)
    result = head_reduce_scatter(
        lax.dot_general(
            attn_t, w_out, (((0,), (0,)), ((), ())), preferred_element_type=jnp.float32
        ),
        n_head,
    )
    return result[None]


def solution(mesh):
    placed = (
        P("page", "head", None),
        P(),
        P(None, None, "head"),
        P("head", None),
        P(None, "page", None, "head"),
        P(),
        P(),
        P(),
        P("page", None),
        P("page", None),
    )
    return jax.shard_map(
        shards, mesh=mesh, in_specs=placed, out_specs=P("page", "head", None), check_vma=False
    )
```

```python
import jax
import jax.numpy as jnp
from jax import lax
from jax.experimental import pallas as pl
from jax.experimental.pallas import tpu as pltpu
from jax.sharding import PartitionSpec as P

HD = 64
EPSILON = 1e-06
FLOOR_SCORE = -1e30
Q_BLOCK = 256
K_BLOCK = 128
INTERPRET = False


def lookup(indices, lookup_table):
    matches = indices[:, None] == jnp.arange(lookup_table.shape[0], dtype=jnp.int32)[None, :]
    return jnp.sum(jnp.where(matches, lookup_table[None, :], 0), axis=1)


def attn_kernel(
    plist_ref, pcount_ref, pnode_ref, pfill_ref, kfirst_ref,
    qt_ref, tok_ref, kn_ref, vnt_ref, segk_ref, cache_ref,
    o_ref,
    ma_sc, la_sc, acca_sc, mb_sc, lb_sc, accb_sc, cvt_ref,
):
    i = pl.program_id(0)
    width, tq = qt_ref.shape
    groups = width // HD
    pages = cache_ref.shape[1]
    kb = cache_ref.shape[2]

    @pl.when(i == 0)
    def _():
        def transpose_page(g, carry):
            cvt_ref[g] = cache_ref[1, g].astype(jnp.float32).T.astype(cvt_ref.dtype)
            return carry

        lax.fori_loop(0, pages, transpose_page, 0)

    qt = qt_ref[...] * jnp.asarray(0.125, jnp.bfloat16)
    seg_q = tok_ref[0:1, :]
    leaf = tok_ref[1:2, :]
    upper = tok_ref[2:3, :]
    root = tok_ref[3:4, :]
    for m_sc, l_sc, acc_sc in ((ma_sc, la_sc, acca_sc), (mb_sc, lb_sc, accb_sc)):
        m_sc[...] = jnp.full(m_sc.shape, FLOOR_SCORE, jnp.float32)
        l_sc[...] = jnp.zeros(l_sc.shape, jnp.float32)
        acc_sc[...] = jnp.zeros(acc_sc.shape, jnp.float32)
    col_head = lax.broadcasted_iota(jnp.int32, (kb, width), 1) // HD
    row_head = lax.broadcasted_iota(jnp.int32, (width, kb), 0) // HD
    slot = lax.broadcasted_iota(jnp.int32, (kb, 1), 0)

    def update(state, k, vt, mask):
        m_sc, l_sc, acc_sc = state
        zk = jnp.zeros_like(k)
        kbd = jnp.concatenate([jnp.where(col_head == h, k, zk) for h in range(groups)], axis=0)
        st = jnp.dot(kbd, qt, preferred_element_type=jnp.float32)
        probs = []
        scales = []
        for h in range(groups):
            s_h = jnp.where(mask, st[h * kb:(h + 1) * kb, :], FLOOR_SCORE)
            m_old = m_sc[h]
            m_new = jnp.maximum(m_old, jnp.max(s_h, axis=0, keepdims=True))
            alpha = jnp.exp(m_old - m_new)
            p_h = jnp.exp(s_h - m_new)
            l_sc[h] = alpha * l_sc[h] + jnp.sum(p_h, axis=0, keepdims=True)
            m_sc[h] = m_new
            probs.append(p_h.astype(jnp.bfloat16))
            scales.append(jnp.broadcast_to(alpha, (HD, tq)))
        zv = jnp.zeros_like(vt)
        vbdt = jnp.concatenate([jnp.where(row_head == h, vt, zv) for h in range(groups)], axis=1)
        pv = jnp.dot(vbdt, jnp.concatenate(probs, axis=0), preferred_element_type=jnp.float32)
        acc_sc[...] = acc_sc[...] * jnp.concatenate(scales, axis=0) + pv

    chain_a = (ma_sc, la_sc, acca_sc)
    chain_b = (mb_sc, lb_sc, accb_sc)
    qpos = i * tq + lax.broadcasted_iota(jnp.int32, (1, tq), 1)

    def suffix_step(b, carry):
        start = pl.multiple_of(b * kb, kb)
        kpos = start + slot
        mask = (segk_ref[pl.ds(start, kb), :] == seg_q) & (kpos <= qpos)
        update(chain_a, kn_ref[pl.ds(start, kb), :], vnt_ref[:, pl.ds(start, kb)], mask)
        return carry

    last = (i * tq + tq - 1) // kb
    lax.fori_loop(kfirst_ref[i], last + 1, suffix_step, 0)

    count = pcount_ref[i]

    def page_mask(g, valid):
        node = pnode_ref[g]
        fill = jnp.where(valid, pfill_ref[g], 0)
        tok_ok = (leaf == node) | (upper == node) | (root == node)
        return tok_ok & (slot < fill)

    def pair_step(j, carry):
        g0 = plist_ref[i * pages + 2 * j]
        g1 = plist_ref[i * pages + 2 * j + 1]
        update(chain_a, cache_ref[0, g0], cvt_ref[g0], page_mask(g0, True))
        update(chain_b, cache_ref[0, g1], cvt_ref[g1], page_mask(g1, 2 * j + 1 < count))
        return carry

    lax.fori_loop(0, (count + 1) // 2, pair_step, 0)

    parts = []
    for h in range(groups):
        m_all = jnp.maximum(ma_sc[h], mb_sc[h])
        wa = jnp.exp(ma_sc[h] - m_all)
        wb = jnp.exp(mb_sc[h] - m_all)
        l_all = la_sc[h] * wa + lb_sc[h] * wb
        rows = slice(h * HD, (h + 1) * HD)
        acc_h = acca_sc[rows, :] * wa + accb_sc[rows, :] * wb
        parts.append(acc_h / l_all)
    o_ref[...] = jnp.concatenate(parts, axis=0).astype(o_ref.dtype)


def attention(plist, pcount, page_node, page_fill, kfirst, qt, tok, proj, vnt, segk, cache):
    width, tokens = qt.shape
    groups = width // HD
    nqb = tokens // Q_BLOCK
    state = [
        pltpu.VMEM((groups, 1, Q_BLOCK), jnp.float32),
        pltpu.VMEM((groups, 1, Q_BLOCK), jnp.float32),
        pltpu.VMEM((width, Q_BLOCK), jnp.float32),
    ]
    grid_spec = pltpu.PrefetchScalarGridSpec(
        num_scalar_prefetch=5,
        grid=(nqb,),
        in_specs=[
            pl.BlockSpec((width, Q_BLOCK), lambda i, *_: (0, i)),
            pl.BlockSpec((tok.shape[0], Q_BLOCK), lambda i, *_: (0, i)),
            pl.BlockSpec((tokens, width), lambda i, *_: (0, 1)),
            pl.BlockSpec(memory_space=pltpu.VMEM),
            pl.BlockSpec(memory_space=pltpu.VMEM),
            pl.BlockSpec(memory_space=pltpu.VMEM),
        ],
        out_specs=pl.BlockSpec((width, Q_BLOCK), lambda i, *_: (0, i)),
        scratch_shapes=state + state + [
            pltpu.VMEM((cache.shape[1], width, cache.shape[2]), jnp.bfloat16),
        ],
    )
    return pl.pallas_call(
        attn_kernel,
        grid_spec=grid_spec,
        interpret=INTERPRET,
        out_shape=jax.ShapeDtypeStruct((width, tokens), jnp.bfloat16),
        compiler_params=pltpu.CompilerParams(
            dimension_semantics=("arbitrary",), vmem_limit_bytes=48 * 1024 * 1024
        ),
    )(plist, pcount, page_node, page_fill, kfirst, qt, tok, proj, vnt, segk, cache)


def shift_perm(n, d):
    return [(j, (j + d) % n) for j in range(n)]


def head_gather(x, n):
    me = lax.axis_index("head")
    parts = [x] + [lax.ppermute(x, "head", shift_perm(n, d)) for d in range(1, n)]
    stacked = jnp.stack(parts)
    order = (me - jnp.arange(n, dtype=jnp.int32)) % n
    gathered = jnp.take(stacked, order, axis=0)
    return gathered.reshape(n * x.shape[0], x.shape[1])


def head_reduce_scatter(partial, n):
    me = lax.axis_index("head")
    rows = partial.shape[0] // n
    chunks = partial.reshape(n, rows, partial.shape[1])
    total = lax.dynamic_index_in_dim(chunks, me, 0, keepdims=False)
    for d in range(1, n):
        send = lax.dynamic_index_in_dim(chunks, (me + d) % n, 0, keepdims=False)
        recv = lax.ppermute(send.astype(jnp.bfloat16), "head", shift_perm(n, d))
        total = total + recv.astype(jnp.float32)
    return total.astype(jnp.bfloat16)


def shards(
    hidden_in,
    norm_gain,
    w_qkv,
    w_out,
    cache_kv,
    page_node,
    page_fill,
    node_parent,
    tok_seg,
    req_leaf,
):
    widened = hidden_in[0].astype(jnp.float32)
    normed = (
        widened
        * lax.rsqrt(jnp.mean(widened * widened, axis=1, keepdims=True) + EPSILON)
        * norm_gain
    ).astype(jnp.bfloat16)
    model_width = widened.shape[1]
    group_width = w_qkv.shape[2]
    weight_flat = w_qkv.reshape(model_width, 3 * group_width)
    n_head = tok_seg.shape[1] // hidden_in.shape[1]
    projected = jnp.dot(
        head_gather(normed, n_head),
        weight_flat,
        preferred_element_type=jnp.float32,
    ).astype(jnp.bfloat16)
    tokens = projected.shape[0]
    segment = tok_seg[0]
    leaf_node = lookup(segment, req_leaf[0])
    upper_node = lookup(leaf_node, node_parent)
    root_node = lookup(upper_node, node_parent)
    zero_row = jnp.zeros_like(segment)
    tok = jnp.stack(
        [segment, leaf_node, upper_node, root_node] + [zero_row] * 4, axis=0
    )
    pages = page_node.shape[0]
    seen = (
        (page_node[None, :] == leaf_node[:, None])
        | (page_node[None, :] == upper_node[:, None])
        | (page_node[None, :] == root_node[:, None])
    )
    nqb = tokens // Q_BLOCK
    vis = jnp.any(seen.reshape(nqb, Q_BLOCK, pages), axis=1).astype(jnp.int32)
    rank = jnp.cumsum(vis, axis=1) - 1
    picked = (vis[:, :, None] > 0) & (rank[:, :, None] == jnp.arange(pages)[None, None, :])
    plist = jnp.sum(
        jnp.where(picked, jnp.arange(pages, dtype=jnp.int32)[None, :, None], 0), axis=1
    ).astype(jnp.int32).reshape(-1)
    pcount = jnp.sum(vis, axis=1).astype(jnp.int32)
    first_seg = segment[::Q_BLOCK]
    kfirst = (
        jnp.sum((segment[None, :] < first_seg[:, None]).astype(jnp.int32), axis=1) // K_BLOCK
    ).astype(jnp.int32)
    segk = segment[:, None]
    qt = projected[:, :group_width].T
    vnt = projected[:, 2 * group_width:].T
    cache = lax.all_gather(cache_kv, "page", axis=1, tiled=True)
    attn_t = attention(
        plist, pcount, page_node, page_fill, kfirst, qt, tok, projected, vnt, segk, cache
    )
    result = head_reduce_scatter(
        lax.dot_general(
            attn_t, w_out, (((0,), (0,)), ((), ())), preferred_element_type=jnp.float32
        ),
        n_head,
    )
    return result[None]


def solution(mesh):
    placed = (
        P("page", "head", None),
        P(),
        P(None, None, "head"),
        P("head", None),
        P(None, "page", None, "head"),
        P(),
        P(),
        P(),
        P("page", None),
        P("page", None),
    )
    return jax.shard_map(
        shards, mesh=mesh, in_specs=placed, out_specs=P("page", "head", None), check_vma=False
    )
```

```python
import jax
import jax.numpy as jnp
from jax import lax
from jax.experimental import pallas as pl
from jax.experimental.pallas import tpu as pltpu
from jax.sharding import PartitionSpec as P

HD = 64
EPSILON = 1e-06
FLOOR_SCORE = -1e30
Q_BLOCK = 256
K_BLOCK = 128
INTERPRET = False


def lookup(indices, lookup_table):
    matches = indices[:, None] == jnp.arange(lookup_table.shape[0], dtype=jnp.int32)[None, :]
    return jnp.sum(jnp.where(matches, lookup_table[None, :], 0), axis=1)


def attn_kernel(
    plist_ref, pcount_ref, pnode_ref, pfill_ref, kfirst_ref,
    qt_ref, tok_ref, kn_ref, vnt_ref, segk_ref, ck_ref, cv_ref,
    o_ref,
    ma_sc, la_sc, acca_sc, mb_sc, lb_sc, accb_sc, cvt_ref,
):
    i = pl.program_id(0)
    width, tq = qt_ref.shape
    groups = width // HD
    pages = ck_ref.shape[0]
    kb = ck_ref.shape[1]

    @pl.when(i == 0)
    def _():
        def transpose_page(g, carry):
            cvt_ref[g] = cv_ref[g].astype(jnp.float32).T.astype(cvt_ref.dtype)
            return carry

        lax.fori_loop(0, pages, transpose_page, 0)

    qt = qt_ref[...] * jnp.asarray(0.125, jnp.bfloat16)
    seg_q = tok_ref[0:1, :]
    leaf = tok_ref[1:2, :]
    upper = tok_ref[2:3, :]
    root = tok_ref[3:4, :]
    for m_sc, l_sc, acc_sc in ((ma_sc, la_sc, acca_sc), (mb_sc, lb_sc, accb_sc)):
        m_sc[...] = jnp.full(m_sc.shape, FLOOR_SCORE, jnp.float32)
        l_sc[...] = jnp.zeros(l_sc.shape, jnp.float32)
        acc_sc[...] = jnp.zeros(acc_sc.shape, jnp.float32)
    col_head = lax.broadcasted_iota(jnp.int32, (kb, width), 1) // HD
    row_head = lax.broadcasted_iota(jnp.int32, (width, kb), 0) // HD
    slot = lax.broadcasted_iota(jnp.int32, (kb, 1), 0)

    def update(state, k, vt, mask):
        m_sc, l_sc, acc_sc = state
        zk = jnp.zeros_like(k)
        kbd = jnp.concatenate([jnp.where(col_head == h, k, zk) for h in range(groups)], axis=0)
        st = jnp.dot(kbd, qt, preferred_element_type=jnp.float32)
        probs = []
        scales = []
        for h in range(groups):
            s_h = jnp.where(mask, st[h * kb:(h + 1) * kb, :], FLOOR_SCORE)
            m_old = m_sc[h]
            m_new = jnp.maximum(m_old, jnp.max(s_h, axis=0, keepdims=True))
            alpha = jnp.exp(m_old - m_new)
            p_h = jnp.exp(s_h - m_new)
            l_sc[h] = alpha * l_sc[h] + jnp.sum(p_h, axis=0, keepdims=True)
            m_sc[h] = m_new
            probs.append(p_h.astype(jnp.bfloat16))
            scales.append(jnp.broadcast_to(alpha, (HD, tq)))
        zv = jnp.zeros_like(vt)
        vbdt = jnp.concatenate([jnp.where(row_head == h, vt, zv) for h in range(groups)], axis=1)
        pv = jnp.dot(vbdt, jnp.concatenate(probs, axis=0), preferred_element_type=jnp.float32)
        acc_sc[...] = acc_sc[...] * jnp.concatenate(scales, axis=0) + pv

    chain_a = (ma_sc, la_sc, acca_sc)
    chain_b = (mb_sc, lb_sc, accb_sc)
    qpos = i * tq + lax.broadcasted_iota(jnp.int32, (1, tq), 1)

    def suffix_step(b, carry):
        start = pl.multiple_of(b * kb, kb)
        kpos = start + slot
        mask = (segk_ref[pl.ds(start, kb), :] == seg_q) & (kpos <= qpos)
        update(chain_a, kn_ref[pl.ds(start, kb), :], vnt_ref[:, pl.ds(start, kb)], mask)
        return carry

    last = (i * tq + tq - 1) // kb
    lax.fori_loop(kfirst_ref[i], last + 1, suffix_step, 0)

    count = pcount_ref[i]

    def page_mask(g, valid):
        node = pnode_ref[g]
        fill = jnp.where(valid, pfill_ref[g], 0)
        tok_ok = (leaf == node) | (upper == node) | (root == node)
        return tok_ok & (slot < fill)

    def pair_step(j, carry):
        g0 = plist_ref[i * pages + 2 * j]
        g1 = plist_ref[i * pages + 2 * j + 1]
        update(chain_a, ck_ref[g0], cvt_ref[g0], page_mask(g0, True))
        update(chain_b, ck_ref[g1], cvt_ref[g1], page_mask(g1, 2 * j + 1 < count))
        return carry

    lax.fori_loop(0, (count + 1) // 2, pair_step, 0)

    parts = []
    for h in range(groups):
        m_all = jnp.maximum(ma_sc[h], mb_sc[h])
        wa = jnp.exp(ma_sc[h] - m_all)
        wb = jnp.exp(mb_sc[h] - m_all)
        l_all = la_sc[h] * wa + lb_sc[h] * wb
        rows = slice(h * HD, (h + 1) * HD)
        acc_h = acca_sc[rows, :] * wa + accb_sc[rows, :] * wb
        parts.append(acc_h / l_all)
    o_ref[...] = jnp.concatenate(parts, axis=0).astype(o_ref.dtype)


def attention(plist, pcount, page_node, page_fill, kfirst, qt, tok, proj, vnt, segk, ck, cv):
    width, tokens = qt.shape
    groups = width // HD
    nqb = tokens // Q_BLOCK
    state = [
        pltpu.VMEM((groups, 1, Q_BLOCK), jnp.float32),
        pltpu.VMEM((groups, 1, Q_BLOCK), jnp.float32),
        pltpu.VMEM((width, Q_BLOCK), jnp.float32),
    ]
    grid_spec = pltpu.PrefetchScalarGridSpec(
        num_scalar_prefetch=5,
        grid=(nqb,),
        in_specs=[
            pl.BlockSpec((width, Q_BLOCK), lambda i, *_: (0, i)),
            pl.BlockSpec((tok.shape[0], Q_BLOCK), lambda i, *_: (0, i)),
            pl.BlockSpec((tokens, width), lambda i, *_: (0, 1)),
            pl.BlockSpec(memory_space=pltpu.VMEM),
            pl.BlockSpec(memory_space=pltpu.VMEM),
            pl.BlockSpec(memory_space=pltpu.VMEM),
            pl.BlockSpec(memory_space=pltpu.VMEM),
        ],
        out_specs=pl.BlockSpec((width, Q_BLOCK), lambda i, *_: (0, i)),
        scratch_shapes=state + state + [
            pltpu.VMEM((ck.shape[0], width, ck.shape[1]), jnp.bfloat16),
        ],
    )
    return pl.pallas_call(
        attn_kernel,
        grid_spec=grid_spec,
        interpret=INTERPRET,
        out_shape=jax.ShapeDtypeStruct((width, tokens), jnp.bfloat16),
        compiler_params=pltpu.CompilerParams(
            dimension_semantics=("arbitrary",), vmem_limit_bytes=48 * 1024 * 1024
        ),
    )(plist, pcount, page_node, page_fill, kfirst, qt, tok, proj, vnt, segk, ck, cv)


def shift_perm(n, d):
    return [(j, (j + d) % n) for j in range(n)]


def head_gather(x, n):
    me = lax.axis_index("head")
    parts = [x] + [lax.ppermute(x, "head", shift_perm(n, d)) for d in range(1, n)]
    stacked = jnp.stack(parts)
    order = (me - jnp.arange(n, dtype=jnp.int32)) % n
    gathered = jnp.take(stacked, order, axis=0)
    return gathered.reshape(n * x.shape[0], x.shape[1])


def head_reduce_scatter(partial, n):
    me = lax.axis_index("head")
    rows = partial.shape[0] // n
    chunks = partial.reshape(n, rows, partial.shape[1])
    total = lax.dynamic_index_in_dim(chunks, me, 0, keepdims=False)
    for d in range(1, n):
        send = lax.dynamic_index_in_dim(chunks, (me + d) % n, 0, keepdims=False)
        recv = lax.ppermute(send.astype(jnp.bfloat16), "head", shift_perm(n, d))
        total = total + recv.astype(jnp.float32)
    return total.astype(jnp.bfloat16)


def shards(
    hidden_in,
    norm_gain,
    w_qkv,
    w_out,
    cache_kv,
    page_node,
    page_fill,
    node_parent,
    tok_seg,
    req_leaf,
):
    widened = hidden_in[0].astype(jnp.float32)
    normed = (
        widened
        * lax.rsqrt(jnp.mean(widened * widened, axis=1, keepdims=True) + EPSILON)
        * norm_gain
    ).astype(jnp.bfloat16)
    model_width = widened.shape[1]
    group_width = w_qkv.shape[2]
    weight_flat = w_qkv.reshape(model_width, 3 * group_width)
    n_head = tok_seg.shape[1] // hidden_in.shape[1]
    projected = jnp.dot(
        head_gather(normed, n_head),
        weight_flat,
        preferred_element_type=jnp.float32,
    ).astype(jnp.bfloat16)
    tokens = projected.shape[0]
    segment = tok_seg[0]
    leaf_node = lookup(segment, req_leaf[0])
    upper_node = lookup(leaf_node, node_parent)
    root_node = lookup(upper_node, node_parent)
    zero_row = jnp.zeros_like(segment)
    tok = jnp.stack(
        [segment, leaf_node, upper_node, root_node] + [zero_row] * 4, axis=0
    )
    pages = page_node.shape[0]
    seen = (
        (page_node[None, :] == leaf_node[:, None])
        | (page_node[None, :] == upper_node[:, None])
        | (page_node[None, :] == root_node[:, None])
    )
    nqb = tokens // Q_BLOCK
    vis = jnp.any(seen.reshape(nqb, Q_BLOCK, pages), axis=1).astype(jnp.int32)
    rank = jnp.cumsum(vis, axis=1) - 1
    picked = (vis[:, :, None] > 0) & (rank[:, :, None] == jnp.arange(pages)[None, None, :])
    plist = jnp.sum(
        jnp.where(picked, jnp.arange(pages, dtype=jnp.int32)[None, :, None], 0), axis=1
    ).astype(jnp.int32).reshape(-1)
    pcount = jnp.sum(vis, axis=1).astype(jnp.int32)
    first_seg = segment[::Q_BLOCK]
    kfirst = (
        jnp.sum((segment[None, :] < first_seg[:, None]).astype(jnp.int32), axis=1) // K_BLOCK
    ).astype(jnp.int32)
    segk = segment[:, None]
    qt = projected[:, :group_width].T
    vnt = projected[:, 2 * group_width:].T
    chip_cache = lax.all_gather(cache_kv, "pc", axis=1, tiled=True)
    core = lax.axis_index("pc")
    mine = lax.dynamic_index_in_dim(chip_cache, core, 0, keepdims=False)
    mine = lax.all_gather(mine, "chip", axis=0, tiled=True)
    other = lax.ppermute(mine, "pc", [(0, 1), (1, 0)])
    ck = jnp.where(core == 0, mine, other)
    cv = jnp.where(core == 0, other, mine)
    attn_t = attention(
        plist, pcount, page_node, page_fill, kfirst, qt, tok, projected, vnt, segk, ck, cv
    )
    result = head_reduce_scatter(
        lax.dot_general(
            attn_t, w_out, (((0,), (0,)), ((), ())), preferred_element_type=jnp.float32
        ),
        n_head,
    )
    return result[None]


def solution(mesh):
    devices = mesh.devices
    sub = jax.sharding.Mesh(
        devices.reshape(devices.shape[0], devices.shape[1] // 2, 2), ("head", "chip", "pc")
    )
    page = ("chip", "pc")
    placed = (
        P(page, "head", None),
        P(),
        P(None, None, "head"),
        P("head", None),
        P(None, page, None, "head"),
        P(),
        P(),
        P(),
        P(page, None),
        P(page, None),
    )
    return jax.shard_map(
        shards, mesh=sub, in_specs=placed, out_specs=P(page, "head", None), check_vma=False
    )
```

```python
import jax
import jax.numpy as jnp
from jax import lax
from jax.experimental import pallas as pl
from jax.experimental.pallas import tpu as pltpu
from jax.sharding import PartitionSpec as P

HD = 64
EPSILON = 1e-06
FLOOR_SCORE = -1e30
Q_BLOCK = 256
K_BLOCK = 128
INTERPRET = False


def lookup(indices, lookup_table):
    matches = indices[:, None] == jnp.arange(lookup_table.shape[0], dtype=jnp.int32)[None, :]
    return jnp.sum(jnp.where(matches, lookup_table[None, :], 0), axis=1)


def attn_kernel(
    plist_ref, pcount_ref, pnode_ref, pfill_ref, kfirst_ref, qsel_ref,
    qt_ref, tok_ref, kn_ref, vnt_ref, segk_ref, ck_ref, cvt_ref,
    o_ref,
    ma_sc, la_sc, acca_sc, mb_sc, lb_sc, accb_sc,
):
    i = qsel_ref[0]
    width, tq = qt_ref.shape
    groups = width // HD
    pages = ck_ref.shape[0]
    kb = ck_ref.shape[1]

    qt = qt_ref[...] * jnp.asarray(0.125, jnp.bfloat16)
    seg_q = tok_ref[0:1, :]
    leaf = tok_ref[1:2, :]
    upper = tok_ref[2:3, :]
    root = tok_ref[3:4, :]
    for m_sc, l_sc, acc_sc in ((ma_sc, la_sc, acca_sc), (mb_sc, lb_sc, accb_sc)):
        m_sc[...] = jnp.full(m_sc.shape, FLOOR_SCORE, jnp.float32)
        l_sc[...] = jnp.zeros(l_sc.shape, jnp.float32)
        acc_sc[...] = jnp.zeros(acc_sc.shape, jnp.float32)
    col_head = lax.broadcasted_iota(jnp.int32, (kb, width), 1) // HD
    row_head = lax.broadcasted_iota(jnp.int32, (width, kb), 0) // HD
    slot = lax.broadcasted_iota(jnp.int32, (kb, 1), 0)

    def update(state, k, vt, mask):
        m_sc, l_sc, acc_sc = state
        zk = jnp.zeros_like(k)
        kbd = jnp.concatenate([jnp.where(col_head == h, k, zk) for h in range(groups)], axis=0)
        st = jnp.dot(kbd, qt, preferred_element_type=jnp.float32)
        probs = []
        scales = []
        for h in range(groups):
            s_h = jnp.where(mask, st[h * kb:(h + 1) * kb, :], FLOOR_SCORE)
            m_old = m_sc[h]
            m_new = jnp.maximum(m_old, jnp.max(s_h, axis=0, keepdims=True))
            alpha = jnp.exp(m_old - m_new)
            p_h = jnp.exp(s_h - m_new)
            l_sc[h] = alpha * l_sc[h] + jnp.sum(p_h, axis=0, keepdims=True)
            m_sc[h] = m_new
            probs.append(p_h.astype(jnp.bfloat16))
            scales.append(jnp.broadcast_to(alpha, (HD, tq)))
        zv = jnp.zeros_like(vt)
        vbdt = jnp.concatenate([jnp.where(row_head == h, vt, zv) for h in range(groups)], axis=1)
        pv = jnp.dot(vbdt, jnp.concatenate(probs, axis=0), preferred_element_type=jnp.float32)
        acc_sc[...] = acc_sc[...] * jnp.concatenate(scales, axis=0) + pv

    chain_a = (ma_sc, la_sc, acca_sc)
    chain_b = (mb_sc, lb_sc, accb_sc)
    qpos = i * tq + lax.broadcasted_iota(jnp.int32, (1, tq), 1)

    def suffix_step(b, carry):
        start = pl.multiple_of(b * kb, kb)
        kpos = start + slot
        mask = (segk_ref[pl.ds(start, kb), :] == seg_q) & (kpos <= qpos)
        update(chain_a, kn_ref[pl.ds(start, kb), :], vnt_ref[:, pl.ds(start, kb)], mask)
        return carry

    last = (i * tq + tq - 1) // kb
    lax.fori_loop(kfirst_ref[i], last + 1, suffix_step, 0)

    count = pcount_ref[i]

    def page_mask(g, valid):
        node = pnode_ref[g]
        fill = jnp.where(valid, pfill_ref[g], 0)
        tok_ok = (leaf == node) | (upper == node) | (root == node)
        return tok_ok & (slot < fill)

    def pair_step(j, carry):
        g0 = plist_ref[i * pages + 2 * j]
        g1 = plist_ref[i * pages + 2 * j + 1]
        update(chain_a, ck_ref[g0], cvt_ref[g0], page_mask(g0, True))
        update(chain_b, ck_ref[g1], cvt_ref[g1], page_mask(g1, 2 * j + 1 < count))
        return carry

    lax.fori_loop(0, (count + 1) // 2, pair_step, 0)

    parts = []
    for h in range(groups):
        m_all = jnp.maximum(ma_sc[h], mb_sc[h])
        wa = jnp.exp(ma_sc[h] - m_all)
        wb = jnp.exp(mb_sc[h] - m_all)
        l_all = la_sc[h] * wa + lb_sc[h] * wb
        rows = slice(h * HD, (h + 1) * HD)
        acc_h = acca_sc[rows, :] * wa + accb_sc[rows, :] * wb
        parts.append(acc_h / l_all)
    o_ref[...] = jnp.concatenate(parts, axis=0).astype(o_ref.dtype)


def attention(plist, pcount, page_node, page_fill, kfirst, qsel, qt, tok, proj, vnt, segk, ck, cvt):
    width, tokens = qt.shape
    groups = width // HD
    state = [
        pltpu.VMEM((groups, 1, Q_BLOCK), jnp.float32),
        pltpu.VMEM((groups, 1, Q_BLOCK), jnp.float32),
        pltpu.VMEM((width, Q_BLOCK), jnp.float32),
    ]
    grid_spec = pltpu.PrefetchScalarGridSpec(
        num_scalar_prefetch=6,
        grid=(1,),
        in_specs=[
            pl.BlockSpec((width, Q_BLOCK), lambda i, *r: (0, r[5][0])),
            pl.BlockSpec((tok.shape[0], Q_BLOCK), lambda i, *r: (0, r[5][0])),
            pl.BlockSpec((tokens, width), lambda i, *r: (0, 1)),
            pl.BlockSpec(memory_space=pltpu.VMEM),
            pl.BlockSpec(memory_space=pltpu.VMEM),
            pl.BlockSpec(memory_space=pltpu.VMEM),
            pl.BlockSpec(memory_space=pltpu.VMEM),
        ],
        out_specs=pl.BlockSpec((width, Q_BLOCK), lambda i, *r: (0, 0)),
        scratch_shapes=state + state,
    )
    return pl.pallas_call(
        attn_kernel,
        grid_spec=grid_spec,
        interpret=INTERPRET,
        out_shape=jax.ShapeDtypeStruct((width, Q_BLOCK), jnp.bfloat16),
        compiler_params=pltpu.CompilerParams(
            dimension_semantics=("arbitrary",), vmem_limit_bytes=48 * 1024 * 1024
        ),
    )(plist, pcount, page_node, page_fill, kfirst, qsel, qt, tok, proj, vnt, segk, ck, cvt)


def shift_perm(n, d):
    return [(j, (j + d) % n) for j in range(n)]


def head_gather(x, n):
    me = lax.axis_index("head")
    parts = [x] + [lax.ppermute(x, "head", shift_perm(n, d)) for d in range(1, n)]
    stacked = jnp.stack(parts)
    order = (me - jnp.arange(n, dtype=jnp.int32)) % n
    gathered = jnp.take(stacked, order, axis=0)
    return gathered.reshape(n * x.shape[0], x.shape[1])


def head_reduce_scatter(partial, n):
    me = lax.axis_index("head")
    rows = partial.shape[0] // n
    chunks = partial.reshape(n, rows, partial.shape[1])
    total = lax.dynamic_index_in_dim(chunks, me, 0, keepdims=False)
    for d in range(1, n):
        send = lax.dynamic_index_in_dim(chunks, (me + d) % n, 0, keepdims=False)
        recv = lax.ppermute(send.astype(jnp.bfloat16), "head", shift_perm(n, d))
        total = total + recv.astype(jnp.float32)
    return total.astype(jnp.bfloat16)


def shards(
    hidden_in,
    norm_gain,
    w_qkv,
    w_out,
    cache_kv,
    page_node,
    page_fill,
    node_parent,
    tok_seg,
    req_leaf,
):
    widened = hidden_in[0].astype(jnp.float32)
    normed = (
        widened
        * lax.rsqrt(jnp.mean(widened * widened, axis=1, keepdims=True) + EPSILON)
        * norm_gain
    ).astype(jnp.bfloat16)
    model_width = widened.shape[1]
    group_width = w_qkv.shape[2]
    weight_flat = w_qkv.reshape(model_width, 3 * group_width)
    n_head = tok_seg.shape[1] // hidden_in.shape[1]
    projected = jnp.dot(
        head_gather(normed, n_head),
        weight_flat,
        preferred_element_type=jnp.float32,
    ).astype(jnp.bfloat16)
    tokens = projected.shape[0]
    segment = tok_seg[0]
    leaf_node = lookup(segment, req_leaf[0])
    upper_node = lookup(leaf_node, node_parent)
    root_node = lookup(upper_node, node_parent)
    zero_row = jnp.zeros_like(segment)
    tok = jnp.stack(
        [segment, leaf_node, upper_node, root_node] + [zero_row] * 4, axis=0
    )
    pages = page_node.shape[0]
    seen = (
        (page_node[None, :] == leaf_node[:, None])
        | (page_node[None, :] == upper_node[:, None])
        | (page_node[None, :] == root_node[:, None])
    )
    nqb = tokens // Q_BLOCK
    vis = jnp.any(seen.reshape(nqb, Q_BLOCK, pages), axis=1).astype(jnp.int32)
    rank = jnp.cumsum(vis, axis=1) - 1
    picked = (vis[:, :, None] > 0) & (rank[:, :, None] == jnp.arange(pages)[None, None, :])
    plist = jnp.sum(
        jnp.where(picked, jnp.arange(pages, dtype=jnp.int32)[None, :, None], 0), axis=1
    ).astype(jnp.int32).reshape(-1)
    pcount = jnp.sum(vis, axis=1).astype(jnp.int32)
    first_seg = segment[::Q_BLOCK]
    kfirst = (
        jnp.sum((segment[None, :] < first_seg[:, None]).astype(jnp.int32), axis=1) // K_BLOCK
    ).astype(jnp.int32)
    segk = segment[:, None]
    qt = projected[:, :group_width].T
    vnt = projected[:, 2 * group_width:].T
    cache = lax.all_gather(cache_kv, "page", axis=1, tiled=True)
    ck = cache[0]
    cvt = jnp.swapaxes(cache[1], 1, 2)
    me = lax.axis_index("head")
    total = None
    received = []
    for d in list(range(1, n_head)) + [0]:
        block = ((me + d) % n_head).astype(jnp.int32)[None]
        attn_t = attention(
            plist, pcount, page_node, page_fill, kfirst, block, qt, tok, projected, vnt, segk,
            ck, cvt,
        )
        partial = lax.dot_general(
            attn_t, w_out, (((0,), (0,)), ((), ())), preferred_element_type=jnp.float32
        )
        if d == 0:
            total = partial
        else:
            send, qt = lax.optimization_barrier((partial.astype(jnp.bfloat16), qt))
            received.append(lax.ppermute(send, "head", shift_perm(n_head, d)))
    for recv in received:
        total = total + recv.astype(jnp.float32)
    return total.astype(jnp.bfloat16)[None]


def solution(mesh):
    placed = (
        P("page", "head", None),
        P(),
        P(None, None, "head"),
        P("head", None),
        P(None, "page", None, "head"),
        P(),
        P(),
        P(),
        P("page", None),
        P("page", None),
    )
    return jax.shard_map(
        shards, mesh=mesh, in_specs=placed, out_specs=P("page", "head", None), check_vma=False
    )
```

```python
import jax
import jax.numpy as jnp
from jax import lax
from jax.experimental import pallas as pl
from jax.experimental.pallas import tpu as pltpu
from jax.sharding import PartitionSpec as P

HD = 64
EPSILON = 1e-06
FLOOR_SCORE = -1e30
Q_BLOCK = 512
K_BLOCK = 128
INTERPRET = False


def lookup(indices, lookup_table):
    matches = indices[:, None] == jnp.arange(lookup_table.shape[0], dtype=jnp.int32)[None, :]
    return jnp.sum(jnp.where(matches, lookup_table[None, :], 0), axis=1)


def attn_kernel(
    plist_ref, pcount_ref, pnode_ref, pfill_ref, kfirst_ref,
    qt_ref, tok_ref, kn_ref, vnt_ref, segk_ref, cache_ref,
    o_ref,
    ma_sc, la_sc, acca_sc, mb_sc, lb_sc, accb_sc, cvt_ref,
):
    i = pl.program_id(0)
    width, tq = qt_ref.shape
    groups = width // HD
    pages = cache_ref.shape[1]
    kb = cache_ref.shape[2]

    @pl.when(i == 0)
    def _():
        def transpose_page(g, carry):
            cvt_ref[g] = cache_ref[1, g].astype(jnp.float32).T.astype(cvt_ref.dtype)
            return carry

        lax.fori_loop(0, pages, transpose_page, 0)

    qt = qt_ref[...] * jnp.asarray(0.125, jnp.bfloat16)
    seg_q = tok_ref[0:1, :]
    leaf = tok_ref[1:2, :]
    upper = tok_ref[2:3, :]
    root = tok_ref[3:4, :]
    for m_sc, l_sc, acc_sc in ((ma_sc, la_sc, acca_sc), (mb_sc, lb_sc, accb_sc)):
        m_sc[...] = jnp.full(m_sc.shape, FLOOR_SCORE, jnp.float32)
        l_sc[...] = jnp.zeros(l_sc.shape, jnp.float32)
        acc_sc[...] = jnp.zeros(acc_sc.shape, jnp.float32)
    col_head = lax.broadcasted_iota(jnp.int32, (kb, width), 1) // HD
    row_head = lax.broadcasted_iota(jnp.int32, (width, kb), 0) // HD
    slot = lax.broadcasted_iota(jnp.int32, (kb, 1), 0)

    def update(state, k, vt, mask):
        m_sc, l_sc, acc_sc = state
        zk = jnp.zeros_like(k)
        kbd = jnp.concatenate([jnp.where(col_head == h, k, zk) for h in range(groups)], axis=0)
        st = jnp.dot(kbd, qt, preferred_element_type=jnp.float32)
        probs = []
        scales = []
        for h in range(groups):
            s_h = jnp.where(mask, st[h * kb:(h + 1) * kb, :], FLOOR_SCORE)
            m_old = m_sc[h]
            m_new = jnp.maximum(m_old, jnp.max(s_h, axis=0, keepdims=True))
            alpha = jnp.exp(m_old - m_new)
            p_h = jnp.exp(s_h - m_new)
            l_sc[h] = alpha * l_sc[h] + jnp.sum(p_h, axis=0, keepdims=True)
            m_sc[h] = m_new
            probs.append(p_h.astype(jnp.bfloat16))
            scales.append(jnp.broadcast_to(alpha, (HD, tq)))
        zv = jnp.zeros_like(vt)
        vbdt = jnp.concatenate([jnp.where(row_head == h, vt, zv) for h in range(groups)], axis=1)
        pv = jnp.dot(vbdt, jnp.concatenate(probs, axis=0), preferred_element_type=jnp.float32)
        acc_sc[...] = acc_sc[...] * jnp.concatenate(scales, axis=0) + pv

    chain_a = (ma_sc, la_sc, acca_sc)
    chain_b = (mb_sc, lb_sc, accb_sc)
    qpos = i * tq + lax.broadcasted_iota(jnp.int32, (1, tq), 1)

    def suffix_step(b, carry):
        start = pl.multiple_of(b * kb, kb)
        kpos = start + slot
        mask = (segk_ref[pl.ds(start, kb), :] == seg_q) & (kpos <= qpos)
        update(chain_a, kn_ref[pl.ds(start, kb), :], vnt_ref[:, pl.ds(start, kb)], mask)
        return carry

    last = (i * tq + tq - 1) // kb
    lax.fori_loop(kfirst_ref[i], last + 1, suffix_step, 0)

    count = pcount_ref[i]

    def page_mask(g, valid):
        node = pnode_ref[g]
        fill = jnp.where(valid, pfill_ref[g], 0)
        tok_ok = (leaf == node) | (upper == node) | (root == node)
        return tok_ok & (slot < fill)

    def pair_step(j, carry):
        g0 = plist_ref[i * pages + 2 * j]
        g1 = plist_ref[i * pages + 2 * j + 1]
        update(chain_a, cache_ref[0, g0], cvt_ref[g0], page_mask(g0, True))
        update(chain_b, cache_ref[0, g1], cvt_ref[g1], page_mask(g1, 2 * j + 1 < count))
        return carry

    lax.fori_loop(0, (count + 1) // 2, pair_step, 0)

    parts = []
    for h in range(groups):
        m_all = jnp.maximum(ma_sc[h], mb_sc[h])
        wa = jnp.exp(ma_sc[h] - m_all)
        wb = jnp.exp(mb_sc[h] - m_all)
        l_all = la_sc[h] * wa + lb_sc[h] * wb
        rows = slice(h * HD, (h + 1) * HD)
        acc_h = acca_sc[rows, :] * wa + accb_sc[rows, :] * wb
        parts.append(acc_h / l_all)
    o_ref[...] = jnp.concatenate(parts, axis=0).astype(o_ref.dtype)


def attention(plist, pcount, page_node, page_fill, kfirst, qt, tok, proj, vnt, segk, cache):
    width, tokens = qt.shape
    groups = width // HD
    nqb = tokens // Q_BLOCK
    state = [
        pltpu.VMEM((groups, 1, Q_BLOCK), jnp.float32),
        pltpu.VMEM((groups, 1, Q_BLOCK), jnp.float32),
        pltpu.VMEM((width, Q_BLOCK), jnp.float32),
    ]
    grid_spec = pltpu.PrefetchScalarGridSpec(
        num_scalar_prefetch=5,
        grid=(nqb,),
        in_specs=[
            pl.BlockSpec((width, Q_BLOCK), lambda i, *_: (0, i)),
            pl.BlockSpec((tok.shape[0], Q_BLOCK), lambda i, *_: (0, i)),
            pl.BlockSpec((tokens, width), lambda i, *_: (0, 1)),
            pl.BlockSpec(memory_space=pltpu.VMEM),
            pl.BlockSpec(memory_space=pltpu.VMEM),
            pl.BlockSpec(memory_space=pltpu.VMEM),
        ],
        out_specs=pl.BlockSpec((width, Q_BLOCK), lambda i, *_: (0, i)),
        scratch_shapes=state + state + [
            pltpu.VMEM((cache.shape[1], width, cache.shape[2]), jnp.bfloat16),
        ],
    )
    return pl.pallas_call(
        attn_kernel,
        grid_spec=grid_spec,
        interpret=INTERPRET,
        out_shape=jax.ShapeDtypeStruct((width, tokens), jnp.bfloat16),
        compiler_params=pltpu.CompilerParams(
            dimension_semantics=("arbitrary",), vmem_limit_bytes=48 * 1024 * 1024
        ),
    )(plist, pcount, page_node, page_fill, kfirst, qt, tok, proj, vnt, segk, cache)


def shift_perm(n, d):
    return [(j, (j + d) % n) for j in range(n)]


def head_gather(x, n):
    me = lax.axis_index("head")
    parts = [x] + [lax.ppermute(x, "head", shift_perm(n, d)) for d in range(1, n)]
    stacked = jnp.stack(parts)
    order = (me - jnp.arange(n, dtype=jnp.int32)) % n
    gathered = jnp.take(stacked, order, axis=0)
    return gathered.reshape(n * x.shape[0], x.shape[1])


def head_reduce_scatter(partial, n):
    me = lax.axis_index("head")
    rows = partial.shape[0] // n
    chunks = partial.reshape(n, rows, partial.shape[1])
    total = lax.dynamic_index_in_dim(chunks, me, 0, keepdims=False)
    for d in range(1, n):
        send = lax.dynamic_index_in_dim(chunks, (me + d) % n, 0, keepdims=False)
        recv = lax.ppermute(send.astype(jnp.bfloat16), "head", shift_perm(n, d))
        total = total + recv.astype(jnp.float32)
    return total.astype(jnp.bfloat16)


def shards(
    hidden_in,
    norm_gain,
    w_qkv,
    w_out,
    cache_kv,
    page_node,
    page_fill,
    node_parent,
    tok_seg,
    req_leaf,
):
    widened = hidden_in[0].astype(jnp.float32)
    normed = (
        widened
        * lax.rsqrt(jnp.mean(widened * widened, axis=1, keepdims=True) + EPSILON)
        * norm_gain
    ).astype(jnp.bfloat16)
    model_width = widened.shape[1]
    group_width = w_qkv.shape[2]
    weight_flat = w_qkv.reshape(model_width, 3 * group_width)
    n_head = tok_seg.shape[1] // hidden_in.shape[1]
    projected = jnp.dot(
        head_gather(normed, n_head),
        weight_flat,
        preferred_element_type=jnp.float32,
    ).astype(jnp.bfloat16)
    tokens = projected.shape[0]
    segment = tok_seg[0]
    leaf_node = lookup(segment, req_leaf[0])
    upper_node = lookup(leaf_node, node_parent)
    root_node = lookup(upper_node, node_parent)
    zero_row = jnp.zeros_like(segment)
    tok = jnp.stack(
        [segment, leaf_node, upper_node, root_node] + [zero_row] * 4, axis=0
    )
    pages = page_node.shape[0]
    seen = (
        (page_node[None, :] == leaf_node[:, None])
        | (page_node[None, :] == upper_node[:, None])
        | (page_node[None, :] == root_node[:, None])
    )
    nqb = tokens // Q_BLOCK
    vis = jnp.any(seen.reshape(nqb, Q_BLOCK, pages), axis=1).astype(jnp.int32)
    rank = jnp.cumsum(vis, axis=1) - 1
    picked = (vis[:, :, None] > 0) & (rank[:, :, None] == jnp.arange(pages)[None, None, :])
    plist = jnp.sum(
        jnp.where(picked, jnp.arange(pages, dtype=jnp.int32)[None, :, None], 0), axis=1
    ).astype(jnp.int32).reshape(-1)
    pcount = jnp.sum(vis, axis=1).astype(jnp.int32)
    first_seg = segment[::Q_BLOCK]
    kfirst = (
        jnp.sum((segment[None, :] < first_seg[:, None]).astype(jnp.int32), axis=1) // K_BLOCK
    ).astype(jnp.int32)
    segk = segment[:, None]
    qt = projected[:, :group_width].T
    vnt = projected[:, 2 * group_width:].T
    cache = lax.all_gather(cache_kv, "page", axis=1, tiled=True)
    attn_t = attention(
        plist, pcount, page_node, page_fill, kfirst, qt, tok, projected, vnt, segk, cache
    )
    result = head_reduce_scatter(
        lax.dot_general(
            attn_t, w_out, (((0,), (0,)), ((), ())), preferred_element_type=jnp.float32
        ),
        n_head,
    )
    return result[None]


def solution(mesh):
    placed = (
        P("page", "head", None),
        P(),
        P(None, None, "head"),
        P("head", None),
        P(None, "page", None, "head"),
        P(),
        P(),
        P(),
        P("page", None),
        P("page", None),
    )
    return jax.shard_map(
        shards, mesh=mesh, in_specs=placed, out_specs=P("page", "head", None), check_vma=False
    )
```

```python
import jax
import jax.numpy as jnp
from jax import lax
from jax.experimental import pallas as pl
from jax.experimental.pallas import tpu as pltpu
from jax.sharding import PartitionSpec as P


HD = 64
EPSILON = 1e-06
FLOOR_SCORE = -1e30
Q_BLOCK = 256
K_BLOCK = 128
INTERPRET = False


def lookup(indices, lookup_table):
    matches = indices[:, None] == jnp.arange(lookup_table.shape[0], dtype=jnp.int32)[None, :]
    return jnp.sum(jnp.where(matches, lookup_table[None, :], 0), axis=1)


def attn_kernel(
    plist_ref, pcount_ref, pnode_ref, pfill_ref, kfirst_ref, qsel_ref,
    qt_ref, tok_ref, kn_ref, vnt_ref, segk_ref, cache_ref, cvt_ref,
    o_ref,
    ma_sc, la_sc, acca_sc, mb_sc, lb_sc, accb_sc,
):
    i = qsel_ref[0]
    width, tq = qt_ref.shape
    groups = width // HD
    pages = cache_ref.shape[1]
    kb = cache_ref.shape[2]

    qt = qt_ref[...] * jnp.asarray(0.125, jnp.bfloat16)
    seg_q = tok_ref[0:1, :]
    leaf = tok_ref[1:2, :]
    upper = tok_ref[2:3, :]
    root = tok_ref[3:4, :]
    for m_sc, l_sc, acc_sc in ((ma_sc, la_sc, acca_sc), (mb_sc, lb_sc, accb_sc)):
        m_sc[...] = jnp.full(m_sc.shape, FLOOR_SCORE, jnp.float32)
        l_sc[...] = jnp.zeros(l_sc.shape, jnp.float32)
        acc_sc[...] = jnp.zeros(acc_sc.shape, jnp.float32)
    col_head = lax.broadcasted_iota(jnp.int32, (kb, width), 1) // HD
    row_head = lax.broadcasted_iota(jnp.int32, (width, kb), 0) // HD
    slot = lax.broadcasted_iota(jnp.int32, (kb, 1), 0)

    def update(state, k, vt, mask):
        m_sc, l_sc, acc_sc = state
        zk = jnp.zeros_like(k)
        kbd = jnp.concatenate([jnp.where(col_head == h, k, zk) for h in range(groups)], axis=0)
        st = jnp.dot(kbd, qt, preferred_element_type=jnp.float32)
        probs = []
        scales = []
        for h in range(groups):
            s_h = jnp.where(mask, st[h * kb:(h + 1) * kb, :], FLOOR_SCORE)
            m_old = m_sc[h]
            m_new = jnp.maximum(m_old, jnp.max(s_h, axis=0, keepdims=True))
            alpha = jnp.exp(m_old - m_new)
            p_h = jnp.exp(s_h - m_new)
            l_sc[h] = alpha * l_sc[h] + jnp.sum(p_h, axis=0, keepdims=True)
            m_sc[h] = m_new
            probs.append(p_h.astype(jnp.bfloat16))
            scales.append(jnp.broadcast_to(alpha, (HD, tq)))
        zv = jnp.zeros_like(vt)
        vbdt = jnp.concatenate([jnp.where(row_head == h, vt, zv) for h in range(groups)], axis=1)
        pv = jnp.dot(vbdt, jnp.concatenate(probs, axis=0), preferred_element_type=jnp.float32)
        acc_sc[...] = acc_sc[...] * jnp.concatenate(scales, axis=0) + pv

    chain_a = (ma_sc, la_sc, acca_sc)
    chain_b = (mb_sc, lb_sc, accb_sc)
    qpos = i * tq + lax.broadcasted_iota(jnp.int32, (1, tq), 1)

    def suffix_step(b, carry):
        start = pl.multiple_of(b * kb, kb)
        kpos = start + slot
        mask = (segk_ref[pl.ds(start, kb), :] == seg_q) & (kpos <= qpos)
        update(chain_a, kn_ref[pl.ds(start, kb), :], vnt_ref[:, pl.ds(start, kb)], mask)
        return carry

    last = (i * tq + tq - 1) // kb
    lax.fori_loop(kfirst_ref[i], last + 1, suffix_step, 0)

    count = pcount_ref[i]

    def page_mask(g, valid):
        node = pnode_ref[g]
        fill = jnp.where(valid, pfill_ref[g], 0)
        tok_ok = (leaf == node) | (upper == node) | (root == node)
        return tok_ok & (slot < fill)

    def pair_step(j, carry):
        g0 = plist_ref[i * pages + 2 * j]
        g1 = plist_ref[i * pages + 2 * j + 1]
        update(chain_a, cache_ref[0, g0], cvt_ref[g0], page_mask(g0, True))
        update(chain_b, cache_ref[0, g1], cvt_ref[g1], page_mask(g1, 2 * j + 1 < count))
        return carry

    lax.fori_loop(0, (count + 1) // 2, pair_step, 0)

    parts = []
    for h in range(groups):
        m_all = jnp.maximum(ma_sc[h], mb_sc[h])
        wa = jnp.exp(ma_sc[h] - m_all)
        wb = jnp.exp(mb_sc[h] - m_all)
        l_all = la_sc[h] * wa + lb_sc[h] * wb
        rows = slice(h * HD, (h + 1) * HD)
        acc_h = acca_sc[rows, :] * wa + accb_sc[rows, :] * wb
        parts.append(acc_h / l_all)
    o_ref[...] = jnp.concatenate(parts, axis=0).astype(o_ref.dtype)


def attention(plist, pcount, page_node, page_fill, kfirst, qsel, qt, tok, proj, vnt, segk, cache, cvt):
    width, tokens = qt.shape
    groups = width // HD
    state = [
        pltpu.VMEM((groups, 1, Q_BLOCK), jnp.float32),
        pltpu.VMEM((groups, 1, Q_BLOCK), jnp.float32),
        pltpu.VMEM((width, Q_BLOCK), jnp.float32),
    ]
    grid_spec = pltpu.PrefetchScalarGridSpec(
        num_scalar_prefetch=6,
        grid=(1,),
        in_specs=[
            pl.BlockSpec((width, Q_BLOCK), lambda i, *r: (0, r[5][0])),
            pl.BlockSpec((tok.shape[0], Q_BLOCK), lambda i, *r: (0, r[5][0])),
            pl.BlockSpec((tokens, width), lambda i, *r: (0, 1)),
            pl.BlockSpec(memory_space=pltpu.VMEM),
            pl.BlockSpec(memory_space=pltpu.VMEM),
            pl.BlockSpec(memory_space=pltpu.VMEM),
            pl.BlockSpec(memory_space=pltpu.VMEM),
        ],
        out_specs=pl.BlockSpec((width, Q_BLOCK), lambda i, *r: (0, 0)),
        scratch_shapes=state + state,
    )
    return pl.pallas_call(
        attn_kernel,
        grid_spec=grid_spec,
        interpret=INTERPRET,
        out_shape=jax.ShapeDtypeStruct((width, Q_BLOCK), jnp.bfloat16),
        compiler_params=pltpu.CompilerParams(
            dimension_semantics=("arbitrary",), vmem_limit_bytes=48 * 1024 * 1024
        ),
    )(plist, pcount, page_node, page_fill, kfirst, qsel, qt, tok, proj, vnt, segk, cache, cvt)


def transpose_kernel(v_ref, o_ref):
    o_ref[0] = v_ref[0, 0].astype(jnp.float32).T.astype(o_ref.dtype)


def transpose_values(cache):
    pages, kb, width = cache.shape[1:]
    return pl.pallas_call(
        transpose_kernel,
        grid=(pages,),
        in_specs=[pl.BlockSpec((1, 1, kb, width), lambda g: (1, g, 0, 0))],
        out_specs=pl.BlockSpec((1, width, kb), lambda g: (g, 0, 0)),
        out_shape=jax.ShapeDtypeStruct((pages, width, kb), cache.dtype),
        interpret=INTERPRET,
    )(cache)


def shift_perm(n, d):
    return [(j, (j + d) % n) for j in range(n)]


def head_gather(x, n):
    me = lax.axis_index("head")
    parts = [x] + [lax.ppermute(x, "head", shift_perm(n, d)) for d in range(1, n)]
    stacked = jnp.stack(parts)
    order = (me - jnp.arange(n, dtype=jnp.int32)) % n
    gathered = jnp.take(stacked, order, axis=0)
    return gathered.reshape(n * x.shape[0], x.shape[1])


def shards_body(
    hidden_in,
    norm_gain,
    w_qkv,
    w_out,
    cache_kv,
    page_node,
    page_fill,
    node_parent,
    tok_seg,
    req_leaf,
):
    widened = hidden_in[0].astype(jnp.float32)
    normed = (
        widened
        * lax.rsqrt(jnp.mean(widened * widened, axis=1, keepdims=True) + EPSILON)
        * norm_gain
    ).astype(jnp.bfloat16)
    model_width = widened.shape[1]
    group_width = w_qkv.shape[2]
    weight_flat = w_qkv.reshape(model_width, 3 * group_width)
    n_head = tok_seg.shape[1] // hidden_in.shape[1]
    projected = jnp.dot(
        head_gather(normed, n_head),
        weight_flat,
        preferred_element_type=jnp.float32,
    ).astype(jnp.bfloat16)
    tokens = projected.shape[0]
    segment = tok_seg[0]
    leaf_node = lookup(segment, req_leaf[0])
    upper_node = lookup(leaf_node, node_parent)
    root_node = lookup(upper_node, node_parent)
    zero_row = jnp.zeros_like(segment)
    tok = jnp.stack(
        [segment, leaf_node, upper_node, root_node] + [zero_row] * 4, axis=0
    )
    pages = page_node.shape[0]
    seen = (
        (page_node[None, :] == leaf_node[:, None])
        | (page_node[None, :] == upper_node[:, None])
        | (page_node[None, :] == root_node[:, None])
    )
    nqb = tokens // Q_BLOCK
    vis = jnp.any(seen.reshape(nqb, Q_BLOCK, pages), axis=1).astype(jnp.int32)
    rank = jnp.cumsum(vis, axis=1) - 1
    picked = (vis[:, :, None] > 0) & (rank[:, :, None] == jnp.arange(pages)[None, None, :])
    plist = jnp.sum(
        jnp.where(picked, jnp.arange(pages, dtype=jnp.int32)[None, :, None], 0), axis=1
    ).astype(jnp.int32).reshape(-1)
    pcount = jnp.sum(vis, axis=1).astype(jnp.int32)
    first_seg = segment[::Q_BLOCK]
    kfirst = (
        jnp.sum((segment[None, :] < first_seg[:, None]).astype(jnp.int32), axis=1) // K_BLOCK
    ).astype(jnp.int32)
    segk = segment[:, None]
    qt = projected[:, :group_width].T
    vnt = projected[:, 2 * group_width:].T
    cache = lax.all_gather(cache_kv, "page", axis=1, tiled=True)
    cvt = transpose_values(cache)
    me = lax.axis_index("head")
    total = None
    received = []
    for d in list(range(1, n_head)) + [0]:
        block = ((me + d) % n_head).astype(jnp.int32)[None]
        attn_t = attention(
            plist, pcount, page_node, page_fill, kfirst, block, qt, tok, projected, vnt,
            segk, cache, cvt,
        )
        partial = lax.dot_general(
            attn_t, w_out, (((0,), (0,)), ((), ())), preferred_element_type=jnp.float32
        )
        if d == 0:
            total = partial
        else:
            send, qt = lax.optimization_barrier((partial.astype(jnp.bfloat16), qt))
            received.append(lax.ppermute(send, "head", shift_perm(n_head, d)))
    for recv in received:
        total = total + recv.astype(jnp.float32)
    return total.astype(jnp.bfloat16)[None]


def solution(mesh):
    placed = (
        P("page", "head", None),
        P(),
        P(None, None, "head"),
        P("head", None),
        P(None, "page", None, "head"),
        P(),
        P(),
        P(),
        P("page", None),
        P("page", None),
    )
    return jax.shard_map(
        shards_body, mesh=mesh, in_specs=placed, out_specs=P("page", "head", None), check_vma=False
    )
```

```python
import jax
import jax.numpy as jnp
from jax import lax
from jax.experimental import pallas as pl
from jax.experimental.pallas import tpu as pltpu
from jax.sharding import PartitionSpec as P


HD = 64
EPSILON = 1e-06
FLOOR_SCORE = -1e30
Q_BLOCK = 256
K_BLOCK = 128
INTERPRET = False


def lookup(indices, lookup_table):
    matches = indices[:, None] == jnp.arange(lookup_table.shape[0], dtype=jnp.int32)[None, :]
    return jnp.sum(jnp.where(matches, lookup_table[None, :], 0), axis=1)


def attn_kernel(
    plist_ref, pcount_ref, pnode_ref, pfill_ref, kfirst_ref, qsel_ref,
    qt_ref, tok_ref, kn_ref, vnt_ref, segk_ref, cache_ref, cvt_ref,
    o_ref,
    ma_sc, la_sc, acca_sc, mb_sc, lb_sc, accb_sc,
):
    i = qsel_ref[0]
    width, tq = qt_ref.shape
    groups = width // HD
    pages = cache_ref.shape[1]
    kb = cache_ref.shape[2]

    qt = qt_ref[...] * jnp.asarray(0.125, jnp.bfloat16)
    seg_q = tok_ref[0:1, :]
    leaf = tok_ref[1:2, :]
    upper = tok_ref[2:3, :]
    root = tok_ref[3:4, :]
    for m_sc, l_sc, acc_sc in ((ma_sc, la_sc, acca_sc), (mb_sc, lb_sc, accb_sc)):
        m_sc[...] = jnp.full(m_sc.shape, FLOOR_SCORE, jnp.float32)
        l_sc[...] = jnp.zeros(l_sc.shape, jnp.float32)
        acc_sc[...] = jnp.zeros(acc_sc.shape, jnp.float32)
    col_head = lax.broadcasted_iota(jnp.int32, (kb, width), 1) // HD
    row_head = lax.broadcasted_iota(jnp.int32, (width, kb), 0) // HD
    slot = lax.broadcasted_iota(jnp.int32, (kb, 1), 0)

    def update(state, k, vt, mask):
        m_sc, l_sc, acc_sc = state
        zk = jnp.zeros_like(k)
        kbd = jnp.concatenate([jnp.where(col_head == h, k, zk) for h in range(groups)], axis=0)
        st = jnp.dot(kbd, qt, preferred_element_type=jnp.float32)
        probs = []
        scales = []
        for h in range(groups):
            s_h = jnp.where(mask, st[h * kb:(h + 1) * kb, :], FLOOR_SCORE)
            m_old = m_sc[h]
            m_new = jnp.maximum(m_old, jnp.max(s_h, axis=0, keepdims=True))
            alpha = jnp.exp(m_old - m_new)
            p_h = jnp.exp(s_h - m_new)
            l_sc[h] = alpha * l_sc[h] + jnp.sum(p_h, axis=0, keepdims=True)
            m_sc[h] = m_new
            probs.append(p_h.astype(jnp.bfloat16))
            scales.append(jnp.broadcast_to(alpha, (HD, tq)))
        zv = jnp.zeros_like(vt)
        vbdt = jnp.concatenate([jnp.where(row_head == h, vt, zv) for h in range(groups)], axis=1)
        pv = jnp.dot(vbdt, jnp.concatenate(probs, axis=0), preferred_element_type=jnp.float32)
        acc_sc[...] = acc_sc[...] * jnp.concatenate(scales, axis=0) + pv

    chain_a = (ma_sc, la_sc, acca_sc)
    chain_b = (mb_sc, lb_sc, accb_sc)
    qpos = i * tq + lax.broadcasted_iota(jnp.int32, (1, tq), 1)

    def suffix_step(b, carry):
        start = pl.multiple_of(b * kb, kb)
        kpos = start + slot
        mask = (segk_ref[pl.ds(start, kb), :] == seg_q) & (kpos <= qpos)
        update(chain_a, kn_ref[pl.ds(start, kb), :], vnt_ref[:, pl.ds(start, kb)], mask)
        return carry

    last = (i * tq + tq - 1) // kb
    lax.fori_loop(kfirst_ref[i], last + 1, suffix_step, 0)

    count = pcount_ref[i]

    def page_mask(g, valid):
        node = pnode_ref[g]
        fill = jnp.where(valid, pfill_ref[g], 0)
        tok_ok = (leaf == node) | (upper == node) | (root == node)
        return tok_ok & (slot < fill)

    def pair_step(j, carry):
        g0 = plist_ref[i * pages + 2 * j]
        g1 = plist_ref[i * pages + 2 * j + 1]
        update(chain_a, cache_ref[0, g0], cvt_ref[g0], page_mask(g0, True))
        update(chain_b, cache_ref[0, g1], cvt_ref[g1], page_mask(g1, 2 * j + 1 < count))
        return carry

    lax.fori_loop(0, (count + 1) // 2, pair_step, 0)

    parts = []
    for h in range(groups):
        m_all = jnp.maximum(ma_sc[h], mb_sc[h])
        wa = jnp.exp(ma_sc[h] - m_all)
        wb = jnp.exp(mb_sc[h] - m_all)
        l_all = la_sc[h] * wa + lb_sc[h] * wb
        rows = slice(h * HD, (h + 1) * HD)
        acc_h = acca_sc[rows, :] * wa + accb_sc[rows, :] * wb
        parts.append(acc_h / l_all)
    o_ref[...] = jnp.concatenate(parts, axis=0).astype(o_ref.dtype)


def attention(plist, pcount, page_node, page_fill, kfirst, qsel, qt, tok, proj, vnt, segk, cache, cvt):
    width, tokens = qt.shape
    groups = width // HD
    state = [
        pltpu.VMEM((groups, 1, Q_BLOCK), jnp.float32),
        pltpu.VMEM((groups, 1, Q_BLOCK), jnp.float32),
        pltpu.VMEM((width, Q_BLOCK), jnp.float32),
    ]
    grid_spec = pltpu.PrefetchScalarGridSpec(
        num_scalar_prefetch=6,
        grid=(1,),
        in_specs=[
            pl.BlockSpec((width, Q_BLOCK), lambda i, *r: (0, r[5][0])),
            pl.BlockSpec((tok.shape[0], Q_BLOCK), lambda i, *r: (0, r[5][0])),
            pl.BlockSpec((tokens, width), lambda i, *r: (0, 1)),
            pl.BlockSpec(memory_space=pltpu.VMEM),
            pl.BlockSpec(memory_space=pltpu.VMEM),
            pl.BlockSpec((1,) + cache.shape[1:], lambda i, *r: (0, 0, 0, 0)),
            pl.BlockSpec(memory_space=pltpu.VMEM),
        ],
        out_specs=pl.BlockSpec((width, Q_BLOCK), lambda i, *r: (0, 0)),
        scratch_shapes=state + state,
    )
    return pl.pallas_call(
        attn_kernel,
        grid_spec=grid_spec,
        interpret=INTERPRET,
        out_shape=jax.ShapeDtypeStruct((width, Q_BLOCK), jnp.bfloat16),
        compiler_params=pltpu.CompilerParams(
            dimension_semantics=("arbitrary",), vmem_limit_bytes=48 * 1024 * 1024
        ),
    )(plist, pcount, page_node, page_fill, kfirst, qsel, qt, tok, proj, vnt, segk, cache, cvt)


def transpose_kernel(v_ref, o_ref):
    def page(g, carry):
        o_ref[g] = v_ref[0, g].astype(jnp.float32).T.astype(o_ref.dtype)
        return carry

    lax.fori_loop(0, o_ref.shape[0], page, 0)


def transpose_values(cache):
    pages, kb, width = cache.shape[1:]
    return pl.pallas_call(
        transpose_kernel,
        grid=(1,),
        in_specs=[pl.BlockSpec((1, pages, kb, width), lambda g: (1, 0, 0, 0))],
        out_specs=pl.BlockSpec((pages, width, kb), lambda g: (0, 0, 0)),
        out_shape=jax.ShapeDtypeStruct((pages, width, kb), cache.dtype),
        compiler_params=pltpu.CompilerParams(vmem_limit_bytes=48 * 1024 * 1024),
        interpret=INTERPRET,
    )(cache)


def shift_perm(n, d):
    return [(j, (j + d) % n) for j in range(n)]


def head_gather(x, n):
    me = lax.axis_index("head")
    parts = [x] + [lax.ppermute(x, "head", shift_perm(n, d)) for d in range(1, n)]
    stacked = jnp.stack(parts)
    order = (me - jnp.arange(n, dtype=jnp.int32)) % n
    gathered = jnp.take(stacked, order, axis=0)
    return gathered.reshape(n * x.shape[0], x.shape[1])


def shards_body(
    hidden_in,
    norm_gain,
    w_qkv,
    w_out,
    cache_kv,
    page_node,
    page_fill,
    node_parent,
    tok_seg,
    req_leaf,
):
    widened = hidden_in[0].astype(jnp.float32)
    normed = (
        widened
        * lax.rsqrt(jnp.mean(widened * widened, axis=1, keepdims=True) + EPSILON)
        * norm_gain
    ).astype(jnp.bfloat16)
    model_width = widened.shape[1]
    group_width = w_qkv.shape[2]
    weight_flat = w_qkv.reshape(model_width, 3 * group_width)
    n_head = tok_seg.shape[1] // hidden_in.shape[1]
    projected = jnp.dot(
        head_gather(normed, n_head),
        weight_flat,
        preferred_element_type=jnp.float32,
    ).astype(jnp.bfloat16)
    tokens = projected.shape[0]
    segment = tok_seg[0]
    leaf_node = lookup(segment, req_leaf[0])
    upper_node = lookup(leaf_node, node_parent)
    root_node = lookup(upper_node, node_parent)
    zero_row = jnp.zeros_like(segment)
    tok = jnp.stack(
        [segment, leaf_node, upper_node, root_node] + [zero_row] * 4, axis=0
    )
    pages = page_node.shape[0]
    seen = (
        (page_node[None, :] == leaf_node[:, None])
        | (page_node[None, :] == upper_node[:, None])
        | (page_node[None, :] == root_node[:, None])
    )
    nqb = tokens // Q_BLOCK
    vis = jnp.any(seen.reshape(nqb, Q_BLOCK, pages), axis=1).astype(jnp.int32)
    rank = jnp.cumsum(vis, axis=1) - 1
    picked = (vis[:, :, None] > 0) & (rank[:, :, None] == jnp.arange(pages)[None, None, :])
    plist = jnp.sum(
        jnp.where(picked, jnp.arange(pages, dtype=jnp.int32)[None, :, None], 0), axis=1
    ).astype(jnp.int32).reshape(-1)
    pcount = jnp.sum(vis, axis=1).astype(jnp.int32)
    first_seg = segment[::Q_BLOCK]
    kfirst = (
        jnp.sum((segment[None, :] < first_seg[:, None]).astype(jnp.int32), axis=1) // K_BLOCK
    ).astype(jnp.int32)
    segk = segment[:, None]
    qt = projected[:, :group_width].T
    vnt = projected[:, 2 * group_width:].T
    cache = lax.all_gather(cache_kv, "page", axis=1, tiled=True)
    cvt = transpose_values(cache)
    me = lax.axis_index("head")
    total = None
    received = []
    for d in list(range(1, n_head)) + [0]:
        block = ((me + d) % n_head).astype(jnp.int32)[None]
        attn_t = attention(
            plist, pcount, page_node, page_fill, kfirst, block, qt, tok, projected, vnt,
            segk, cache, cvt,
        )
        partial = lax.dot_general(
            attn_t, w_out, (((0,), (0,)), ((), ())), preferred_element_type=jnp.float32
        )
        if d == 0:
            total = partial
        else:
            send, qt = lax.optimization_barrier((partial.astype(jnp.bfloat16), qt))
            received.append(lax.ppermute(send, "head", shift_perm(n_head, d)))
    for recv in received:
        total = total + recv.astype(jnp.float32)
    return total.astype(jnp.bfloat16)[None]


def solution(mesh):
    placed = (
        P("page", "head", None),
        P(),
        P(None, None, "head"),
        P("head", None),
        P(None, "page", None, "head"),
        P(),
        P(),
        P(),
        P("page", None),
        P("page", None),
    )
    return jax.shard_map(
        shards_body, mesh=mesh, in_specs=placed, out_specs=P("page", "head", None), check_vma=False
    )
```

```python
import jax
import jax.numpy as jnp
from jax import lax
from jax.experimental import pallas as pl
from jax.experimental.pallas import tpu as pltpu
from jax.sharding import PartitionSpec as P

HD = 64
EPSILON = 1e-06
FLOOR_SCORE = -1e30
Q_BLOCK = 256
K_BLOCK = 128
INTERPRET = False


def lookup(indices, lookup_table):
    matches = indices[:, None] == jnp.arange(lookup_table.shape[0], dtype=jnp.int32)[None, :]
    return jnp.sum(jnp.where(matches, lookup_table[None, :], 0), axis=1)


def attn_kernel(
    plist_ref, pcount_ref, pnode_ref, pfill_ref, kfirst_ref,
    qt_ref, tok_ref, kn_ref, vnt_ref, segk_ref, cache_ref,
    o_ref,
    ma_sc, la_sc, acca_sc, mb_sc, lb_sc, accb_sc, cvt_ref,
):
    i = pl.program_id(0)
    width, tq = qt_ref.shape
    groups = width // HD
    pages = cache_ref.shape[1]
    kb = cache_ref.shape[2]

    @pl.when(i == 0)
    def _():
        def transpose_page(g, carry):
            cvt_ref[g] = cache_ref[1, g].astype(jnp.float32).T.astype(cvt_ref.dtype)
            return carry

        lax.fori_loop(0, pages, transpose_page, 0)

    qt = qt_ref[...] * jnp.asarray(0.125, jnp.bfloat16)
    seg_q = tok_ref[0:1, :]
    leaf = tok_ref[1:2, :]
    upper = tok_ref[2:3, :]
    root = tok_ref[3:4, :]
    for m_sc, l_sc, acc_sc in ((ma_sc, la_sc, acca_sc), (mb_sc, lb_sc, accb_sc)):
        m_sc[...] = jnp.full(m_sc.shape, FLOOR_SCORE, jnp.float32)
        l_sc[...] = jnp.zeros(l_sc.shape, jnp.float32)
        acc_sc[...] = jnp.zeros(acc_sc.shape, jnp.float32)
    col_head = lax.broadcasted_iota(jnp.int32, (kb, width), 1) // HD
    row_head = lax.broadcasted_iota(jnp.int32, (width, kb), 0) // HD
    slot = lax.broadcasted_iota(jnp.int32, (kb, 1), 0)

    def update(state, k, vt, mask):
        m_sc, l_sc, acc_sc = state
        zk = jnp.zeros_like(k)
        kbd = jnp.concatenate([jnp.where(col_head == h, k, zk) for h in range(groups)], axis=0)
        st = jnp.dot(kbd, qt, preferred_element_type=jnp.float32)
        probs = []
        scales = []
        for h in range(groups):
            s_h = jnp.where(mask, st[h * kb:(h + 1) * kb, :], FLOOR_SCORE)
            m_old = m_sc[h]
            m_new = jnp.maximum(m_old, jnp.max(s_h, axis=0, keepdims=True))
            alpha = jnp.exp(m_old - m_new)
            p_h = jnp.exp(s_h - m_new)
            l_sc[h] = alpha * l_sc[h] + jnp.sum(p_h, axis=0, keepdims=True)
            m_sc[h] = m_new
            probs.append(p_h.astype(jnp.bfloat16))
            scales.append(jnp.broadcast_to(alpha, (HD, tq)))
        zv = jnp.zeros_like(vt)
        vbdt = jnp.concatenate([jnp.where(row_head == h, vt, zv) for h in range(groups)], axis=1)
        pv = jnp.dot(vbdt, jnp.concatenate(probs, axis=0), preferred_element_type=jnp.float32)
        acc_sc[...] = acc_sc[...] * jnp.concatenate(scales, axis=0) + pv

    chain_a = (ma_sc, la_sc, acca_sc)
    chain_b = (mb_sc, lb_sc, accb_sc)
    qpos = i * tq + lax.broadcasted_iota(jnp.int32, (1, tq), 1)

    def suffix_step(b, carry):
        start = pl.multiple_of(b * kb, kb)
        kpos = start + slot
        mask = (segk_ref[pl.ds(start, kb), :] == seg_q) & (kpos <= qpos)
        update(chain_a, kn_ref[pl.ds(start, kb), :], vnt_ref[:, pl.ds(start, kb)], mask)
        return carry

    last = (i * tq + tq - 1) // kb
    lax.fori_loop(kfirst_ref[i], last + 1, suffix_step, 0)

    count = pcount_ref[i]

    def page_mask(g, valid):
        node = pnode_ref[g]
        fill = jnp.where(valid, pfill_ref[g], 0)
        tok_ok = (leaf == node) | (upper == node) | (root == node)
        return tok_ok & (slot < fill)

    def pair_step(j, carry):
        g0 = plist_ref[i * pages + 2 * j]
        g1 = plist_ref[i * pages + 2 * j + 1]
        update(chain_a, cache_ref[0, g0], cvt_ref[g0], page_mask(g0, True))
        update(chain_b, cache_ref[0, g1], cvt_ref[g1], page_mask(g1, 2 * j + 1 < count))
        return carry

    lax.fori_loop(0, (count + 1) // 2, pair_step, 0)

    parts = []
    for h in range(groups):
        m_all = jnp.maximum(ma_sc[h], mb_sc[h])
        wa = jnp.exp(ma_sc[h] - m_all)
        wb = jnp.exp(mb_sc[h] - m_all)
        l_all = la_sc[h] * wa + lb_sc[h] * wb
        rows = slice(h * HD, (h + 1) * HD)
        acc_h = acca_sc[rows, :] * wa + accb_sc[rows, :] * wb
        parts.append(acc_h / l_all)
    o_ref[...] = jnp.concatenate(parts, axis=0).astype(o_ref.dtype)


def attention(plist, pcount, page_node, page_fill, kfirst, qt, tok, proj, vnt, segk, cache):
    width, tokens = qt.shape
    groups = width // HD
    nqb = tokens // Q_BLOCK
    state = [
        pltpu.VMEM((groups, 1, Q_BLOCK), jnp.float32),
        pltpu.VMEM((groups, 1, Q_BLOCK), jnp.float32),
        pltpu.VMEM((width, Q_BLOCK), jnp.float32),
    ]
    grid_spec = pltpu.PrefetchScalarGridSpec(
        num_scalar_prefetch=5,
        grid=(nqb,),
        in_specs=[
            pl.BlockSpec((width, Q_BLOCK), lambda i, *_: (0, i)),
            pl.BlockSpec((tok.shape[0], Q_BLOCK), lambda i, *_: (0, i)),
            pl.BlockSpec((tokens, width), lambda i, *_: (0, 1)),
            pl.BlockSpec(memory_space=pltpu.VMEM),
            pl.BlockSpec(memory_space=pltpu.VMEM),
            pl.BlockSpec(memory_space=pltpu.VMEM),
        ],
        out_specs=pl.BlockSpec((width, Q_BLOCK), lambda i, *_: (0, i)),
        scratch_shapes=state + state + [
            pltpu.VMEM((cache.shape[1], width, cache.shape[2]), jnp.bfloat16),
        ],
    )
    return pl.pallas_call(
        attn_kernel,
        grid_spec=grid_spec,
        interpret=INTERPRET,
        out_shape=jax.ShapeDtypeStruct((width, tokens), jnp.bfloat16),
        compiler_params=pltpu.CompilerParams(
            dimension_semantics=("arbitrary",), vmem_limit_bytes=48 * 1024 * 1024
        ),
    )(plist, pcount, page_node, page_fill, kfirst, qt, tok, proj, vnt, segk, cache)


def shift_perm(n, d):
    return [(j, (j + d) % n) for j in range(n)]


def head_gather(x, n):
    me = lax.axis_index("head")
    parts = [x] + [lax.ppermute(x, "head", shift_perm(n, d)) for d in range(1, n)]
    stacked = jnp.stack(parts)
    order = (me - jnp.arange(n, dtype=jnp.int32)) % n
    gathered = jnp.take(stacked, order, axis=0)
    return gathered.reshape(n * x.shape[0], x.shape[1])


def head_reduce_scatter(partial, n):
    me = lax.axis_index("head")
    rows = partial.shape[0] // n
    chunks = partial.reshape(n, rows, partial.shape[1])
    total = lax.dynamic_index_in_dim(chunks, me, 0, keepdims=False)
    for d in range(1, n):
        send = lax.dynamic_index_in_dim(chunks, (me + d) % n, 0, keepdims=False)
        recv = lax.ppermute(send.astype(jnp.bfloat16), "head", shift_perm(n, d))
        total = total + recv.astype(jnp.float32)
    return total.astype(jnp.bfloat16)


def shards(
    hidden_in,
    norm_gain,
    w_qkv,
    w_out,
    cache_kv,
    page_node,
    page_fill,
    node_parent,
    tok_seg,
    req_leaf,
):
    widened = hidden_in[0].astype(jnp.float32)
    normed = (
        widened
        * lax.rsqrt(jnp.mean(widened * widened, axis=1, keepdims=True) + EPSILON)
        * norm_gain
    ).astype(jnp.bfloat16)
    model_width = widened.shape[1]
    group_width = w_qkv.shape[2]
    weight_flat = w_qkv.reshape(model_width, 3 * group_width)
    n_head = tok_seg.shape[1] // hidden_in.shape[1]
    w_full = head_gather(w_out, n_head)
    projected = jnp.dot(
        head_gather(normed, n_head),
        weight_flat,
        preferred_element_type=jnp.float32,
    ).astype(jnp.bfloat16)
    tokens = projected.shape[0]
    segment = tok_seg[0]
    leaf_node = lookup(segment, req_leaf[0])
    upper_node = lookup(leaf_node, node_parent)
    root_node = lookup(upper_node, node_parent)
    zero_row = jnp.zeros_like(segment)
    tok = jnp.stack(
        [segment, leaf_node, upper_node, root_node] + [zero_row] * 4, axis=0
    )
    pages = page_node.shape[0]
    seen = (
        (page_node[None, :] == leaf_node[:, None])
        | (page_node[None, :] == upper_node[:, None])
        | (page_node[None, :] == root_node[:, None])
    )
    nqb = tokens // Q_BLOCK
    vis = jnp.any(seen.reshape(nqb, Q_BLOCK, pages), axis=1).astype(jnp.int32)
    rank = jnp.cumsum(vis, axis=1) - 1
    picked = (vis[:, :, None] > 0) & (rank[:, :, None] == jnp.arange(pages)[None, None, :])
    plist = jnp.sum(
        jnp.where(picked, jnp.arange(pages, dtype=jnp.int32)[None, :, None], 0), axis=1
    ).astype(jnp.int32).reshape(-1)
    pcount = jnp.sum(vis, axis=1).astype(jnp.int32)
    first_seg = segment[::Q_BLOCK]
    kfirst = (
        jnp.sum((segment[None, :] < first_seg[:, None]).astype(jnp.int32), axis=1) // K_BLOCK
    ).astype(jnp.int32)
    segk = segment[:, None]
    qt = projected[:, :group_width].T
    vnt = projected[:, 2 * group_width:].T
    cache = lax.all_gather(cache_kv, "page", axis=1, tiled=True)
    attn_t = attention(
        plist, pcount, page_node, page_fill, kfirst, qt, tok, projected, vnt, segk, cache
    )
    me = lax.axis_index("head")
    rows = tokens // n_head
    parts = [lax.dynamic_slice_in_dim(attn_t, me * rows, rows, axis=1)]
    for d in range(1, n_head):
        send = lax.dynamic_slice_in_dim(attn_t, ((me + d) % n_head) * rows, rows, axis=1)
        parts.append(lax.ppermute(send, "head", shift_perm(n_head, d)))
    order = (me - jnp.arange(n_head, dtype=jnp.int32)) % n_head
    mine = jnp.take(jnp.stack(parts), order, axis=0)
    mine = mine.reshape(n_head * mine.shape[1], rows)
    result = lax.dot_general(
        mine, w_full, (((0,), (0,)), ((), ())), preferred_element_type=jnp.float32
    ).astype(jnp.bfloat16)
    return result[None]


def solution(mesh):
    placed = (
        P("page", "head", None),
        P(),
        P(None, None, "head"),
        P("head", None),
        P(None, "page", None, "head"),
        P(),
        P(),
        P(),
        P("page", None),
        P("page", None),
    )
    return jax.shard_map(
        shards, mesh=mesh, in_specs=placed, out_specs=P("page", "head", None), check_vma=False
    )
```

```python
import jax
import jax.numpy as jnp
from jax import lax
from jax.experimental import pallas as pl
from jax.experimental.pallas import tpu as pltpu
from jax.sharding import PartitionSpec as P

HD = 64
EPSILON = 1e-06
FLOOR_SCORE = -1e30
Q_BLOCK = 256
K_BLOCK = 128
INTERPRET = False


def lookup(indices, lookup_table):
    matches = indices[:, None] == jnp.arange(lookup_table.shape[0], dtype=jnp.int32)[None, :]
    return jnp.sum(jnp.where(matches, lookup_table[None, :], 0), axis=1)


def attn_kernel(
    plist_ref, pcount_ref, pnode_ref, pfill_ref, kfirst_ref,
    qt_ref, tok_ref, kn_ref, vnt_ref, segk_ref, cache_ref,
    o_ref,
    ma_sc, la_sc, acca_sc, mb_sc, lb_sc, accb_sc, cvt_ref,
):
    i = pl.program_id(0)
    width, tq = qt_ref.shape
    groups = width // HD
    pages = cache_ref.shape[1]
    kb = cache_ref.shape[2]

    @pl.when(i == 0)
    def _():
        def transpose_page(g, carry):
            cvt_ref[g] = cache_ref[1, g].astype(jnp.float32).T.astype(cvt_ref.dtype)
            return carry

        lax.fori_loop(0, pages, transpose_page, 0)

    qt = qt_ref[...] * jnp.asarray(0.125, jnp.bfloat16)
    seg_q = tok_ref[0:1, :]
    leaf = tok_ref[1:2, :]
    upper = tok_ref[2:3, :]
    root = tok_ref[3:4, :]
    for m_sc, l_sc, acc_sc in ((ma_sc, la_sc, acca_sc), (mb_sc, lb_sc, accb_sc)):
        m_sc[...] = jnp.full(m_sc.shape, FLOOR_SCORE, jnp.float32)
        l_sc[...] = jnp.zeros(l_sc.shape, jnp.float32)
        acc_sc[...] = jnp.zeros(acc_sc.shape, jnp.float32)
    col_head = lax.broadcasted_iota(jnp.int32, (kb, width), 1) // HD
    row_head = lax.broadcasted_iota(jnp.int32, (width, kb), 0) // HD
    slot = lax.broadcasted_iota(jnp.int32, (kb, 1), 0)

    def update(state, k, vt, mask):
        m_sc, l_sc, acc_sc = state
        zk = jnp.zeros_like(k)
        kbd = jnp.concatenate([jnp.where(col_head == h, k, zk) for h in range(groups)], axis=0)
        st = jnp.dot(kbd, qt, preferred_element_type=jnp.float32)
        probs = []
        scales = []
        for h in range(groups):
            s_h = jnp.where(mask, st[h * kb:(h + 1) * kb, :], FLOOR_SCORE)
            m_old = m_sc[h]
            m_new = jnp.maximum(m_old, jnp.max(s_h, axis=0, keepdims=True))
            alpha = jnp.exp(m_old - m_new)
            p_h = jnp.exp(s_h - m_new)
            l_sc[h] = alpha * l_sc[h] + jnp.sum(p_h, axis=0, keepdims=True)
            m_sc[h] = m_new
            probs.append(p_h.astype(jnp.bfloat16))
            scales.append(jnp.broadcast_to(alpha, (HD, tq)))
        zv = jnp.zeros_like(vt)
        vbdt = jnp.concatenate([jnp.where(row_head == h, vt, zv) for h in range(groups)], axis=1)
        pv = jnp.dot(vbdt, jnp.concatenate(probs, axis=0), preferred_element_type=jnp.float32)
        acc_sc[...] = acc_sc[...] * jnp.concatenate(scales, axis=0) + pv

    chain_a = (ma_sc, la_sc, acca_sc)
    chain_b = (mb_sc, lb_sc, accb_sc)
    qpos = i * tq + lax.broadcasted_iota(jnp.int32, (1, tq), 1)

    def suffix_step(b, carry):
        start = pl.multiple_of(b * kb, kb)
        kpos = start + slot
        mask = (segk_ref[pl.ds(start, kb), :] == seg_q) & (kpos <= qpos)
        update(chain_a, kn_ref[pl.ds(start, kb), :], vnt_ref[:, pl.ds(start, kb)], mask)
        return carry

    last = (i * tq + tq - 1) // kb
    lax.fori_loop(kfirst_ref[i], last + 1, suffix_step, 0)

    count = pcount_ref[i]

    def page_mask(g, valid):
        node = pnode_ref[g]
        fill = jnp.where(valid, pfill_ref[g], 0)
        tok_ok = (leaf == node) | (upper == node) | (root == node)
        return tok_ok & (slot < fill)

    def pair_step(j, carry):
        g0 = plist_ref[i * pages + 2 * j]
        g1 = plist_ref[i * pages + 2 * j + 1]
        update(chain_a, cache_ref[0, g0], cvt_ref[g0], page_mask(g0, True))
        update(chain_b, cache_ref[0, g1], cvt_ref[g1], page_mask(g1, 2 * j + 1 < count))
        return carry

    lax.fori_loop(0, (count + 1) // 2, pair_step, 0)

    parts = []
    for h in range(groups):
        m_all = jnp.maximum(ma_sc[h], mb_sc[h])
        wa = jnp.exp(ma_sc[h] - m_all)
        wb = jnp.exp(mb_sc[h] - m_all)
        l_all = la_sc[h] * wa + lb_sc[h] * wb
        rows = slice(h * HD, (h + 1) * HD)
        acc_h = acca_sc[rows, :] * wa + accb_sc[rows, :] * wb
        parts.append(acc_h / l_all)
    o_ref[...] = jnp.concatenate(parts, axis=0).astype(o_ref.dtype)


def attention(plist, pcount, page_node, page_fill, kfirst, qt, tok, proj, vnt, segk, cache):
    width, tokens = qt.shape
    groups = width // HD
    nqb = tokens // Q_BLOCK
    state = [
        pltpu.VMEM((groups, 1, Q_BLOCK), jnp.float32),
        pltpu.VMEM((groups, 1, Q_BLOCK), jnp.float32),
        pltpu.VMEM((width, Q_BLOCK), jnp.float32),
    ]
    grid_spec = pltpu.PrefetchScalarGridSpec(
        num_scalar_prefetch=5,
        grid=(nqb,),
        in_specs=[
            pl.BlockSpec((width, Q_BLOCK), lambda i, *_: (0, i)),
            pl.BlockSpec((tok.shape[0], Q_BLOCK), lambda i, *_: (0, i)),
            pl.BlockSpec((tokens, width), lambda i, *_: (0, 1)),
            pl.BlockSpec(memory_space=pltpu.VMEM),
            pl.BlockSpec(memory_space=pltpu.VMEM),
            pl.BlockSpec(memory_space=pltpu.VMEM),
        ],
        out_specs=pl.BlockSpec((width, Q_BLOCK), lambda i, *_: (0, i)),
        scratch_shapes=state + state + [
            pltpu.VMEM((cache.shape[1], width, cache.shape[2]), jnp.bfloat16),
        ],
    )
    return pl.pallas_call(
        attn_kernel,
        grid_spec=grid_spec,
        interpret=INTERPRET,
        out_shape=jax.ShapeDtypeStruct((width, tokens), jnp.bfloat16),
        compiler_params=pltpu.CompilerParams(
            dimension_semantics=("arbitrary",), vmem_limit_bytes=48 * 1024 * 1024
        ),
    )(plist, pcount, page_node, page_fill, kfirst, qt, tok, proj, vnt, segk, cache)


def shift_perm(n, d):
    return [(j, (j + d) % n) for j in range(n)]


def head_gather(x, n):
    me = lax.axis_index("head")
    parts = [x] + [lax.ppermute(x, "head", shift_perm(n, d)) for d in range(1, n)]
    stacked = jnp.stack(parts)
    order = (me - jnp.arange(n, dtype=jnp.int32)) % n
    gathered = jnp.take(stacked, order, axis=0)
    return gathered.reshape(n * x.shape[0], x.shape[1])


def head_reduce_scatter(partial, n):
    me = lax.axis_index("head")
    rows = partial.shape[0] // n
    chunks = partial.reshape(n, rows, partial.shape[1])
    total = lax.dynamic_index_in_dim(chunks, me, 0, keepdims=False)
    for d in range(1, n):
        send = lax.dynamic_index_in_dim(chunks, (me + d) % n, 0, keepdims=False)
        recv = lax.ppermute(send.astype(jnp.bfloat16), "head", shift_perm(n, d))
        total = total + recv.astype(jnp.float32)
    return total.astype(jnp.bfloat16)


def shards(
    hidden_in,
    norm_gain,
    w_qkv,
    w_out,
    cache_kv,
    page_node,
    page_fill,
    node_parent,
    tok_seg,
    req_leaf,
):
    widened = hidden_in[0].astype(jnp.float32)
    normed = (
        widened
        * lax.rsqrt(jnp.mean(widened * widened, axis=1, keepdims=True) + EPSILON)
        * norm_gain
    ).astype(jnp.bfloat16)
    model_width = widened.shape[1]
    group_width = w_qkv.shape[2]
    weight_flat = w_qkv.reshape(model_width, 3 * group_width)
    n_head = tok_seg.shape[1] // hidden_in.shape[1]
    w_shifted = jnp.concatenate(
        [w_out] + [lax.ppermute(w_out, "head", shift_perm(n_head, d)) for d in range(1, n_head)],
        axis=0,
    )
    projected = jnp.dot(
        head_gather(normed, n_head),
        weight_flat,
        preferred_element_type=jnp.float32,
    ).astype(jnp.bfloat16)
    tokens = projected.shape[0]
    segment = tok_seg[0]
    leaf_node = lookup(segment, req_leaf[0])
    upper_node = lookup(leaf_node, node_parent)
    root_node = lookup(upper_node, node_parent)
    zero_row = jnp.zeros_like(segment)
    tok = jnp.stack(
        [segment, leaf_node, upper_node, root_node] + [zero_row] * 4, axis=0
    )
    pages = page_node.shape[0]
    seen = (
        (page_node[None, :] == leaf_node[:, None])
        | (page_node[None, :] == upper_node[:, None])
        | (page_node[None, :] == root_node[:, None])
    )
    nqb = tokens // Q_BLOCK
    vis = jnp.any(seen.reshape(nqb, Q_BLOCK, pages), axis=1).astype(jnp.int32)
    rank = jnp.cumsum(vis, axis=1) - 1
    picked = (vis[:, :, None] > 0) & (rank[:, :, None] == jnp.arange(pages)[None, None, :])
    plist = jnp.sum(
        jnp.where(picked, jnp.arange(pages, dtype=jnp.int32)[None, :, None], 0), axis=1
    ).astype(jnp.int32).reshape(-1)
    pcount = jnp.sum(vis, axis=1).astype(jnp.int32)
    first_seg = segment[::Q_BLOCK]
    kfirst = (
        jnp.sum((segment[None, :] < first_seg[:, None]).astype(jnp.int32), axis=1) // K_BLOCK
    ).astype(jnp.int32)
    segk = segment[:, None]
    qt = projected[:, :group_width].T
    vnt = projected[:, 2 * group_width:].T
    cache = lax.all_gather(cache_kv, "page", axis=1, tiled=True)
    attn_t = attention(
        plist, pcount, page_node, page_fill, kfirst, qt, tok, projected, vnt, segk, cache
    )
    me = lax.axis_index("head")
    rows = tokens // n_head
    parts = [lax.dynamic_slice_in_dim(attn_t, me * rows, rows, axis=1)]
    for d in range(1, n_head):
        send = lax.dynamic_slice_in_dim(attn_t, ((me + d) % n_head) * rows, rows, axis=1)
        parts.append(lax.ppermute(send, "head", shift_perm(n_head, d)))
    mine = jnp.concatenate(parts, axis=0)
    result = lax.dot_general(
        mine, w_shifted, (((0,), (0,)), ((), ())), preferred_element_type=jnp.float32
    ).astype(jnp.bfloat16)
    return result[None]


def solution(mesh):
    placed = (
        P("page", "head", None),
        P(),
        P(None, None, "head"),
        P("head", None),
        P(None, "page", None, "head"),
        P(),
        P(),
        P(),
        P("page", None),
        P("page", None),
    )
    return jax.shard_map(
        shards, mesh=mesh, in_specs=placed, out_specs=P("page", "head", None), check_vma=False
    )
```

```python
import jax
import jax.numpy as jnp
from jax import lax
from jax.experimental import pallas as pl
from jax.experimental.pallas import tpu as pltpu
from jax.sharding import PartitionSpec as P

HD = 64
EPSILON = 1e-06
FLOOR_SCORE = -1e30
Q_BLOCK = 256
K_BLOCK = 128
CHAINS = 3
INTERPRET = False


def lookup(indices, lookup_table):
    matches = indices[:, None] == jnp.arange(lookup_table.shape[0], dtype=jnp.int32)[None, :]
    return jnp.sum(jnp.where(matches, lookup_table[None, :], 0), axis=1)


def attn_kernel(
    plist_ref, pcount_ref, pnode_ref, pfill_ref, kfirst_ref,
    qt_ref, tok_ref, kn_ref, vnt_ref, segk_ref, cache_ref,
    o_ref,
    *scratch,
):
    cvt_ref = scratch[-1]
    chains = [tuple(scratch[3 * c:3 * c + 3]) for c in range(CHAINS)]
    i = pl.program_id(0)
    width, tq = qt_ref.shape
    groups = width // HD
    pages = cache_ref.shape[1]
    kb = cache_ref.shape[2]

    @pl.when(i == 0)
    def _():
        def transpose_page(g, carry):
            cvt_ref[g] = cache_ref[1, g].astype(jnp.float32).T.astype(cvt_ref.dtype)
            return carry

        lax.fori_loop(0, pages, transpose_page, 0)

    qt = qt_ref[...] * jnp.asarray(0.125, jnp.bfloat16)
    seg_q = tok_ref[0:1, :]
    leaf = tok_ref[1:2, :]
    upper = tok_ref[2:3, :]
    root = tok_ref[3:4, :]
    for m_sc, l_sc, acc_sc in chains:
        m_sc[...] = jnp.full(m_sc.shape, FLOOR_SCORE, jnp.float32)
        l_sc[...] = jnp.zeros(l_sc.shape, jnp.float32)
        acc_sc[...] = jnp.zeros(acc_sc.shape, jnp.float32)
    col_head = lax.broadcasted_iota(jnp.int32, (kb, width), 1) // HD
    row_head = lax.broadcasted_iota(jnp.int32, (width, kb), 0) // HD
    slot = lax.broadcasted_iota(jnp.int32, (kb, 1), 0)

    def update(state, k, vt, mask):
        m_sc, l_sc, acc_sc = state
        zk = jnp.zeros_like(k)
        kbd = jnp.concatenate([jnp.where(col_head == h, k, zk) for h in range(groups)], axis=0)
        st = jnp.dot(kbd, qt, preferred_element_type=jnp.float32)
        probs = []
        scales = []
        for h in range(groups):
            s_h = jnp.where(mask, st[h * kb:(h + 1) * kb, :], FLOOR_SCORE)
            m_old = m_sc[h]
            m_new = jnp.maximum(m_old, jnp.max(s_h, axis=0, keepdims=True))
            alpha = jnp.exp(m_old - m_new)
            p_h = jnp.exp(s_h - m_new)
            l_sc[h] = alpha * l_sc[h] + jnp.sum(p_h, axis=0, keepdims=True)
            m_sc[h] = m_new
            probs.append(p_h.astype(jnp.bfloat16))
            scales.append(jnp.broadcast_to(alpha, (HD, tq)))
        zv = jnp.zeros_like(vt)
        vbdt = jnp.concatenate([jnp.where(row_head == h, vt, zv) for h in range(groups)], axis=1)
        pv = jnp.dot(vbdt, jnp.concatenate(probs, axis=0), preferred_element_type=jnp.float32)
        acc_sc[...] = acc_sc[...] * jnp.concatenate(scales, axis=0) + pv

    chain_a = chains[0]
    stride = plist_ref.shape[0] // kfirst_ref.shape[0]
    qpos = i * tq + lax.broadcasted_iota(jnp.int32, (1, tq), 1)

    def suffix_step(b, carry):
        start = pl.multiple_of(b * kb, kb)
        kpos = start + slot
        mask = (segk_ref[pl.ds(start, kb), :] == seg_q) & (kpos <= qpos)
        update(chain_a, kn_ref[pl.ds(start, kb), :], vnt_ref[:, pl.ds(start, kb)], mask)
        return carry

    last = (i * tq + tq - 1) // kb
    lax.fori_loop(kfirst_ref[i], last + 1, suffix_step, 0)

    count = pcount_ref[i]

    def page_mask(g, valid):
        node = pnode_ref[g]
        fill = jnp.where(valid, pfill_ref[g], 0)
        tok_ok = (leaf == node) | (upper == node) | (root == node)
        return tok_ok & (slot < fill)

    def group_step(j, carry):
        for c in range(CHAINS):
            at = CHAINS * j + c
            g = plist_ref[i * stride + at]
            update(chains[c], cache_ref[0, g], cvt_ref[g], page_mask(g, at < count))
        return carry

    lax.fori_loop(0, (count + CHAINS - 1) // CHAINS, group_step, 0)

    parts = []
    for h in range(groups):
        m_all = chains[0][0][h]
        for c in range(1, CHAINS):
            m_all = jnp.maximum(m_all, chains[c][0][h])
        rows = slice(h * HD, (h + 1) * HD)
        l_all = None
        acc_h = None
        for m_sc, l_sc, acc_sc in chains:
            w = jnp.exp(m_sc[h] - m_all)
            l_part = l_sc[h] * w
            acc_part = acc_sc[rows, :] * w
            l_all = l_part if l_all is None else l_all + l_part
            acc_h = acc_part if acc_h is None else acc_h + acc_part
        parts.append(acc_h / l_all)
    o_ref[...] = jnp.concatenate(parts, axis=0).astype(o_ref.dtype)


def attention(plist, pcount, page_node, page_fill, kfirst, qt, tok, proj, vnt, segk, cache):
    width, tokens = qt.shape
    groups = width // HD
    nqb = tokens // Q_BLOCK
    state = [
        pltpu.VMEM((groups, 1, Q_BLOCK), jnp.float32),
        pltpu.VMEM((groups, 1, Q_BLOCK), jnp.float32),
        pltpu.VMEM((width, Q_BLOCK), jnp.float32),
    ]
    grid_spec = pltpu.PrefetchScalarGridSpec(
        num_scalar_prefetch=5,
        grid=(nqb,),
        in_specs=[
            pl.BlockSpec((width, Q_BLOCK), lambda i, *_: (0, i)),
            pl.BlockSpec((tok.shape[0], Q_BLOCK), lambda i, *_: (0, i)),
            pl.BlockSpec((tokens, width), lambda i, *_: (0, 1)),
            pl.BlockSpec(memory_space=pltpu.VMEM),
            pl.BlockSpec(memory_space=pltpu.VMEM),
            pl.BlockSpec(memory_space=pltpu.VMEM),
        ],
        out_specs=pl.BlockSpec((width, Q_BLOCK), lambda i, *_: (0, i)),
        scratch_shapes=state * CHAINS + [
            pltpu.VMEM((cache.shape[1], width, cache.shape[2]), jnp.bfloat16),
        ],
    )
    return pl.pallas_call(
        attn_kernel,
        grid_spec=grid_spec,
        interpret=INTERPRET,
        out_shape=jax.ShapeDtypeStruct((width, tokens), jnp.bfloat16),
        compiler_params=pltpu.CompilerParams(
            dimension_semantics=("arbitrary",), vmem_limit_bytes=48 * 1024 * 1024
        ),
    )(plist, pcount, page_node, page_fill, kfirst, qt, tok, proj, vnt, segk, cache)


def shift_perm(n, d):
    return [(j, (j + d) % n) for j in range(n)]


def head_gather(x, n):
    me = lax.axis_index("head")
    parts = [x] + [lax.ppermute(x, "head", shift_perm(n, d)) for d in range(1, n)]
    stacked = jnp.stack(parts)
    order = (me - jnp.arange(n, dtype=jnp.int32)) % n
    gathered = jnp.take(stacked, order, axis=0)
    return gathered.reshape(n * x.shape[0], x.shape[1])


def head_reduce_scatter(partial, n):
    me = lax.axis_index("head")
    rows = partial.shape[0] // n
    chunks = partial.reshape(n, rows, partial.shape[1])
    total = lax.dynamic_index_in_dim(chunks, me, 0, keepdims=False)
    for d in range(1, n):
        send = lax.dynamic_index_in_dim(chunks, (me + d) % n, 0, keepdims=False)
        recv = lax.ppermute(send.astype(jnp.bfloat16), "head", shift_perm(n, d))
        total = total + recv.astype(jnp.float32)
    return total.astype(jnp.bfloat16)


def shards(
    hidden_in,
    norm_gain,
    w_qkv,
    w_out,
    cache_kv,
    page_node,
    page_fill,
    node_parent,
    tok_seg,
    req_leaf,
):
    widened = hidden_in[0].astype(jnp.float32)
    normed = (
        widened
        * lax.rsqrt(jnp.mean(widened * widened, axis=1, keepdims=True) + EPSILON)
        * norm_gain
    ).astype(jnp.bfloat16)
    model_width = widened.shape[1]
    group_width = w_qkv.shape[2]
    weight_flat = w_qkv.reshape(model_width, 3 * group_width)
    n_head = tok_seg.shape[1] // hidden_in.shape[1]
    w_full = head_gather(w_out, n_head)
    projected = jnp.dot(
        head_gather(normed, n_head),
        weight_flat,
        preferred_element_type=jnp.float32,
    ).astype(jnp.bfloat16)
    tokens = projected.shape[0]
    segment = tok_seg[0]
    leaf_node = lookup(segment, req_leaf[0])
    upper_node = lookup(leaf_node, node_parent)
    root_node = lookup(upper_node, node_parent)
    zero_row = jnp.zeros_like(segment)
    tok = jnp.stack(
        [segment, leaf_node, upper_node, root_node] + [zero_row] * 4, axis=0
    )
    pages = page_node.shape[0]
    seen = (
        (page_node[None, :] == leaf_node[:, None])
        | (page_node[None, :] == upper_node[:, None])
        | (page_node[None, :] == root_node[:, None])
    )
    nqb = tokens // Q_BLOCK
    vis = jnp.any(seen.reshape(nqb, Q_BLOCK, pages), axis=1).astype(jnp.int32)
    rank = jnp.cumsum(vis, axis=1) - 1
    picked = (vis[:, :, None] > 0) & (rank[:, :, None] == jnp.arange(pages)[None, None, :])
    plist = jnp.sum(
        jnp.where(picked, jnp.arange(pages, dtype=jnp.int32)[None, :, None], 0), axis=1
    ).astype(jnp.int32)
    plist = jnp.pad(plist, ((0, 0), (0, CHAINS))).reshape(-1)
    pcount = jnp.sum(vis, axis=1).astype(jnp.int32)
    first_seg = segment[::Q_BLOCK]
    kfirst = (
        jnp.sum((segment[None, :] < first_seg[:, None]).astype(jnp.int32), axis=1) // K_BLOCK
    ).astype(jnp.int32)
    segk = segment[:, None]
    qt = projected[:, :group_width].T
    vnt = projected[:, 2 * group_width:].T
    cache = lax.all_gather(cache_kv, "page", axis=1, tiled=True)
    attn_t = attention(
        plist, pcount, page_node, page_fill, kfirst, qt, tok, projected, vnt, segk, cache
    )
    me = lax.axis_index("head")
    rows = tokens // n_head
    parts = [lax.dynamic_slice_in_dim(attn_t, me * rows, rows, axis=1)]
    for d in range(1, n_head):
        send = lax.dynamic_slice_in_dim(attn_t, ((me + d) % n_head) * rows, rows, axis=1)
        parts.append(lax.ppermute(send, "head", shift_perm(n_head, d)))
    order = (me - jnp.arange(n_head, dtype=jnp.int32)) % n_head
    mine = jnp.take(jnp.stack(parts), order, axis=0)
    mine = mine.reshape(n_head * mine.shape[1], rows)
    result = lax.dot_general(
        mine, w_full, (((0,), (0,)), ((), ())), preferred_element_type=jnp.float32
    ).astype(jnp.bfloat16)
    return result[None]


def solution(mesh):
    placed = (
        P("page", "head", None),
        P(),
        P(None, None, "head"),
        P("head", None),
        P(None, "page", None, "head"),
        P(),
        P(),
        P(),
        P("page", None),
        P("page", None),
    )
    return jax.shard_map(
        shards, mesh=mesh, in_specs=placed, out_specs=P("page", "head", None), check_vma=False
    )
```

```python
import jax
import jax.numpy as jnp
from jax import lax
from jax.experimental import pallas as pl
from jax.experimental.pallas import tpu as pltpu
from jax.sharding import PartitionSpec as P

HD = 64
EPSILON = 1e-06
FLOOR_SCORE = -1e30
Q_BLOCK = 256
K_BLOCK = 128
CHAINS = 3
INTERPRET = False


def lookup(indices, lookup_table):
    matches = indices[:, None] == jnp.arange(lookup_table.shape[0], dtype=jnp.int32)[None, :]
    return jnp.sum(jnp.where(matches, lookup_table[None, :], 0), axis=1)


def attn_kernel(
    plist_ref, pcount_ref, pnode_ref, pfill_ref, kfirst_ref,
    qt_ref, tok_ref, kn_ref, vnt_ref, segk_ref, cache_ref,
    o_ref,
    *scratch,
):
    cvt_ref = scratch[-1]
    chains = [tuple(scratch[3 * c:3 * c + 3]) for c in range(CHAINS)]
    i = pl.program_id(0)
    width, tq = qt_ref.shape
    groups = width // HD
    pages = cache_ref.shape[1]
    kb = cache_ref.shape[2]

    @pl.when(i == 0)
    def _():
        def transpose_page(g, carry):
            cvt_ref[g] = cache_ref[1, g].astype(jnp.float32).T.astype(cvt_ref.dtype)
            return carry

        lax.fori_loop(0, pages, transpose_page, 0)

    qt = qt_ref[...] * jnp.asarray(0.125, jnp.bfloat16)
    seg_q = tok_ref[0:1, :]
    leaf = tok_ref[1:2, :]
    upper = tok_ref[2:3, :]
    root = tok_ref[3:4, :]
    for m_sc, l_sc, acc_sc in chains:
        m_sc[...] = jnp.full(m_sc.shape, FLOOR_SCORE, jnp.float32)
        l_sc[...] = jnp.zeros(l_sc.shape, jnp.float32)
        acc_sc[...] = jnp.zeros(acc_sc.shape, jnp.float32)
    col_head = lax.broadcasted_iota(jnp.int32, (kb, width), 1) // HD
    row_head = lax.broadcasted_iota(jnp.int32, (width, kb), 0) // HD
    slot = lax.broadcasted_iota(jnp.int32, (kb, 1), 0)

    def update(state, k, vt, mask):
        m_sc, l_sc, acc_sc = state
        zk = jnp.zeros_like(k)
        kbd = jnp.concatenate([jnp.where(col_head == h, k, zk) for h in range(groups)], axis=0)
        st = jnp.dot(kbd, qt, preferred_element_type=jnp.float32)
        probs = []
        scales = []
        for h in range(groups):
            s_h = jnp.where(mask, st[h * kb:(h + 1) * kb, :], FLOOR_SCORE)
            m_old = m_sc[h]
            m_new = jnp.maximum(m_old, jnp.max(s_h, axis=0, keepdims=True))
            alpha = jnp.exp(m_old - m_new)
            p_h = jnp.exp(s_h - m_new)
            l_sc[h] = alpha * l_sc[h] + jnp.sum(p_h, axis=0, keepdims=True)
            m_sc[h] = m_new
            probs.append(p_h.astype(jnp.bfloat16))
            scales.append(jnp.broadcast_to(alpha, (HD, tq)))
        zv = jnp.zeros_like(vt)
        vbdt = jnp.concatenate([jnp.where(row_head == h, vt, zv) for h in range(groups)], axis=1)
        pv = jnp.dot(vbdt, jnp.concatenate(probs, axis=0), preferred_element_type=jnp.float32)
        acc_sc[...] = acc_sc[...] * jnp.concatenate(scales, axis=0) + pv

    stride = plist_ref.shape[0] // kfirst_ref.shape[0]
    qpos = i * tq + lax.broadcasted_iota(jnp.int32, (1, tq), 1)

    last = (i * tq + tq - 1) // kb
    first = kfirst_ref[i]

    def suffix_step(j, carry):
        for c in range(CHAINS):
            b = first + CHAINS * j + c
            valid = b <= last
            start = pl.multiple_of(jnp.minimum(b, last) * kb, kb)
            kpos = start + slot
            mask = (segk_ref[pl.ds(start, kb), :] == seg_q) & (kpos <= qpos) & valid
            update(chains[c], kn_ref[pl.ds(start, kb), :], vnt_ref[:, pl.ds(start, kb)], mask)
        return carry

    lax.fori_loop(0, (last - first + CHAINS) // CHAINS, suffix_step, 0)

    count = pcount_ref[i]

    def page_mask(g, valid):
        node = pnode_ref[g]
        fill = jnp.where(valid, pfill_ref[g], 0)
        tok_ok = (leaf == node) | (upper == node) | (root == node)
        return tok_ok & (slot < fill)

    def group_step(j, carry):
        for c in range(CHAINS):
            at = CHAINS * j + c
            g = plist_ref[i * stride + at]
            update(chains[c], cache_ref[0, g], cvt_ref[g], page_mask(g, at < count))
        return carry

    lax.fori_loop(0, (count + CHAINS - 1) // CHAINS, group_step, 0)

    parts = []
    for h in range(groups):
        m_all = chains[0][0][h]
        for c in range(1, CHAINS):
            m_all = jnp.maximum(m_all, chains[c][0][h])
        rows = slice(h * HD, (h + 1) * HD)
        l_all = None
        acc_h = None
        for m_sc, l_sc, acc_sc in chains:
            w = jnp.exp(m_sc[h] - m_all)
            l_part = l_sc[h] * w
            acc_part = acc_sc[rows, :] * w
            l_all = l_part if l_all is None else l_all + l_part
            acc_h = acc_part if acc_h is None else acc_h + acc_part
        parts.append(acc_h / l_all)
    o_ref[...] = jnp.concatenate(parts, axis=0).astype(o_ref.dtype)


def attention(plist, pcount, page_node, page_fill, kfirst, qt, tok, proj, vnt, segk, cache):
    width, tokens = qt.shape
    groups = width // HD
    nqb = tokens // Q_BLOCK
    state = [
        pltpu.VMEM((groups, 1, Q_BLOCK), jnp.float32),
        pltpu.VMEM((groups, 1, Q_BLOCK), jnp.float32),
        pltpu.VMEM((width, Q_BLOCK), jnp.float32),
    ]
    grid_spec = pltpu.PrefetchScalarGridSpec(
        num_scalar_prefetch=5,
        grid=(nqb,),
        in_specs=[
            pl.BlockSpec((width, Q_BLOCK), lambda i, *_: (0, i)),
            pl.BlockSpec((tok.shape[0], Q_BLOCK), lambda i, *_: (0, i)),
            pl.BlockSpec((tokens, width), lambda i, *_: (0, 1)),
            pl.BlockSpec(memory_space=pltpu.VMEM),
            pl.BlockSpec(memory_space=pltpu.VMEM),
            pl.BlockSpec(memory_space=pltpu.VMEM),
        ],
        out_specs=pl.BlockSpec((width, Q_BLOCK), lambda i, *_: (0, i)),
        scratch_shapes=state * CHAINS + [
            pltpu.VMEM((cache.shape[1], width, cache.shape[2]), jnp.bfloat16),
        ],
    )
    return pl.pallas_call(
        attn_kernel,
        grid_spec=grid_spec,
        interpret=INTERPRET,
        out_shape=jax.ShapeDtypeStruct((width, tokens), jnp.bfloat16),
        compiler_params=pltpu.CompilerParams(
            dimension_semantics=("arbitrary",), vmem_limit_bytes=48 * 1024 * 1024
        ),
    )(plist, pcount, page_node, page_fill, kfirst, qt, tok, proj, vnt, segk, cache)


def shift_perm(n, d):
    return [(j, (j + d) % n) for j in range(n)]


def head_gather(x, n):
    me = lax.axis_index("head")
    parts = [x] + [lax.ppermute(x, "head", shift_perm(n, d)) for d in range(1, n)]
    stacked = jnp.stack(parts)
    order = (me - jnp.arange(n, dtype=jnp.int32)) % n
    gathered = jnp.take(stacked, order, axis=0)
    return gathered.reshape(n * x.shape[0], x.shape[1])


def head_reduce_scatter(partial, n):
    me = lax.axis_index("head")
    rows = partial.shape[0] // n
    chunks = partial.reshape(n, rows, partial.shape[1])
    total = lax.dynamic_index_in_dim(chunks, me, 0, keepdims=False)
    for d in range(1, n):
        send = lax.dynamic_index_in_dim(chunks, (me + d) % n, 0, keepdims=False)
        recv = lax.ppermute(send.astype(jnp.bfloat16), "head", shift_perm(n, d))
        total = total + recv.astype(jnp.float32)
    return total.astype(jnp.bfloat16)


def shards(
    hidden_in,
    norm_gain,
    w_qkv,
    w_out,
    cache_kv,
    page_node,
    page_fill,
    node_parent,
    tok_seg,
    req_leaf,
):
    widened = hidden_in[0].astype(jnp.float32)
    normed = (
        widened
        * lax.rsqrt(jnp.mean(widened * widened, axis=1, keepdims=True) + EPSILON)
        * norm_gain
    ).astype(jnp.bfloat16)
    model_width = widened.shape[1]
    group_width = w_qkv.shape[2]
    weight_flat = w_qkv.reshape(model_width, 3 * group_width)
    n_head = tok_seg.shape[1] // hidden_in.shape[1]
    w_full = head_gather(w_out, n_head)
    projected = jnp.dot(
        head_gather(normed, n_head),
        weight_flat,
        preferred_element_type=jnp.float32,
    ).astype(jnp.bfloat16)
    tokens = projected.shape[0]
    segment = tok_seg[0]
    leaf_node = lookup(segment, req_leaf[0])
    upper_node = lookup(leaf_node, node_parent)
    root_node = lookup(upper_node, node_parent)
    zero_row = jnp.zeros_like(segment)
    tok = jnp.stack(
        [segment, leaf_node, upper_node, root_node] + [zero_row] * 4, axis=0
    )
    pages = page_node.shape[0]
    seen = (
        (page_node[None, :] == leaf_node[:, None])
        | (page_node[None, :] == upper_node[:, None])
        | (page_node[None, :] == root_node[:, None])
    )
    nqb = tokens // Q_BLOCK
    vis = jnp.any(seen.reshape(nqb, Q_BLOCK, pages), axis=1).astype(jnp.int32)
    rank = jnp.cumsum(vis, axis=1) - 1
    picked = (vis[:, :, None] > 0) & (rank[:, :, None] == jnp.arange(pages)[None, None, :])
    plist = jnp.sum(
        jnp.where(picked, jnp.arange(pages, dtype=jnp.int32)[None, :, None], 0), axis=1
    ).astype(jnp.int32)
    plist = jnp.pad(plist, ((0, 0), (0, CHAINS))).reshape(-1)
    pcount = jnp.sum(vis, axis=1).astype(jnp.int32)
    first_seg = segment[::Q_BLOCK]
    kfirst = (
        jnp.sum((segment[None, :] < first_seg[:, None]).astype(jnp.int32), axis=1) // K_BLOCK
    ).astype(jnp.int32)
    segk = segment[:, None]
    qt = projected[:, :group_width].T
    vnt = projected[:, 2 * group_width:].T
    cache = lax.all_gather(cache_kv, "page", axis=1, tiled=True)
    attn_t = attention(
        plist, pcount, page_node, page_fill, kfirst, qt, tok, projected, vnt, segk, cache
    )
    me = lax.axis_index("head")
    rows = tokens // n_head
    parts = [lax.dynamic_slice_in_dim(attn_t, me * rows, rows, axis=1)]
    for d in range(1, n_head):
        send = lax.dynamic_slice_in_dim(attn_t, ((me + d) % n_head) * rows, rows, axis=1)
        parts.append(lax.ppermute(send, "head", shift_perm(n_head, d)))
    order = (me - jnp.arange(n_head, dtype=jnp.int32)) % n_head
    mine = jnp.take(jnp.stack(parts), order, axis=0)
    mine = mine.reshape(n_head * mine.shape[1], rows)
    result = lax.dot_general(
        mine, w_full, (((0,), (0,)), ((), ())), preferred_element_type=jnp.float32
    ).astype(jnp.bfloat16)
    return result[None]


def solution(mesh):
    placed = (
        P("page", "head", None),
        P(),
        P(None, None, "head"),
        P("head", None),
        P(None, "page", None, "head"),
        P(),
        P(),
        P(),
        P("page", None),
        P("page", None),
    )
    return jax.shard_map(
        shards, mesh=mesh, in_specs=placed, out_specs=P("page", "head", None), check_vma=False
    )
```

```python
import jax
import jax.numpy as jnp
from jax import lax
from jax.experimental import pallas as pl
from jax.experimental.pallas import tpu as pltpu
from jax.sharding import PartitionSpec as P

HD = 64
EPSILON = 1e-06
FLOOR_SCORE = -1e30
Q_BLOCK = 256
K_BLOCK = 128
CHAINS = 4
INTERPRET = False


def lookup(indices, lookup_table):
    matches = indices[:, None] == jnp.arange(lookup_table.shape[0], dtype=jnp.int32)[None, :]
    return jnp.sum(jnp.where(matches, lookup_table[None, :], 0), axis=1)


def attn_kernel(
    plist_ref, pcount_ref, pnode_ref, pfill_ref, kfirst_ref,
    qt_ref, tok_ref, kn_ref, vnt_ref, segk_ref, cache_ref,
    o_ref,
    *scratch,
):
    cvt_ref = scratch[-1]
    chains = [tuple(scratch[3 * c:3 * c + 3]) for c in range(CHAINS)]
    i = pl.program_id(0)
    width, tq = qt_ref.shape
    groups = width // HD
    pages = cache_ref.shape[1]
    kb = cache_ref.shape[2]

    @pl.when(i == 0)
    def _():
        def transpose_page(g, carry):
            cvt_ref[g] = cache_ref[1, g].astype(jnp.float32).T.astype(cvt_ref.dtype)
            return carry

        lax.fori_loop(0, pages, transpose_page, 0)

    qt = qt_ref[...] * jnp.asarray(0.125, jnp.bfloat16)
    seg_q = tok_ref[0:1, :]
    leaf = tok_ref[1:2, :]
    upper = tok_ref[2:3, :]
    root = tok_ref[3:4, :]
    for m_sc, l_sc, acc_sc in chains:
        m_sc[...] = jnp.full(m_sc.shape, FLOOR_SCORE, jnp.float32)
        l_sc[...] = jnp.zeros(l_sc.shape, jnp.float32)
        acc_sc[...] = jnp.zeros(acc_sc.shape, jnp.float32)
    col_head = lax.broadcasted_iota(jnp.int32, (kb, width), 1) // HD
    row_head = lax.broadcasted_iota(jnp.int32, (width, kb), 0) // HD
    slot = lax.broadcasted_iota(jnp.int32, (kb, 1), 0)

    def update(state, k, vt, mask):
        m_sc, l_sc, acc_sc = state
        zk = jnp.zeros_like(k)
        kbd = jnp.concatenate([jnp.where(col_head == h, k, zk) for h in range(groups)], axis=0)
        st = jnp.dot(kbd, qt, preferred_element_type=jnp.float32)
        probs = []
        scales = []
        for h in range(groups):
            s_h = jnp.where(mask, st[h * kb:(h + 1) * kb, :], FLOOR_SCORE)
            m_old = m_sc[h]
            m_new = jnp.maximum(m_old, jnp.max(s_h, axis=0, keepdims=True))
            alpha = jnp.exp(m_old - m_new)
            p_h = jnp.exp(s_h - m_new)
            l_sc[h] = alpha * l_sc[h] + jnp.sum(p_h, axis=0, keepdims=True)
            m_sc[h] = m_new
            probs.append(p_h.astype(jnp.bfloat16))
            scales.append(jnp.broadcast_to(alpha, (HD, tq)))
        zv = jnp.zeros_like(vt)
        vbdt = jnp.concatenate([jnp.where(row_head == h, vt, zv) for h in range(groups)], axis=1)
        pv = jnp.dot(vbdt, jnp.concatenate(probs, axis=0), preferred_element_type=jnp.float32)
        acc_sc[...] = acc_sc[...] * jnp.concatenate(scales, axis=0) + pv

    stride = plist_ref.shape[0] // kfirst_ref.shape[0]
    qpos = i * tq + lax.broadcasted_iota(jnp.int32, (1, tq), 1)

    last = (i * tq + tq - 1) // kb
    first = kfirst_ref[i]

    def suffix_step(j, carry):
        for c in range(CHAINS):
            b = first + CHAINS * j + c
            valid = b <= last
            start = pl.multiple_of(jnp.minimum(b, last) * kb, kb)
            kpos = start + slot
            mask = (segk_ref[pl.ds(start, kb), :] == seg_q) & (kpos <= qpos) & valid
            update(chains[c], kn_ref[pl.ds(start, kb), :], vnt_ref[:, pl.ds(start, kb)], mask)
        return carry

    lax.fori_loop(0, (last - first + CHAINS) // CHAINS, suffix_step, 0)

    count = pcount_ref[i]

    def page_mask(g, valid):
        node = pnode_ref[g]
        fill = jnp.where(valid, pfill_ref[g], 0)
        tok_ok = (leaf == node) | (upper == node) | (root == node)
        return tok_ok & (slot < fill)

    def group_step(j, carry):
        for c in range(CHAINS):
            at = CHAINS * j + c
            g = plist_ref[i * stride + at]
            update(chains[c], cache_ref[0, g], cvt_ref[g], page_mask(g, at < count))
        return carry

    lax.fori_loop(0, (count + CHAINS - 1) // CHAINS, group_step, 0)

    parts = []
    for h in range(groups):
        m_all = chains[0][0][h]
        for c in range(1, CHAINS):
            m_all = jnp.maximum(m_all, chains[c][0][h])
        rows = slice(h * HD, (h + 1) * HD)
        l_all = None
        acc_h = None
        for m_sc, l_sc, acc_sc in chains:
            w = jnp.exp(m_sc[h] - m_all)
            l_part = l_sc[h] * w
            acc_part = acc_sc[rows, :] * w
            l_all = l_part if l_all is None else l_all + l_part
            acc_h = acc_part if acc_h is None else acc_h + acc_part
        parts.append(acc_h / l_all)
    o_ref[...] = jnp.concatenate(parts, axis=0).astype(o_ref.dtype)


def attention(plist, pcount, page_node, page_fill, kfirst, qt, tok, proj, vnt, segk, cache):
    width, tokens = qt.shape
    groups = width // HD
    nqb = tokens // Q_BLOCK
    state = [
        pltpu.VMEM((groups, 1, Q_BLOCK), jnp.float32),
        pltpu.VMEM((groups, 1, Q_BLOCK), jnp.float32),
        pltpu.VMEM((width, Q_BLOCK), jnp.float32),
    ]
    grid_spec = pltpu.PrefetchScalarGridSpec(
        num_scalar_prefetch=5,
        grid=(nqb,),
        in_specs=[
            pl.BlockSpec((width, Q_BLOCK), lambda i, *_: (0, i)),
            pl.BlockSpec((tok.shape[0], Q_BLOCK), lambda i, *_: (0, i)),
            pl.BlockSpec((tokens, width), lambda i, *_: (0, 1)),
            pl.BlockSpec(memory_space=pltpu.VMEM),
            pl.BlockSpec(memory_space=pltpu.VMEM),
            pl.BlockSpec(memory_space=pltpu.VMEM),
        ],
        out_specs=pl.BlockSpec((width, Q_BLOCK), lambda i, *_: (0, i)),
        scratch_shapes=state * CHAINS + [
            pltpu.VMEM((cache.shape[1], width, cache.shape[2]), jnp.bfloat16),
        ],
    )
    return pl.pallas_call(
        attn_kernel,
        grid_spec=grid_spec,
        interpret=INTERPRET,
        out_shape=jax.ShapeDtypeStruct((width, tokens), jnp.bfloat16),
        compiler_params=pltpu.CompilerParams(
            dimension_semantics=("arbitrary",), vmem_limit_bytes=48 * 1024 * 1024
        ),
    )(plist, pcount, page_node, page_fill, kfirst, qt, tok, proj, vnt, segk, cache)


def shift_perm(n, d):
    return [(j, (j + d) % n) for j in range(n)]


def head_gather(x, n):
    me = lax.axis_index("head")
    parts = [x] + [lax.ppermute(x, "head", shift_perm(n, d)) for d in range(1, n)]
    stacked = jnp.stack(parts)
    order = (me - jnp.arange(n, dtype=jnp.int32)) % n
    gathered = jnp.take(stacked, order, axis=0)
    return gathered.reshape(n * x.shape[0], x.shape[1])


def head_reduce_scatter(partial, n):
    me = lax.axis_index("head")
    rows = partial.shape[0] // n
    chunks = partial.reshape(n, rows, partial.shape[1])
    total = lax.dynamic_index_in_dim(chunks, me, 0, keepdims=False)
    for d in range(1, n):
        send = lax.dynamic_index_in_dim(chunks, (me + d) % n, 0, keepdims=False)
        recv = lax.ppermute(send.astype(jnp.bfloat16), "head", shift_perm(n, d))
        total = total + recv.astype(jnp.float32)
    return total.astype(jnp.bfloat16)


def shards(
    hidden_in,
    norm_gain,
    w_qkv,
    w_out,
    cache_kv,
    page_node,
    page_fill,
    node_parent,
    tok_seg,
    req_leaf,
):
    widened = hidden_in[0].astype(jnp.float32)
    normed = (
        widened
        * lax.rsqrt(jnp.mean(widened * widened, axis=1, keepdims=True) + EPSILON)
        * norm_gain
    ).astype(jnp.bfloat16)
    model_width = widened.shape[1]
    group_width = w_qkv.shape[2]
    weight_flat = w_qkv.reshape(model_width, 3 * group_width)
    n_head = tok_seg.shape[1] // hidden_in.shape[1]
    w_full = head_gather(w_out, n_head)
    projected = jnp.dot(
        head_gather(normed, n_head),
        weight_flat,
        preferred_element_type=jnp.float32,
    ).astype(jnp.bfloat16)
    tokens = projected.shape[0]
    segment = tok_seg[0]
    leaf_node = lookup(segment, req_leaf[0])
    upper_node = lookup(leaf_node, node_parent)
    root_node = lookup(upper_node, node_parent)
    zero_row = jnp.zeros_like(segment)
    tok = jnp.stack(
        [segment, leaf_node, upper_node, root_node] + [zero_row] * 4, axis=0
    )
    pages = page_node.shape[0]
    seen = (
        (page_node[None, :] == leaf_node[:, None])
        | (page_node[None, :] == upper_node[:, None])
        | (page_node[None, :] == root_node[:, None])
    )
    nqb = tokens // Q_BLOCK
    vis = jnp.any(seen.reshape(nqb, Q_BLOCK, pages), axis=1).astype(jnp.int32)
    rank = jnp.cumsum(vis, axis=1) - 1
    picked = (vis[:, :, None] > 0) & (rank[:, :, None] == jnp.arange(pages)[None, None, :])
    plist = jnp.sum(
        jnp.where(picked, jnp.arange(pages, dtype=jnp.int32)[None, :, None], 0), axis=1
    ).astype(jnp.int32)
    plist = jnp.pad(plist, ((0, 0), (0, CHAINS))).reshape(-1)
    pcount = jnp.sum(vis, axis=1).astype(jnp.int32)
    first_seg = segment[::Q_BLOCK]
    kfirst = (
        jnp.sum((segment[None, :] < first_seg[:, None]).astype(jnp.int32), axis=1) // K_BLOCK
    ).astype(jnp.int32)
    segk = segment[:, None]
    qt = projected[:, :group_width].T
    vnt = projected[:, 2 * group_width:].T
    cache = lax.all_gather(cache_kv, "page", axis=1, tiled=True)
    attn_t = attention(
        plist, pcount, page_node, page_fill, kfirst, qt, tok, projected, vnt, segk, cache
    )
    me = lax.axis_index("head")
    rows = tokens // n_head
    parts = [lax.dynamic_slice_in_dim(attn_t, me * rows, rows, axis=1)]
    for d in range(1, n_head):
        send = lax.dynamic_slice_in_dim(attn_t, ((me + d) % n_head) * rows, rows, axis=1)
        parts.append(lax.ppermute(send, "head", shift_perm(n_head, d)))
    order = (me - jnp.arange(n_head, dtype=jnp.int32)) % n_head
    mine = jnp.take(jnp.stack(parts), order, axis=0)
    mine = mine.reshape(n_head * mine.shape[1], rows)
    result = lax.dot_general(
        mine, w_full, (((0,), (0,)), ((), ())), preferred_element_type=jnp.float32
    ).astype(jnp.bfloat16)
    return result[None]


def solution(mesh):
    placed = (
        P("page", "head", None),
        P(),
        P(None, None, "head"),
        P("head", None),
        P(None, "page", None, "head"),
        P(),
        P(),
        P(),
        P("page", None),
        P("page", None),
    )
    return jax.shard_map(
        shards, mesh=mesh, in_specs=placed, out_specs=P("page", "head", None), check_vma=False
    )
```

```python
import jax
import jax.numpy as jnp
from jax import lax
from jax.experimental import pallas as pl
from jax.experimental.pallas import tpu as pltpu
from jax.sharding import PartitionSpec as P

HD = 64
EPSILON = 1e-06
FLOOR_SCORE = -1e30
Q_BLOCK = 256
K_BLOCK = 128
CHAINS = 5
INTERPRET = False


def lookup(indices, lookup_table):
    matches = indices[:, None] == jnp.arange(lookup_table.shape[0], dtype=jnp.int32)[None, :]
    return jnp.sum(jnp.where(matches, lookup_table[None, :], 0), axis=1)


def attn_kernel(
    plist_ref, pcount_ref, pnode_ref, pfill_ref, kfirst_ref,
    qt_ref, tok_ref, kn_ref, vnt_ref, segk_ref, cache_ref,
    o_ref,
    *scratch,
):
    cvt_ref = scratch[-1]
    chains = [tuple(scratch[3 * c:3 * c + 3]) for c in range(CHAINS)]
    i = pl.program_id(0)
    width, tq = qt_ref.shape
    groups = width // HD
    pages = cache_ref.shape[1]
    kb = cache_ref.shape[2]

    @pl.when(i == 0)
    def _():
        def transpose_page(g, carry):
            cvt_ref[g] = cache_ref[1, g].astype(jnp.float32).T.astype(cvt_ref.dtype)
            return carry

        lax.fori_loop(0, pages, transpose_page, 0)

    qt = qt_ref[...] * jnp.asarray(0.125, jnp.bfloat16)
    seg_q = tok_ref[0:1, :]
    leaf = tok_ref[1:2, :]
    upper = tok_ref[2:3, :]
    root = tok_ref[3:4, :]
    for m_sc, l_sc, acc_sc in chains:
        m_sc[...] = jnp.full(m_sc.shape, FLOOR_SCORE, jnp.float32)
        l_sc[...] = jnp.zeros(l_sc.shape, jnp.float32)
        acc_sc[...] = jnp.zeros(acc_sc.shape, jnp.float32)
    col_head = lax.broadcasted_iota(jnp.int32, (kb, width), 1) // HD
    row_head = lax.broadcasted_iota(jnp.int32, (width, kb), 0) // HD
    slot = lax.broadcasted_iota(jnp.int32, (kb, 1), 0)

    def update(state, k, vt, mask):
        m_sc, l_sc, acc_sc = state
        zk = jnp.zeros_like(k)
        kbd = jnp.concatenate([jnp.where(col_head == h, k, zk) for h in range(groups)], axis=0)
        st = jnp.dot(kbd, qt, preferred_element_type=jnp.float32)
        probs = []
        scales = []
        for h in range(groups):
            s_h = jnp.where(mask, st[h * kb:(h + 1) * kb, :], FLOOR_SCORE)
            m_old = m_sc[h]
            m_new = jnp.maximum(m_old, jnp.max(s_h, axis=0, keepdims=True))
            alpha = jnp.exp(m_old - m_new)
            p_h = jnp.exp(s_h - m_new)
            l_sc[h] = alpha * l_sc[h] + jnp.sum(p_h, axis=0, keepdims=True)
            m_sc[h] = m_new
            probs.append(p_h.astype(jnp.bfloat16))
            scales.append(jnp.broadcast_to(alpha, (HD, tq)))
        zv = jnp.zeros_like(vt)
        vbdt = jnp.concatenate([jnp.where(row_head == h, vt, zv) for h in range(groups)], axis=1)
        pv = jnp.dot(vbdt, jnp.concatenate(probs, axis=0), preferred_element_type=jnp.float32)
        acc_sc[...] = acc_sc[...] * jnp.concatenate(scales, axis=0) + pv

    stride = plist_ref.shape[0] // kfirst_ref.shape[0]
    qpos = i * tq + lax.broadcasted_iota(jnp.int32, (1, tq), 1)

    last = (i * tq + tq - 1) // kb
    first = kfirst_ref[i]

    def suffix_step(j, carry):
        for c in range(CHAINS):
            b = first + CHAINS * j + c
            valid = b <= last
            start = pl.multiple_of(jnp.minimum(b, last) * kb, kb)
            kpos = start + slot
            mask = (segk_ref[pl.ds(start, kb), :] == seg_q) & (kpos <= qpos) & valid
            update(chains[c], kn_ref[pl.ds(start, kb), :], vnt_ref[:, pl.ds(start, kb)], mask)
        return carry

    lax.fori_loop(0, (last - first + CHAINS) // CHAINS, suffix_step, 0)

    count = pcount_ref[i]

    def page_mask(g, valid):
        node = pnode_ref[g]
        fill = jnp.where(valid, pfill_ref[g], 0)
        tok_ok = (leaf == node) | (upper == node) | (root == node)
        return tok_ok & (slot < fill)

    def group_step(j, carry):
        for c in range(CHAINS):
            at = CHAINS * j + c
            g = plist_ref[i * stride + at]
            update(chains[c], cache_ref[0, g], cvt_ref[g], page_mask(g, at < count))
        return carry

    lax.fori_loop(0, (count + CHAINS - 1) // CHAINS, group_step, 0)

    parts = []
    for h in range(groups):
        m_all = chains[0][0][h]
        for c in range(1, CHAINS):
            m_all = jnp.maximum(m_all, chains[c][0][h])
        rows = slice(h * HD, (h + 1) * HD)
        l_all = None
        acc_h = None
        for m_sc, l_sc, acc_sc in chains:
            w = jnp.exp(m_sc[h] - m_all)
            l_part = l_sc[h] * w
            acc_part = acc_sc[rows, :] * w
            l_all = l_part if l_all is None else l_all + l_part
            acc_h = acc_part if acc_h is None else acc_h + acc_part
        parts.append(acc_h / l_all)
    o_ref[...] = jnp.concatenate(parts, axis=0).astype(o_ref.dtype)


def attention(plist, pcount, page_node, page_fill, kfirst, qt, tok, proj, vnt, segk, cache):
    width, tokens = qt.shape
    groups = width // HD
    nqb = tokens // Q_BLOCK
    state = [
        pltpu.VMEM((groups, 1, Q_BLOCK), jnp.float32),
        pltpu.VMEM((groups, 1, Q_BLOCK), jnp.float32),
        pltpu.VMEM((width, Q_BLOCK), jnp.float32),
    ]
    grid_spec = pltpu.PrefetchScalarGridSpec(
        num_scalar_prefetch=5,
        grid=(nqb,),
        in_specs=[
            pl.BlockSpec((width, Q_BLOCK), lambda i, *_: (0, i)),
            pl.BlockSpec((tok.shape[0], Q_BLOCK), lambda i, *_: (0, i)),
            pl.BlockSpec((tokens, width), lambda i, *_: (0, 1)),
            pl.BlockSpec(memory_space=pltpu.VMEM),
            pl.BlockSpec(memory_space=pltpu.VMEM),
            pl.BlockSpec(memory_space=pltpu.VMEM),
        ],
        out_specs=pl.BlockSpec((width, Q_BLOCK), lambda i, *_: (0, i)),
        scratch_shapes=state * CHAINS + [
            pltpu.VMEM((cache.shape[1], width, cache.shape[2]), jnp.bfloat16),
        ],
    )
    return pl.pallas_call(
        attn_kernel,
        grid_spec=grid_spec,
        interpret=INTERPRET,
        out_shape=jax.ShapeDtypeStruct((width, tokens), jnp.bfloat16),
        compiler_params=pltpu.CompilerParams(
            dimension_semantics=("arbitrary",), vmem_limit_bytes=48 * 1024 * 1024
        ),
    )(plist, pcount, page_node, page_fill, kfirst, qt, tok, proj, vnt, segk, cache)


def shift_perm(n, d):
    return [(j, (j + d) % n) for j in range(n)]


def head_gather(x, n):
    me = lax.axis_index("head")
    parts = [x] + [lax.ppermute(x, "head", shift_perm(n, d)) for d in range(1, n)]
    stacked = jnp.stack(parts)
    order = (me - jnp.arange(n, dtype=jnp.int32)) % n
    gathered = jnp.take(stacked, order, axis=0)
    return gathered.reshape(n * x.shape[0], x.shape[1])


def head_reduce_scatter(partial, n):
    me = lax.axis_index("head")
    rows = partial.shape[0] // n
    chunks = partial.reshape(n, rows, partial.shape[1])
    total = lax.dynamic_index_in_dim(chunks, me, 0, keepdims=False)
    for d in range(1, n):
        send = lax.dynamic_index_in_dim(chunks, (me + d) % n, 0, keepdims=False)
        recv = lax.ppermute(send.astype(jnp.bfloat16), "head", shift_perm(n, d))
        total = total + recv.astype(jnp.float32)
    return total.astype(jnp.bfloat16)


def shards(
    hidden_in,
    norm_gain,
    w_qkv,
    w_out,
    cache_kv,
    page_node,
    page_fill,
    node_parent,
    tok_seg,
    req_leaf,
):
    widened = hidden_in[0].astype(jnp.float32)
    normed = (
        widened
        * lax.rsqrt(jnp.mean(widened * widened, axis=1, keepdims=True) + EPSILON)
        * norm_gain
    ).astype(jnp.bfloat16)
    model_width = widened.shape[1]
    group_width = w_qkv.shape[2]
    weight_flat = w_qkv.reshape(model_width, 3 * group_width)
    n_head = tok_seg.shape[1] // hidden_in.shape[1]
    w_full = head_gather(w_out, n_head)
    projected = jnp.dot(
        head_gather(normed, n_head),
        weight_flat,
        preferred_element_type=jnp.float32,
    ).astype(jnp.bfloat16)
    tokens = projected.shape[0]
    segment = tok_seg[0]
    leaf_node = lookup(segment, req_leaf[0])
    upper_node = lookup(leaf_node, node_parent)
    root_node = lookup(upper_node, node_parent)
    zero_row = jnp.zeros_like(segment)
    tok = jnp.stack(
        [segment, leaf_node, upper_node, root_node] + [zero_row] * 4, axis=0
    )
    pages = page_node.shape[0]
    seen = (
        (page_node[None, :] == leaf_node[:, None])
        | (page_node[None, :] == upper_node[:, None])
        | (page_node[None, :] == root_node[:, None])
    )
    nqb = tokens // Q_BLOCK
    vis = jnp.any(seen.reshape(nqb, Q_BLOCK, pages), axis=1).astype(jnp.int32)
    rank = jnp.cumsum(vis, axis=1) - 1
    picked = (vis[:, :, None] > 0) & (rank[:, :, None] == jnp.arange(pages)[None, None, :])
    plist = jnp.sum(
        jnp.where(picked, jnp.arange(pages, dtype=jnp.int32)[None, :, None], 0), axis=1
    ).astype(jnp.int32)
    plist = jnp.pad(plist, ((0, 0), (0, CHAINS))).reshape(-1)
    pcount = jnp.sum(vis, axis=1).astype(jnp.int32)
    first_seg = segment[::Q_BLOCK]
    kfirst = (
        jnp.sum((segment[None, :] < first_seg[:, None]).astype(jnp.int32), axis=1) // K_BLOCK
    ).astype(jnp.int32)
    segk = segment[:, None]
    qt = projected[:, :group_width].T
    vnt = projected[:, 2 * group_width:].T
    cache = lax.all_gather(cache_kv, "page", axis=1, tiled=True)
    attn_t = attention(
        plist, pcount, page_node, page_fill, kfirst, qt, tok, projected, vnt, segk, cache
    )
    me = lax.axis_index("head")
    rows = tokens // n_head
    parts = [lax.dynamic_slice_in_dim(attn_t, me * rows, rows, axis=1)]
    for d in range(1, n_head):
        send = lax.dynamic_slice_in_dim(attn_t, ((me + d) % n_head) * rows, rows, axis=1)
        parts.append(lax.ppermute(send, "head", shift_perm(n_head, d)))
    order = (me - jnp.arange(n_head, dtype=jnp.int32)) % n_head
    mine = jnp.take(jnp.stack(parts), order, axis=0)
    mine = mine.reshape(n_head * mine.shape[1], rows)
    result = lax.dot_general(
        mine, w_full, (((0,), (0,)), ((), ())), preferred_element_type=jnp.float32
    ).astype(jnp.bfloat16)
    return result[None]


def solution(mesh):
    placed = (
        P("page", "head", None),
        P(),
        P(None, None, "head"),
        P("head", None),
        P(None, "page", None, "head"),
        P(),
        P(),
        P(),
        P("page", None),
        P("page", None),
    )
    return jax.shard_map(
        shards, mesh=mesh, in_specs=placed, out_specs=P("page", "head", None), check_vma=False
    )
```
